128 devices in a mesh: chan: 8 (over y, core), tm: 16 (over x, z).
Axes of the slice: x: 4, y: 4, z: 4, core: 2. Of those that a mesh axis runs over, the one named last changes fastest.
Arguments:
- record: bfloat16 [4096, 32, 2560], P('chan', 'tm'), may hold values from -6 to 6
- partners: int32 [4096, 8], P('chan'), may hold values from 0 to 4095, as said below
- block_owner: int32 [8, 16], P('chan'), may hold values from 0 to 15, each once within a row
Outputs:
- stacks: float32 [32768, 257], P(('chan', 'tm'))
The draws below stay inside these ranges and needn't reach their ends.
Inputs may be any that keep to these rules, and one draw needn't show every extreme that they name: `partners`: every partner is another channel at most 512 channels away; in every channel block one channel has a partner exactly 512 away. `block_owner`: each row names every index of tm once.
All inputs are finite; a program needn't handle non-finite values.
Results may differ from the reference program's by a relative error of at most 0.0028.
Values may be sent and summed in bfloat16 or wider, within the bound.
No kernel may reach another device: no remote copies, remote signals or barrier semaphores. Data moves between devices by JAX's collectives and lax.ppermute only.
A program may use at most 128 MiB of HBM per device.

```python
import math
import jax
import jax.numpy as jnp
from jax import lax

CB = 512
L = 2560
NFB = 512
F0 = 64
K = 8
LAG = 128
SPAN = 512
C = 4096
WINDOWS = 32
NLAG = 257
PADDED = 5120
N_CHAN = 8
N_TM = 16


def draw_record(key, part):
    key_common, key_incoherent = jax.random.split(jax.random.fold_in(key, 23))
    lead_room = N_CHAN * LAG
    common = jax.random.normal(key_common, (WINDOWS, L + lead_room), jnp.float32)
    incoherent = jax.random.normal(key_incoherent, (C, WINDOWS, L), jnp.float32)
    channel = jnp.arange(C, dtype=jnp.int32)[:, None]
    sample_time = jnp.arange(L, dtype=jnp.int32)[None, :]
    sample_index = sample_time + lead_room - channel * LAG // SPAN

    def delayed(series):
        return jnp.take(series, sample_index, axis=0)
    coherent = jax.vmap(delayed, in_axes=0, out_axes=1)(common)
    summed = 0.9 * coherent + 0.45 * incoherent
    return jnp.clip(summed, -6.0, 6.0).astype(jnp.bfloat16)


def draw_partners(key, part):
    key_dist, key_side, key_pick = jax.random.split(jax.random.fold_in(key, 11), 3)
    channel = jnp.arange(C, dtype=jnp.int32)[:, None]
    distance = jax.random.randint(key_dist, (C, K), 1, SPAN + 1, dtype=jnp.int32)
    direction = jax.random.randint(key_side, (C, K), 0, 2, dtype=jnp.int32) * 2 - 1
    offsets = distance * direction
    target = channel + offsets
    outside = (target < 0) | (target >= C)
    target = jnp.where(outside, channel - offsets, target)
    picked = jax.random.randint(key_pick, (N_CHAN,), 0, CB, dtype=jnp.int32)
    flat = channel[:, 0]
    chosen = flat % CB == picked[flat // CB]
    farthest = jnp.where(flat + SPAN < C, flat + SPAN, flat - SPAN)
    slot_zero = jnp.where(chosen, farthest, target[:, 0])
    return jnp.concatenate([slot_zero[:, None], target[:, 1:]], axis=1).astype(jnp.int32)


def setup_inputs(seed: int = 0) -> dict:
    key_of = jax.random.split(jax.random.key(seed), 4)
    return {
        "record": draw_record(jax.random.fold_in(key_of[3], 71), 0),
        "partners": draw_partners(jax.random.fold_in(key_of[3], 71), 0),
        "block_owner": jax.vmap(lambda own: jax.random.permutation(own, N_TM))(jax.random.split(key_of[2], N_CHAN)).reshape((N_CHAN, N_TM)).astype(jnp.int32),
    }


def fourier_table():
    times = jnp.arange(L, dtype=jnp.int32)[:, None]
    freqs = (F0 + jnp.arange(NFB, dtype=jnp.int32))[None, :]
    phase = (times * freqs % PADDED).astype(jnp.float32) * (2.0 * math.pi / PADDED)
    return jnp.concatenate([jnp.cos(phase), -jnp.sin(phase)], axis=1).astype(jnp.bfloat16)

def lag_table():
    freqs = (F0 + jnp.arange(NFB, dtype=jnp.int32))[:, None]
    shifts = (jnp.arange(NLAG, dtype=jnp.int32) - LAG)[None, :]
    phase = (freqs * shifts % PADDED).astype(jnp.float32) * (2.0 * math.pi / PADDED)
    return jnp.concatenate([jnp.cos(phase), -jnp.sin(phase)], axis=0)

def whiten(rows, fourier):
    flat = rows.reshape(-1, L)
    spectra = jnp.dot(flat, fourier, preferred_element_type=jnp.float32)
    real_part = spectra[:, :NFB]
    imag_part = spectra[:, NFB:]
    energy = real_part * real_part + imag_part * imag_part
    level = lax.optimization_barrier(jnp.mean(energy, axis=1, keepdims=True))
    divisor = jnp.sqrt(energy + 0.1 * level + 1e-05)
    whitened = jnp.concatenate([real_part / divisor, imag_part / divisor], axis=1)
    return whitened.astype(jnp.bfloat16).reshape(rows.shape[0], rows.shape[1], 2 * NFB)

def cross_spectra(own_rows, partner_rows):
    own_real = own_rows[:, None, :, :NFB].astype(jnp.float32)
    own_imag = own_rows[:, None, :, NFB:].astype(jnp.float32)
    far_real = partner_rows[:, :, :, :NFB].astype(jnp.float32)
    far_imag = partner_rows[:, :, :, NFB:].astype(jnp.float32)
    cross_real = lax.optimization_barrier(jnp.sum(own_real * far_real + own_imag * far_imag, axis=2))
    cross_imag = lax.optimization_barrier(jnp.sum(own_real * far_imag - own_imag * far_real, axis=2))
    joined = jnp.concatenate([cross_real, cross_imag], axis=2)
    return joined.reshape(-1, 2 * NFB)

def reference(record, partners, block_owner):
    fourier = fourier_table()
    blocks = record.reshape(N_CHAN, CB, WINDOWS, L)
    whitened = lax.map(lambda rows: whiten(rows, fourier), blocks).reshape(C, WINDOWS, 2 * NFB)
    own_blocks = whitened.reshape(N_CHAN, CB, WINDOWS, 2 * NFB)
    partner_blocks = partners.reshape(N_CHAN, CB, K)

    def one_block(inputs):
        own_rows, indices = inputs
        return cross_spectra(own_rows, jnp.take(whitened, indices.astype(jnp.int32), axis=0))
    cross = lax.map(one_block, (own_blocks, partner_blocks)).reshape(C * K, 2 * NFB)
    scale = 1.0 / math.sqrt(WINDOWS * NFB)
    lags = jnp.dot(cross, lag_table(), precision=lax.Precision.HIGHEST, preferred_element_type=jnp.float32) * scale
    lags = lags.reshape(N_CHAN, N_TM, CB * K // N_TM, NLAG)
    inverse = jnp.argsort(block_owner, axis=1).astype(jnp.int32)
    placed = jnp.take_along_axis(lags, inverse[:, :, None, None], axis=1)
    return placed.reshape(C * K, NLAG)
```

```python
import math

import jax
import jax.numpy as jnp
from jax import lax
from jax.sharding import PartitionSpec as P

NFB = 512
F0 = 64
K = 8
LAG = 128


def split_length(samples):
    best = 1
    for b in range(1, samples + 1):
        if samples % b == 0 and b * b <= samples:
            best = b
    return samples // best, best


def fourier_table(samples):
    padded = 2 * samples
    outer, inner = split_length(samples)
    freqs = (F0 + jnp.arange(NFB, dtype=jnp.int32))[None, :]
    step = 2.0 * math.pi / padded
    coarse = (jnp.arange(outer, dtype=jnp.int32)[:, None] * inner * freqs % padded).astype(jnp.float32) * step
    fine = (jnp.arange(inner, dtype=jnp.int32)[:, None] * freqs % padded).astype(jnp.float32) * step
    ca, sa = jnp.cos(coarse)[:, None, :], jnp.sin(coarse)[:, None, :]
    cb, sb = jnp.cos(fine)[None, :, :], jnp.sin(fine)[None, :, :]
    cos_t = (ca * cb - sa * sb).reshape(samples, NFB)
    sin_t = (sa * cb + ca * sb).reshape(samples, NFB)
    return jnp.concatenate([cos_t, -sin_t], axis=1).astype(jnp.bfloat16)


def lag_table(samples):
    freqs = (F0 + jnp.arange(NFB, dtype=jnp.int32))[:, None]
    shifts = (jnp.arange(2 * LAG + 1, dtype=jnp.int32) - LAG)[None, :]
    phase = (freqs * shifts % (2 * samples)).astype(jnp.float32) * (2.0 * math.pi / (2 * samples))
    return jnp.concatenate([jnp.cos(phase), -jnp.sin(phase)], axis=0)


def whiten(rows, fourier):
    spectra = lax.dot_general(
        rows, fourier, (((2,), (0,)), ((), ())), preferred_element_type=jnp.float32
    )
    real_part = spectra[..., :NFB]
    imag_part = spectra[..., NFB:]
    energy = real_part * real_part + imag_part * imag_part
    level = jnp.mean(energy, axis=-1, keepdims=True)
    divisor = jnp.sqrt(energy + 0.1 * level + 1e-05)
    whitened = jnp.concatenate([real_part / divisor, imag_part / divisor], axis=-1)
    return whitened.astype(jnp.bfloat16)


def neighbourhood(own):
    size = lax.axis_size("chan")
    up = [(i, i + 1) for i in range(size - 1)]
    down = [(j, i) for i, j in up]
    below = lax.ppermute(own, "chan", up)
    above = lax.ppermute(own, "chan", down)
    return jnp.concatenate([below, own, above], axis=0)


def shards(record, partners, block_owner):
    block_size, windows_dev, samples = record.shape
    width = windows_dev * 2 * NFB
    fourier = fourier_table(samples)
    own = whiten(record, fourier).reshape(block_size, width)
    near = neighbourhood(own)

    tm_count = lax.axis_size("tm")
    per_block = block_size // tm_count
    owner_row = block_owner[0]
    onehot = (owner_row[None, :] == jnp.arange(tm_count, dtype=jnp.int32)[:, None]).astype(jnp.int32)
    inverse = jnp.sum(onehot * jnp.arange(tm_count, dtype=jnp.int32)[None, :], axis=1)
    own_sorted = jnp.take(own.reshape(tm_count, per_block, width), inverse, axis=0).reshape(block_size, 1, width)
    partners_sorted = jnp.take(partners.reshape(tm_count, per_block, K), inverse, axis=0)
    base_row = lax.axis_index("chan") * block_size - block_size
    local_rows = (partners_sorted - base_row).reshape(-1)
    far = jnp.take(near, local_rows, axis=0, mode="clip").reshape(block_size, K, width)

    cross_real = 0.0
    cross_imag = 0.0
    for w in range(windows_dev):
        lo = w * 2 * NFB
        ar = own_sorted[..., lo : lo + NFB].astype(jnp.float32)
        ai = own_sorted[..., lo + NFB : lo + 2 * NFB].astype(jnp.float32)
        br = far[..., lo : lo + NFB].astype(jnp.float32)
        bi = far[..., lo + NFB : lo + 2 * NFB].astype(jnp.float32)
        cross_real = cross_real + (ar * br + ai * bi)
        cross_imag = cross_imag + (ar * bi - ai * br)
    cross = jnp.concatenate([cross_real, cross_imag], axis=-1).reshape(block_size * K, 2 * NFB)

    partial = jnp.dot(
        cross, lag_table(samples), precision=lax.Precision.HIGH, preferred_element_type=jnp.float32
    )
    summed = lax.psum_scatter(partial, "tm", scatter_dimension=0, tiled=True)
    scale = 1.0 / math.sqrt(windows_dev * tm_count * NFB)
    return summed * scale


def solution(mesh):
    placed = (P("chan", "tm", None), P("chan", None), P("chan", None))
    return jax.shard_map(
        shards, mesh=mesh, in_specs=placed, out_specs=P(("chan", "tm"), None), check_vma=False
    )
```

```python
import math

import jax
import jax.numpy as jnp
from jax import lax
from jax.sharding import PartitionSpec as P

NFB = 512
F0 = 64
K = 8
LAG = 128


def split_length(samples):
    if samples % 128 == 0:
        return samples // 128, 128
    best = 1
    for b in range(1, samples + 1):
        if samples % b == 0 and b * b <= samples:
            best = b
    return samples // best, best


def angle_pair(rows, cols, padded):
    phase = (rows * cols % padded).astype(jnp.float32) * (2.0 * math.pi / padded)
    return jnp.cos(phase), jnp.sin(phase)


def fourier_table_t(samples):
    padded = 2 * samples
    outer, inner = split_length(samples)
    freqs = (F0 + jnp.arange(NFB, dtype=jnp.int32))[:, None]
    ca, sa = angle_pair(freqs, jnp.arange(outer, dtype=jnp.int32)[None, :] * inner, padded)
    cb, sb = angle_pair(freqs, jnp.arange(inner, dtype=jnp.int32)[None, :], padded)
    ca, sa = ca[:, :, None], sa[:, :, None]
    cb, sb = cb[:, None, :], sb[:, None, :]
    cos_t = (ca * cb - sa * sb).reshape(NFB, samples)
    sin_t = (sa * cb + ca * sb).reshape(NFB, samples)
    return jnp.concatenate([cos_t, -sin_t], axis=0).astype(jnp.bfloat16)


def lag_table(samples):
    padded = 2 * samples
    shifts = (jnp.arange(2 * LAG + 1, dtype=jnp.int32) - LAG)[None, :]
    fine = 16
    cu, su = angle_pair((F0 + fine * jnp.arange(NFB // fine, dtype=jnp.int32))[:, None], shifts, padded)
    cv, sv = angle_pair(jnp.arange(fine, dtype=jnp.int32)[:, None], shifts, padded)
    cu, su = cu[:, None, :], su[:, None, :]
    cv, sv = cv[None, :, :], sv[None, :, :]
    cos_t = (cu * cv - su * sv).reshape(NFB, -1)
    sin_t = (su * cv + cu * sv).reshape(NFB, -1)
    return jnp.concatenate([cos_t, -sin_t], axis=0)


def whiten(rows, fourier):
    spectra = lax.dot_general(
        rows, fourier, (((2,), (1,)), ((), ())), preferred_element_type=jnp.float32
    )
    real_part = spectra[..., :NFB]
    imag_part = spectra[..., NFB:]
    energy = real_part * real_part + imag_part * imag_part
    level = jnp.mean(energy, axis=-1, keepdims=True)
    divisor = jnp.sqrt(energy + 0.1 * level + 1e-05)
    whitened = jnp.concatenate([real_part / divisor, imag_part / divisor], axis=-1)
    return whitened.astype(jnp.bfloat16)


def neighbourhood(own):
    size = lax.axis_size("chan")
    up = [(i, i + 1) for i in range(size - 1)]
    down = [(j, i) for i, j in up]
    below = lax.ppermute(own, "chan", up)
    above = lax.ppermute(own, "chan", down)
    return jnp.concatenate([below, own, above], axis=0)


def shards(record, partners, block_owner):
    block_size, windows_dev, samples = record.shape
    width = windows_dev * 2 * NFB
    fourier = fourier_table_t(samples)
    own = whiten(record, fourier).reshape(block_size, width)
    near = neighbourhood(own)

    tm_count = lax.axis_size("tm")
    per_block = block_size // tm_count
    owner_row = block_owner[0]
    onehot = (owner_row[None, :] == jnp.arange(tm_count, dtype=jnp.int32)[:, None]).astype(jnp.int32)
    inverse = jnp.sum(onehot * jnp.arange(tm_count, dtype=jnp.int32)[None, :], axis=1)
    own_sorted = jnp.take(own.reshape(tm_count, per_block, width), inverse, axis=0).reshape(block_size, 1, width)
    partners_sorted = jnp.take(partners.reshape(tm_count, per_block, K), inverse, axis=0)
    base_row = lax.axis_index("chan") * block_size - block_size
    local_rows = partners_sorted - base_row
    own_sorted = own_sorted.reshape(tm_count, per_block, width)
    lags = lag_table(samples)
    scale = 1.0 / math.sqrt(windows_dev * tm_count * NFB)
    chunks = 4
    step = per_block // chunks
    pieces = []
    for q in range(chunks):
        own_q = own_sorted[:, q * step : (q + 1) * step].reshape(tm_count * step, 1, width)
        rows_q = local_rows[:, q * step : (q + 1) * step].reshape(-1)
        far = jnp.take(near, rows_q, axis=0, mode="clip").reshape(tm_count * step, K, width)
        cross_real = 0.0
        cross_imag = 0.0
        for w in range(windows_dev):
            lo = w * 2 * NFB
            ar = own_q[..., lo : lo + NFB].astype(jnp.float32)
            ai = own_q[..., lo + NFB : lo + 2 * NFB].astype(jnp.float32)
            br = far[..., lo : lo + NFB].astype(jnp.float32)
            bi = far[..., lo + NFB : lo + 2 * NFB].astype(jnp.float32)
            cross_real = cross_real + (ar * br + ai * bi)
            cross_imag = cross_imag + (ar * bi - ai * br)
        cross = jnp.concatenate([cross_real, cross_imag], axis=-1).reshape(-1, 2 * NFB)
        partial = jnp.dot(cross, lags, precision=lax.Precision.HIGH, preferred_element_type=jnp.float32)
        pieces.append(lax.psum_scatter(partial, "tm", scatter_dimension=0, tiled=True))
    return jnp.concatenate(pieces, axis=0) * scale


def solution(mesh):
    placed = (P("chan", "tm", None), P("chan", None), P("chan", None))
    return jax.shard_map(
        shards, mesh=mesh, in_specs=placed, out_specs=P(("chan", "tm"), None), check_vma=False
    )
```

```python
import math

import jax
import jax.numpy as jnp
from jax import lax
from jax.sharding import PartitionSpec as P

NFB = 512
F0 = 64
K = 8
LAG = 128


def split_length(samples):
    if samples % 128 == 0:
        return samples // 128, 128
    best = 1
    for b in range(1, samples + 1):
        if samples % b == 0 and b * b <= samples:
            best = b
    return samples // best, best


def angle_pair(rows, cols, padded):
    phase = (rows * cols % padded).astype(jnp.float32) * (2.0 * math.pi / padded)
    return jnp.cos(phase), jnp.sin(phase)


def fourier_table_t(samples):
    padded = 2 * samples
    outer, inner = split_length(samples)
    freqs = (F0 + jnp.arange(NFB, dtype=jnp.int32))[:, None]
    ca, sa = angle_pair(freqs, jnp.arange(outer, dtype=jnp.int32)[None, :] * inner, padded)
    cb, sb = angle_pair(freqs, jnp.arange(inner, dtype=jnp.int32)[None, :], padded)
    ca, sa = ca[:, :, None], sa[:, :, None]
    cb, sb = cb[:, None, :], sb[:, None, :]
    cos_t = (ca * cb - sa * sb).reshape(NFB, samples)
    sin_t = (sa * cb + ca * sb).reshape(NFB, samples)
    return jnp.concatenate([cos_t, -sin_t], axis=0).astype(jnp.bfloat16)


def lag_table(samples):
    padded = 2 * samples
    shifts = (jnp.arange(2 * LAG + 1, dtype=jnp.int32) - LAG)[None, :]
    fine = 16
    cu, su = angle_pair((F0 + fine * jnp.arange(NFB // fine, dtype=jnp.int32))[:, None], shifts, padded)
    cv, sv = angle_pair(jnp.arange(fine, dtype=jnp.int32)[:, None], shifts, padded)
    cu, su = cu[:, None, :], su[:, None, :]
    cv, sv = cv[None, :, :], sv[None, :, :]
    cos_t = (cu * cv - su * sv).reshape(NFB, -1)
    sin_t = (su * cv + cu * sv).reshape(NFB, -1)
    return jnp.concatenate([cos_t, -sin_t], axis=0)


def whiten(rows, fourier):
    spectra = lax.dot_general(
        rows, fourier, (((2,), (1,)), ((), ())), preferred_element_type=jnp.float32
    )
    real_part = spectra[..., :NFB]
    imag_part = spectra[..., NFB:]
    energy = real_part * real_part + imag_part * imag_part
    level = jnp.mean(energy, axis=-1, keepdims=True)
    divisor = jnp.sqrt(energy + 0.1 * level + 1e-05)
    whitened = jnp.concatenate([real_part / divisor, imag_part / divisor], axis=-1)
    return whitened.astype(jnp.bfloat16)


def neighbourhood(own):
    size = lax.axis_size("chan")
    up = [(i, i + 1) for i in range(size - 1)]
    down = [(j, i) for i, j in up]
    below = lax.ppermute(own, "chan", up)
    above = lax.ppermute(own, "chan", down)
    return jnp.concatenate([below, own, above], axis=0)


def shards(record, partners, block_owner):
    block_size, windows_dev, samples = record.shape
    width = windows_dev * 2 * NFB
    fourier = fourier_table_t(samples)
    own = whiten(record, fourier).reshape(block_size, width)
    near = neighbourhood(own)

    tm_count = lax.axis_size("tm")
    per_block = block_size // tm_count
    owner_row = block_owner[0]
    onehot = (owner_row[None, :] == jnp.arange(tm_count, dtype=jnp.int32)[:, None]).astype(jnp.int32)
    inverse = jnp.sum(onehot * jnp.arange(tm_count, dtype=jnp.int32)[None, :], axis=1)
    own_sorted = jnp.take(own.reshape(tm_count, per_block, width), inverse, axis=0).reshape(block_size, 1, width)
    partners_sorted = jnp.take(partners.reshape(tm_count, per_block, K), inverse, axis=0)
    base_row = lax.axis_index("chan") * block_size - block_size
    local_rows = (partners_sorted - base_row).reshape(-1)
    far = jnp.take(near, local_rows, axis=0, mode="clip").reshape(block_size, K, width)
    own_sorted = own_sorted.reshape(block_size, 1, width)

    cross_real = 0.0
    cross_imag = 0.0
    for w in range(windows_dev):
        lo = w * 2 * NFB
        ar = own_sorted[..., lo : lo + NFB].astype(jnp.float32)
        ai = own_sorted[..., lo + NFB : lo + 2 * NFB].astype(jnp.float32)
        br = far[..., lo : lo + NFB].astype(jnp.float32)
        bi = far[..., lo + NFB : lo + 2 * NFB].astype(jnp.float32)
        cross_real = cross_real + (ar * br + ai * bi)
        cross_imag = cross_imag + (ar * bi - ai * br)
    cross = jnp.concatenate([cross_real, cross_imag], axis=-1).reshape(block_size * K, 2 * NFB)

    partial = jnp.dot(cross, lag_table(samples), precision=lax.Precision.HIGH, preferred_element_type=jnp.float32)
    summed = scatter_sum(partial.reshape(tm_count, -1, partial.shape[-1]))
    scale = 1.0 / math.sqrt(windows_dev * tm_count * NFB)
    return summed * scale


def ring_pairs(sizes, axis, shift):
    nx, nz = sizes
    pairs = []
    for d in range(nx * nz):
        x, z = d // nz, d % nz
        if axis == 1:
            pairs.append((d, x * nz + (z + shift) % nz))
        else:
            pairs.append((d, ((x + shift) % nx) * nz + z))
    return pairs


def pick(array, index):
    return lax.dynamic_index_in_dim(array, index, 0, keepdims=False)


def scatter_sum(blocks):
    tm_count = blocks.shape[0]
    nz = 4 if tm_count % 4 == 0 else 1
    nx = tm_count // nz
    me = lax.axis_index("tm")
    mx, mz = me // nz, me % nz
    rows = blocks.shape[1]
    grid = blocks.reshape(nx, nz, rows, blocks.shape[2])
    half = rows // 2
    first = jnp.swapaxes(grid[:, :, :half], 0, 1)
    second = grid[:, :, half:]

    def round_(arrays):
        outs = []
        for array, mine, axis in arrays:
            n = array.shape[0]
            acc = pick(array, mine)
            for shift in range(1, n):
                message = pick(array, (mine + shift) % n)
                acc = acc + lax.ppermute(message, "tm", ring_pairs((nx, nz), axis, shift))
            outs.append(acc)
        return outs

    a, b = round_([(first, mz, 1), (second, mx, 0)])
    a, b = round_([(a, mx, 0), (b, mz, 1)])
    return jnp.concatenate([a, b], axis=0)


def solution(mesh):
    placed = (P("chan", "tm", None), P("chan", None), P("chan", None))
    return jax.shard_map(
        shards, mesh=mesh, in_specs=placed, out_specs=P(("chan", "tm"), None), check_vma=False
    )
```

```python
import math

import jax
import jax.numpy as jnp
from jax import lax
from jax.sharding import PartitionSpec as P

NFB = 512
F0 = 64
K = 8
LAG = 128


def split_length(samples):
    if samples % 128 == 0:
        return samples // 128, 128
    best = 1
    for b in range(1, samples + 1):
        if samples % b == 0 and b * b <= samples:
            best = b
    return samples // best, best


def angle_pair(rows, cols, padded):
    phase = (rows * cols % padded).astype(jnp.float32) * (2.0 * math.pi / padded)
    return jnp.cos(phase), jnp.sin(phase)


def fourier_table_t(samples):
    padded = 2 * samples
    outer, inner = split_length(samples)
    freqs = (F0 + jnp.arange(NFB, dtype=jnp.int32))[:, None]
    ca, sa = angle_pair(freqs, jnp.arange(outer, dtype=jnp.int32)[None, :] * inner, padded)
    cb, sb = angle_pair(freqs, jnp.arange(inner, dtype=jnp.int32)[None, :], padded)
    ca, sa = ca[:, :, None], sa[:, :, None]
    cb, sb = cb[:, None, :], sb[:, None, :]
    cos_t = (ca * cb - sa * sb).reshape(NFB, samples)
    sin_t = (sa * cb + ca * sb).reshape(NFB, samples)
    return jnp.concatenate([cos_t, -sin_t], axis=0).astype(jnp.bfloat16)


def lag_table(samples):
    padded = 2 * samples
    shifts = (jnp.arange(2 * LAG + 1, dtype=jnp.int32) - LAG)[None, :]
    fine = 16
    cu, su = angle_pair((F0 + fine * jnp.arange(NFB // fine, dtype=jnp.int32))[:, None], shifts, padded)
    cv, sv = angle_pair(jnp.arange(fine, dtype=jnp.int32)[:, None], shifts, padded)
    cu, su = cu[:, None, :], su[:, None, :]
    cv, sv = cv[None, :, :], sv[None, :, :]
    cos_t = (cu * cv - su * sv).reshape(NFB, -1)
    sin_t = (su * cv + cu * sv).reshape(NFB, -1)
    return jnp.concatenate([cos_t, -sin_t], axis=0)


def whiten(rows, fourier):
    spectra = lax.dot_general(
        rows, fourier, (((2,), (1,)), ((), ())), preferred_element_type=jnp.float32
    )
    real_part = spectra[..., :NFB]
    imag_part = spectra[..., NFB:]
    energy = real_part * real_part + imag_part * imag_part
    level = jnp.mean(energy, axis=-1, keepdims=True)
    divisor = jnp.sqrt(energy + 0.1 * level + 1e-05)
    whitened = jnp.concatenate([real_part / divisor, imag_part / divisor], axis=-1)
    return whitened.astype(jnp.bfloat16)


def neighbourhood(own):
    size = lax.axis_size("chan")
    up = [(i, i + 1) for i in range(size - 1)]
    down = [(j, i) for i, j in up]
    below = lax.ppermute(own, "chan", up)
    above = lax.ppermute(own, "chan", down)
    return jnp.concatenate([below, own, above], axis=0)


def shards(record, partners, block_owner):
    block_size, windows_dev, samples = record.shape
    width = windows_dev * 2 * NFB
    fourier = fourier_table_t(samples)
    own = whiten(record, fourier).reshape(block_size, width)
    near = neighbourhood(own)

    tm_count = lax.axis_size("tm")
    per_block = block_size // tm_count
    owner_row = block_owner[0]
    onehot = (owner_row[None, :] == jnp.arange(tm_count, dtype=jnp.int32)[:, None]).astype(jnp.int32)
    inverse = jnp.sum(onehot * jnp.arange(tm_count, dtype=jnp.int32)[None, :], axis=1)
    own_sorted = jnp.take(own.reshape(tm_count, per_block, width), inverse, axis=0).reshape(block_size, 1, width)
    partners_sorted = jnp.take(partners.reshape(tm_count, per_block, K), inverse, axis=0)
    base_row = lax.axis_index("chan") * block_size - block_size
    local_rows = (partners_sorted - base_row).reshape(-1)
    far = jnp.take(near, local_rows, axis=0, mode="clip").reshape(block_size, K, width)
    own_sorted = own_sorted.reshape(block_size, 1, width)

    cross_real = 0.0
    cross_imag = 0.0
    for w in range(windows_dev):
        lo = w * 2 * NFB
        ar = own_sorted[..., lo : lo + NFB].astype(jnp.float32)
        ai = own_sorted[..., lo + NFB : lo + 2 * NFB].astype(jnp.float32)
        br = far[..., lo : lo + NFB].astype(jnp.float32)
        bi = far[..., lo + NFB : lo + 2 * NFB].astype(jnp.float32)
        cross_real = cross_real + (ar * br + ai * bi)
        cross_imag = cross_imag + (ar * bi - ai * br)
    lags = lag_table(samples)
    partial = jnp.dot(
        cross_real.reshape(-1, NFB), lags[:NFB], precision=lax.Precision.HIGH, preferred_element_type=jnp.float32
    ) + jnp.dot(
        cross_imag.reshape(-1, NFB), lags[NFB:], precision=lax.Precision.HIGH, preferred_element_type=jnp.float32
    )
    summed = scatter_sum(partial.reshape(tm_count, -1, partial.shape[-1]))
    scale = 1.0 / math.sqrt(windows_dev * tm_count * NFB)
    return summed * scale


def ring_pairs(sizes, axis, shift):
    nx, nz = sizes
    pairs = []
    for d in range(nx * nz):
        x, z = d // nz, d % nz
        if axis == 1:
            pairs.append((d, x * nz + (z + shift) % nz))
        else:
            pairs.append((d, ((x + shift) % nx) * nz + z))
    return pairs


def pick(array, index):
    return lax.dynamic_index_in_dim(array, index, 0, keepdims=False)


def scatter_sum(blocks):
    tm_count = blocks.shape[0]
    nz = 4 if tm_count % 4 == 0 else 1
    nx = tm_count // nz
    me = lax.axis_index("tm")
    mx, mz = me // nz, me % nz
    rows = blocks.shape[1]
    grid = blocks.reshape(nx, nz, rows, blocks.shape[2])
    half = rows // 2
    first = jnp.swapaxes(grid[:, :, :half], 0, 1)
    second = grid[:, :, half:]

    def round_(arrays):
        outs = []
        for array, mine, axis in arrays:
            n = array.shape[0]
            acc = pick(array, mine)
            for shift in range(1, n):
                message = pick(array, (mine + shift) % n)
                acc = acc + lax.ppermute(message, "tm", ring_pairs((nx, nz), axis, shift))
            outs.append(acc)
        return outs

    a, b = round_([(first, mz, 1), (second, mx, 0)])
    a, b = round_([(a, mx, 0), (b, mz, 1)])
    return jnp.concatenate([a, b], axis=0)


def solution(mesh):
    placed = (P("chan", "tm", None), P("chan", None), P("chan", None))
    return jax.shard_map(
        shards, mesh=mesh, in_specs=placed, out_specs=P(("chan", "tm"), None), check_vma=False
    )
```

```python
import math

import jax
import jax.numpy as jnp
from jax import lax
import functools

from jax.experimental import pallas as pl
from jax.experimental.pallas import tpu as pltpu
from jax.sharding import PartitionSpec as P

NFB = 512
F0 = 64
K = 8
LAG = 128


def split_length(samples):
    if samples % 128 == 0:
        return samples // 128, 128
    best = 1
    for b in range(1, samples + 1):
        if samples % b == 0 and b * b <= samples:
            best = b
    return samples // best, best


def angle_pair(rows, cols, padded):
    phase = (rows * cols % padded).astype(jnp.float32) * (2.0 * math.pi / padded)
    return jnp.cos(phase), jnp.sin(phase)


def fourier_table_t(samples):
    padded = 2 * samples
    outer, inner = split_length(samples)
    freqs = (F0 + jnp.arange(NFB, dtype=jnp.int32))[:, None]
    ca, sa = angle_pair(freqs, jnp.arange(outer, dtype=jnp.int32)[None, :] * inner, padded)
    cb, sb = angle_pair(freqs, jnp.arange(inner, dtype=jnp.int32)[None, :], padded)
    ca, sa = ca[:, :, None], sa[:, :, None]
    cb, sb = cb[:, None, :], sb[:, None, :]
    cos_t = (ca * cb - sa * sb).reshape(NFB, samples)
    sin_t = (sa * cb + ca * sb).reshape(NFB, samples)
    return jnp.concatenate([cos_t, -sin_t], axis=0).astype(jnp.bfloat16)


def lag_table(samples):
    padded = 2 * samples
    shifts = (jnp.arange(2 * LAG + 1, dtype=jnp.int32) - LAG)[None, :]
    fine = 16
    cu, su = angle_pair((F0 + fine * jnp.arange(NFB // fine, dtype=jnp.int32))[:, None], shifts, padded)
    cv, sv = angle_pair(jnp.arange(fine, dtype=jnp.int32)[:, None], shifts, padded)
    cu, su = cu[:, None, :], su[:, None, :]
    cv, sv = cv[None, :, :], sv[None, :, :]
    cos_t = (cu * cv - su * sv).reshape(NFB, -1)
    sin_t = (su * cv + cu * sv).reshape(NFB, -1)
    return jnp.concatenate([cos_t, -sin_t], axis=0)


def whiten(rows, fourier):
    spectra = lax.dot_general(
        rows, fourier, (((2,), (1,)), ((), ())), preferred_element_type=jnp.float32
    )
    real_part = spectra[..., :NFB]
    imag_part = spectra[..., NFB:]
    energy = real_part * real_part + imag_part * imag_part
    level = jnp.mean(energy, axis=-1, keepdims=True)
    divisor = jnp.sqrt(energy + 0.1 * level + 1e-05)
    whitened = jnp.concatenate([real_part / divisor, imag_part / divisor], axis=-1)
    return whitened.astype(jnp.bfloat16)


def neighbourhood(own):
    size = lax.axis_size("chan")
    up = [(i, i + 1) for i in range(size - 1)]
    down = [(j, i) for i, j in up]
    below = lax.ppermute(own, "chan", up)
    above = lax.ppermute(own, "chan", down)
    return jnp.concatenate([below, own, above], axis=0)


def pair_kernel(own_idx, far_idx, near_ref, lhi_ref, llo_ref, out_ref, cross_ref, *, group):
    step = pl.program_id(0)

    def channel(i, carry):
        s = step * group + i
        a = near_ref[own_idx[s]].astype(jnp.float32)
        a_swap = jnp.concatenate([-a[4:8], a[0:4], -a[12:16], a[8:12]], axis=0)
        for k in range(K):
            b = near_ref[far_idx[s * K + k]].astype(jnp.float32)
            m = a * b
            n = a_swap * b
            sm = m[0:8] + m[8:16]
            sn = n[0:8] + n[8:16]
            row = jnp.concatenate([sm[0:4] + sm[4:8], sn[0:4] + sn[4:8]], axis=0)
            cross_ref[pl.ds(pl.multiple_of((i * K + k) * 8, 8), 8), :] = row
        return carry

    lax.fori_loop(0, group, channel, 0)
    pairs = group * K
    total = None
    for r in range(8):
        slab = cross_ref[pl.ds(r, pairs, stride=8), :]
        hi = slab.astype(jnp.bfloat16)
        lo = (slab - hi.astype(jnp.float32)).astype(jnp.bfloat16)
        lh = lhi_ref[r * 128 : (r + 1) * 128, :]
        ll = llo_ref[r * 128 : (r + 1) * 128, :]
        part = (jnp.dot(hi, lh, preferred_element_type=jnp.float32)
                + jnp.dot(lo, lh, preferred_element_type=jnp.float32)
                + jnp.dot(hi, ll, preferred_element_type=jnp.float32))
        total = part if total is None else total + part
    out_ref[...] = total


def pair_lags(near, own_idx, far_idx, lag, group):
    rows, sub, lanes = near.shape
    count = own_idx.shape[0]
    nlag = lag.shape[1]
    lhi = lag.astype(jnp.bfloat16)
    llo = (lag - lhi.astype(jnp.float32)).astype(jnp.bfloat16)
    steps = count // group
    spec = pltpu.PrefetchScalarGridSpec(
        num_scalar_prefetch=2,
        grid=(steps,),
        in_specs=[
            pl.BlockSpec((rows, sub, lanes), lambda i, o, f: (0, 0, 0)),
            pl.BlockSpec(lhi.shape, lambda i, o, f: (0, 0)),
            pl.BlockSpec(llo.shape, lambda i, o, f: (0, 0)),
        ],
        out_specs=pl.BlockSpec((group * K, nlag), lambda i, o, f: (i, 0)),
        scratch_shapes=[pltpu.VMEM((group * K * 8, 128), jnp.float32)],
    )
    pairs = count * K
    cost = pl.CostEstimate(flops=pairs * 2048 * 6 + 3 * 2 * pairs * 1024 * nlag, transcendentals=0,
                           bytes_accessed=near.size * 2 + pairs * nlag * 4)
    return pl.pallas_call(
        functools.partial(pair_kernel, group=group),
        grid_spec=spec,
        out_shape=jax.ShapeDtypeStruct((pairs, nlag), jnp.float32),
        compiler_params=pltpu.CompilerParams(dimension_semantics=("arbitrary",), vmem_limit_bytes=48 * 1024 * 1024),
        cost_estimate=cost,
    )(own_idx, far_idx, near, lhi, llo)


def shards(record, partners, block_owner):
    block_size, windows_dev, samples = record.shape
    width = windows_dev * 2 * NFB
    fourier = fourier_table_t(samples)
    own = whiten(record, fourier).reshape(block_size, width // 128, 128)
    near = neighbourhood(own)

    tm_count = lax.axis_size("tm")
    per_block = block_size // tm_count
    owner_row = block_owner[0]
    onehot = (owner_row[None, :] == jnp.arange(tm_count, dtype=jnp.int32)[:, None]).astype(jnp.int32)
    inverse = jnp.sum(onehot * jnp.arange(tm_count, dtype=jnp.int32)[None, :], axis=1)
    own_idx = (block_size + inverse[:, None] * per_block + jnp.arange(per_block, dtype=jnp.int32)[None, :]).reshape(-1)
    partners_sorted = jnp.take(partners.reshape(tm_count, per_block, K), inverse, axis=0)
    base_row = lax.axis_index("chan") * block_size - block_size
    far_idx = jnp.clip(partners_sorted - base_row, 0, 3 * block_size - 1).reshape(-1)

    partial = pair_lags(near, own_idx, far_idx, lag_table(samples), per_block)
    summed = scatter_sum(partial.reshape(tm_count, -1, partial.shape[-1]))
    scale = 1.0 / math.sqrt(windows_dev * tm_count * NFB)
    return summed * scale


def ring_pairs(sizes, axis, shift):
    nx, nz = sizes
    pairs = []
    for d in range(nx * nz):
        x, z = d // nz, d % nz
        if axis == 1:
            pairs.append((d, x * nz + (z + shift) % nz))
        else:
            pairs.append((d, ((x + shift) % nx) * nz + z))
    return pairs


def pick(array, index):
    return lax.dynamic_index_in_dim(array, index, 0, keepdims=False)


def scatter_sum(blocks):
    tm_count = blocks.shape[0]
    nz = 4 if tm_count % 4 == 0 else 1
    nx = tm_count // nz
    me = lax.axis_index("tm")
    mx, mz = me // nz, me % nz
    rows = blocks.shape[1]
    grid = blocks.reshape(nx, nz, rows, blocks.shape[2])
    half = rows // 2
    first = jnp.swapaxes(grid[:, :, :half], 0, 1)
    second = grid[:, :, half:]

    def round_(arrays):
        outs = []
        for array, mine, axis in arrays:
            n = array.shape[0]
            acc = pick(array, mine)
            for shift in range(1, n):
                message = pick(array, (mine + shift) % n)
                acc = acc + lax.ppermute(message, "tm", ring_pairs((nx, nz), axis, shift))
            outs.append(acc)
        return outs

    a, b = round_([(first, mz, 1), (second, mx, 0)])
    a, b = round_([(a, mx, 0), (b, mz, 1)])
    return jnp.concatenate([a, b], axis=0)


def solution(mesh):
    placed = (P("chan", "tm", None), P("chan", None), P("chan", None))
    return jax.shard_map(
        shards, mesh=mesh, in_specs=placed, out_specs=P(("chan", "tm"), None), check_vma=False
    )
```

```python
import math

import jax
import jax.numpy as jnp
from jax import lax
import functools

from jax.experimental import pallas as pl
from jax.experimental.pallas import tpu as pltpu
from jax.sharding import PartitionSpec as P

NFB = 512
F0 = 64
K = 8
LAG = 128


def split_length(samples):
    if samples % 128 == 0:
        return samples // 128, 128
    best = 1
    for b in range(1, samples + 1):
        if samples % b == 0 and b * b <= samples:
            best = b
    return samples // best, best


def angle_pair(rows, cols, padded):
    phase = (rows * cols % padded).astype(jnp.float32) * (2.0 * math.pi / padded)
    return jnp.cos(phase), jnp.sin(phase)


def fourier_table_t(samples):
    padded = 2 * samples
    outer, inner = split_length(samples)
    freqs = (F0 + jnp.arange(NFB, dtype=jnp.int32))[:, None]
    ca, sa = angle_pair(freqs, jnp.arange(outer, dtype=jnp.int32)[None, :] * inner, padded)
    cb, sb = angle_pair(freqs, jnp.arange(inner, dtype=jnp.int32)[None, :], padded)
    ca, sa = ca[:, :, None], sa[:, :, None]
    cb, sb = cb[:, None, :], sb[:, None, :]
    cos_t = (ca * cb - sa * sb).reshape(NFB, samples)
    sin_t = (sa * cb + ca * sb).reshape(NFB, samples)
    return jnp.concatenate([cos_t, -sin_t], axis=0).astype(jnp.bfloat16)


def lag_table(samples):
    padded = 2 * samples
    shifts = (jnp.arange(2 * LAG + 1, dtype=jnp.int32) - LAG)[None, :]
    fine = 16
    cu, su = angle_pair((F0 + fine * jnp.arange(NFB // fine, dtype=jnp.int32))[:, None], shifts, padded)
    cv, sv = angle_pair(jnp.arange(fine, dtype=jnp.int32)[:, None], shifts, padded)
    cu, su = cu[:, None, :], su[:, None, :]
    cv, sv = cv[None, :, :], sv[None, :, :]
    cos_t = (cu * cv - su * sv).reshape(NFB, -1)
    sin_t = (su * cv + cu * sv).reshape(NFB, -1)
    return jnp.concatenate([cos_t, -sin_t], axis=0)


def whiten(rows, fourier):
    spectra = lax.dot_general(
        rows, fourier, (((2,), (1,)), ((), ())), preferred_element_type=jnp.float32
    )
    real_part = spectra[..., :NFB]
    imag_part = spectra[..., NFB:]
    energy = real_part * real_part + imag_part * imag_part
    level = jnp.mean(energy, axis=-1, keepdims=True)
    divisor = jnp.sqrt(energy + 0.1 * level + 1e-05)
    whitened = jnp.concatenate([real_part / divisor, imag_part / divisor], axis=-1)
    return whitened.astype(jnp.bfloat16)


def neighbourhood(own):
    size = lax.axis_size("chan")
    up = [(i, i + 1) for i in range(size - 1)]
    down = [(j, i) for i, j in up]
    below = lax.ppermute(own, "chan", up)
    above = lax.ppermute(own, "chan", down)
    return below, own, above


def pair_kernel(own_idx, far_idx, below_ref, mid_ref, above_ref, lag_ref, out_ref,
                near_ref, lhi_ref, llo_ref, cross_ref, sems, *, group):
    step = pl.program_id(0)
    block = mid_ref.shape[0]

    @pl.when(step == 0)
    def _():
        copies = [
            pltpu.make_async_copy(src, near_ref.at[pl.ds(j * block, block)], sems.at[j])
            for j, src in enumerate((below_ref, mid_ref, above_ref))
        ]
        for c in copies:
            c.start()
        lag = lag_ref[...]
        hi = lag.astype(jnp.bfloat16)
        lhi_ref[...] = hi
        llo_ref[...] = (lag - hi.astype(jnp.float32)).astype(jnp.bfloat16)
        for c in copies:
            c.wait()

    def channel(i, carry):
        s = step * group + i
        a = near_ref[own_idx[s]].astype(jnp.float32)
        a_swap = jnp.concatenate([-a[4:8], a[0:4], -a[12:16], a[8:12]], axis=0)
        for k in range(K):
            b = near_ref[far_idx[s * K + k]].astype(jnp.float32)
            m = a * b
            n = a_swap * b
            sm = m[0:8] + m[8:16]
            sn = n[0:8] + n[8:16]
            row = jnp.concatenate([sm[0:4] + sm[4:8], sn[0:4] + sn[4:8]], axis=0)
            cross_ref[pl.ds(pl.multiple_of((i * K + k) * 8, 8), 8), :] = row
        return carry

    lax.fori_loop(0, group, channel, 0)
    pairs = group * K
    total = None
    for r in range(8):
        slab = cross_ref[pl.ds(r, pairs, stride=8), :]
        hi = slab.astype(jnp.bfloat16)
        lo = (slab - hi.astype(jnp.float32)).astype(jnp.bfloat16)
        lh = lhi_ref[r * 128 : (r + 1) * 128, :]
        ll = llo_ref[r * 128 : (r + 1) * 128, :]
        part = (jnp.dot(hi, lh, preferred_element_type=jnp.float32)
                + jnp.dot(lo, lh, preferred_element_type=jnp.float32)
                + jnp.dot(hi, ll, preferred_element_type=jnp.float32))
        total = part if total is None else total + part
    out_ref[...] = total


def pair_lags(blocks, own_idx, far_idx, lag, group):
    rows, sub, lanes = blocks[1].shape
    count = own_idx.shape[0]
    nlag = lag.shape[1]
    steps = count // group
    hbm = pl.BlockSpec(memory_space=pl.ANY)
    spec = pltpu.PrefetchScalarGridSpec(
        num_scalar_prefetch=2,
        grid=(steps,),
        in_specs=[hbm, hbm, hbm, pl.BlockSpec(lag.shape, lambda i, o, f: (0, 0))],
        out_specs=pl.BlockSpec((group * K, nlag), lambda i, o, f: (i, 0)),
        scratch_shapes=[
            pltpu.VMEM((3 * rows, sub, lanes), jnp.bfloat16),
            pltpu.VMEM(lag.shape, jnp.bfloat16),
            pltpu.VMEM(lag.shape, jnp.bfloat16),
            pltpu.VMEM((group * K * 8, 128), jnp.float32),
            pltpu.SemaphoreType.DMA((3,)),
        ],
    )
    pairs = count * K
    cost = pl.CostEstimate(flops=pairs * 2048 * 6 + 3 * 2 * pairs * 1024 * nlag, transcendentals=0,
                           bytes_accessed=3 * rows * sub * lanes * 2 + pairs * nlag * 4)
    return pl.pallas_call(
        functools.partial(pair_kernel, group=group),
        grid_spec=spec,
        out_shape=jax.ShapeDtypeStruct((pairs, nlag), jnp.float32),
        compiler_params=pltpu.CompilerParams(dimension_semantics=("arbitrary",), vmem_limit_bytes=48 * 1024 * 1024),
        cost_estimate=cost,
    )(own_idx, far_idx, *blocks, lag)


def shards(record, partners, block_owner):
    block_size, windows_dev, samples = record.shape
    width = windows_dev * 2 * NFB
    fourier = fourier_table_t(samples)
    own = whiten(record, fourier).reshape(block_size, width // 128, 128)
    near = neighbourhood(own)

    tm_count = lax.axis_size("tm")
    per_block = block_size // tm_count
    owner_row = block_owner[0]
    onehot = (owner_row[None, :] == jnp.arange(tm_count, dtype=jnp.int32)[:, None]).astype(jnp.int32)
    inverse = jnp.sum(onehot * jnp.arange(tm_count, dtype=jnp.int32)[None, :], axis=1)
    own_idx = (block_size + inverse[:, None] * per_block + jnp.arange(per_block, dtype=jnp.int32)[None, :]).reshape(-1)
    partners_sorted = jnp.take(partners.reshape(tm_count, per_block, K), inverse, axis=0)
    base_row = lax.axis_index("chan") * block_size - block_size
    far_idx = jnp.clip(partners_sorted - base_row, 0, 3 * block_size - 1).reshape(-1)

    partial = pair_lags(near, own_idx, far_idx, lag_table(samples), per_block)
    summed = scatter_sum(partial.reshape(tm_count, -1, partial.shape[-1]))
    scale = 1.0 / math.sqrt(windows_dev * tm_count * NFB)
    return summed * scale


def ring_pairs(sizes, axis, shift):
    nx, nz = sizes
    pairs = []
    for d in range(nx * nz):
        x, z = d // nz, d % nz
        if axis == 1:
            pairs.append((d, x * nz + (z + shift) % nz))
        else:
            pairs.append((d, ((x + shift) % nx) * nz + z))
    return pairs


def pick(array, index):
    return lax.dynamic_index_in_dim(array, index, 0, keepdims=False)


def scatter_sum(blocks):
    tm_count = blocks.shape[0]
    nz = 4 if tm_count % 4 == 0 else 1
    nx = tm_count // nz
    me = lax.axis_index("tm")
    mx, mz = me // nz, me % nz
    rows = blocks.shape[1]
    grid = blocks.reshape(nx, nz, rows, blocks.shape[2])
    half = rows // 2
    first = jnp.swapaxes(grid[:, :, :half], 0, 1)
    second = grid[:, :, half:]

    def round_(arrays):
        outs = []
        for array, mine, axis in arrays:
            n = array.shape[0]
            acc = pick(array, mine)
            for shift in range(1, n):
                message = pick(array, (mine + shift) % n)
                acc = acc + lax.ppermute(message, "tm", ring_pairs((nx, nz), axis, shift))
            outs.append(acc)
        return outs

    a, b = round_([(first, mz, 1), (second, mx, 0)])
    a, b = round_([(a, mx, 0), (b, mz, 1)])
    return jnp.concatenate([a, b], axis=0)


def solution(mesh):
    placed = (P("chan", "tm", None), P("chan", None), P("chan", None))
    return jax.shard_map(
        shards, mesh=mesh, in_specs=placed, out_specs=P(("chan", "tm"), None), check_vma=False
    )
```

```python
import math

import jax
import jax.numpy as jnp
from jax import lax
import functools

from jax.experimental import pallas as pl
from jax.experimental.pallas import tpu as pltpu
from jax.sharding import PartitionSpec as P

NFB = 512
F0 = 64
K = 8
LAG = 128


def split_length(samples):
    if samples % 128 == 0:
        return samples // 128, 128
    best = 1
    for b in range(1, samples + 1):
        if samples % b == 0 and b * b <= samples:
            best = b
    return samples // best, best


def angle_pair(rows, cols, padded):
    phase = (rows * cols % padded).astype(jnp.float32) * (2.0 * math.pi / padded)
    return jnp.cos(phase), jnp.sin(phase)


def fourier_table_t(samples):
    padded = 2 * samples
    outer, inner = split_length(samples)
    freqs = (F0 + jnp.arange(NFB, dtype=jnp.int32))[:, None]
    ca, sa = angle_pair(freqs, jnp.arange(outer, dtype=jnp.int32)[None, :] * inner, padded)
    cb, sb = angle_pair(freqs, jnp.arange(inner, dtype=jnp.int32)[None, :], padded)
    ca, sa = ca[:, :, None], sa[:, :, None]
    cb, sb = cb[:, None, :], sb[:, None, :]
    cos_t = (ca * cb - sa * sb).reshape(NFB, samples)
    sin_t = (sa * cb + ca * sb).reshape(NFB, samples)
    return jnp.concatenate([cos_t, -sin_t], axis=0).astype(jnp.bfloat16)


def lag_table(samples):
    padded = 2 * samples
    shifts = (jnp.arange(2 * LAG + 1, dtype=jnp.int32) - LAG)[None, :]
    fine = 16
    cu, su = angle_pair((F0 + fine * jnp.arange(NFB // fine, dtype=jnp.int32))[:, None], shifts, padded)
    cv, sv = angle_pair(jnp.arange(fine, dtype=jnp.int32)[:, None], shifts, padded)
    cu, su = cu[:, None, :], su[:, None, :]
    cv, sv = cv[None, :, :], sv[None, :, :]
    cos_t = (cu * cv - su * sv).reshape(NFB, -1)
    sin_t = (su * cv + cu * sv).reshape(NFB, -1)
    return jnp.concatenate([cos_t, -sin_t], axis=0)


def whiten(rows, fourier):
    spectra = lax.dot_general(
        rows, fourier, (((2,), (1,)), ((), ())), preferred_element_type=jnp.float32
    )
    real_part = spectra[..., :NFB]
    imag_part = spectra[..., NFB:]
    energy = real_part * real_part + imag_part * imag_part
    level = jnp.mean(energy, axis=-1, keepdims=True)
    divisor = jnp.sqrt(energy + 0.1 * level + 1e-05)
    whitened = jnp.concatenate([real_part / divisor, imag_part / divisor], axis=-1)
    return whitened.astype(jnp.bfloat16)


def neighbourhood(own):
    size = lax.axis_size("chan")
    up = [(i, i + 1) for i in range(size - 1)]
    down = [(j, i) for i, j in up]
    below = lax.ppermute(own, "chan", up)
    above = lax.ppermute(own, "chan", down)
    return below, own, above


def pair_kernel(own_idx, far_idx, below_ref, mid_ref, above_ref, lag_ref, out_ref,
                near_ref, lhi_ref, llo_ref, cross_ref, sems, *, group):
    step = pl.program_id(0)
    block = mid_ref.shape[0]

    @pl.when(step == 0)
    def _():
        copies = [
            pltpu.make_async_copy(src, near_ref.at[pl.ds(j * block, block)], sems.at[j])
            for j, src in enumerate((below_ref, mid_ref, above_ref))
        ]
        for c in copies:
            c.start()
        lag = lag_ref[...]
        hi = lag.astype(jnp.bfloat16)
        lhi_ref[...] = hi
        llo_ref[...] = (lag - hi.astype(jnp.float32)).astype(jnp.bfloat16)
        for c in copies:
            c.wait()

    def channel(i, carry):
        s = step * group + i
        a = near_ref[own_idx[s]].astype(jnp.float32)
        a_swap = jnp.concatenate([-a[4:8], a[0:4], -a[12:16], a[8:12]], axis=0)
        for k in range(K):
            b = near_ref[far_idx[s * K + k]].astype(jnp.float32)
            m = a * b
            n = a_swap * b
            sm = m[0:8] + m[8:16]
            sn = n[0:8] + n[8:16]
            row = jnp.concatenate([sm[0:4] + sm[4:8], sn[0:4] + sn[4:8]], axis=0)
            cross_ref[pl.ds(pl.multiple_of((i * K + k) * 8, 8), 8), :] = row
        return carry

    lax.fori_loop(0, group, channel, 0)
    pairs = group * K
    half = 4
    sums = []
    for part_rows in (range(0, half), range(half, 8)):
        total = None
        for r in part_rows:
            slab = cross_ref[pl.ds(r, pairs, stride=8), :]
            hi = slab.astype(jnp.bfloat16)
            lo = (slab - hi.astype(jnp.float32)).astype(jnp.bfloat16)
            lh = lhi_ref[r * 128 : (r + 1) * 128, :]
            ll = llo_ref[r * 128 : (r + 1) * 128, :]
            part = (jnp.dot(hi, lh, preferred_element_type=jnp.float32)
                    + jnp.dot(lo, lh, preferred_element_type=jnp.float32)
                    + jnp.dot(hi, ll, preferred_element_type=jnp.float32))
            total = part if total is None else total + part
        sums.append(total)
    wide = lhi_ref.shape[1]
    out_ref[:, :wide] = sums[0] + sums[1]
    out_ref[:, wide:] = sums[0][:, 0:1] - sums[1][:, 0:1]


def pair_lags(blocks, own_idx, far_idx, lag, group):
    rows, sub, lanes = blocks[1].shape
    count = own_idx.shape[0]
    nlag = lag.shape[1]
    lag = lag[:, : nlag - 1]
    steps = count // group
    hbm = pl.BlockSpec(memory_space=pl.ANY)
    spec = pltpu.PrefetchScalarGridSpec(
        num_scalar_prefetch=2,
        grid=(steps,),
        in_specs=[hbm, hbm, hbm, pl.BlockSpec(lag.shape, lambda i, o, f: (0, 0))],
        out_specs=pl.BlockSpec((group * K, nlag), lambda i, o, f: (i, 0)),
        scratch_shapes=[
            pltpu.VMEM((3 * rows, sub, lanes), jnp.bfloat16),
            pltpu.VMEM(lag.shape, jnp.bfloat16),
            pltpu.VMEM(lag.shape, jnp.bfloat16),
            pltpu.VMEM((group * K * 8, 128), jnp.float32),
            pltpu.SemaphoreType.DMA((3,)),
        ],
    )
    pairs = count * K
    cost = pl.CostEstimate(flops=pairs * 2048 * 6 + 3 * 2 * pairs * 1024 * (nlag - 1), transcendentals=0,
                           bytes_accessed=3 * rows * sub * lanes * 2 + pairs * nlag * 4)
    return pl.pallas_call(
        functools.partial(pair_kernel, group=group),
        grid_spec=spec,
        out_shape=jax.ShapeDtypeStruct((pairs, nlag), jnp.float32),
        compiler_params=pltpu.CompilerParams(dimension_semantics=("arbitrary",), vmem_limit_bytes=48 * 1024 * 1024),
        cost_estimate=cost,
    )(own_idx, far_idx, *blocks, lag)


def shards(record, partners, block_owner):
    block_size, windows_dev, samples = record.shape
    width = windows_dev * 2 * NFB
    fourier = fourier_table_t(samples)
    own = whiten(record, fourier).reshape(block_size, width // 128, 128)
    near = neighbourhood(own)

    tm_count = lax.axis_size("tm")
    per_block = block_size // tm_count
    owner_row = block_owner[0]
    onehot = (owner_row[None, :] == jnp.arange(tm_count, dtype=jnp.int32)[:, None]).astype(jnp.int32)
    inverse = jnp.sum(onehot * jnp.arange(tm_count, dtype=jnp.int32)[None, :], axis=1)
    nz = 4 if tm_count % 4 == 0 else 1
    nx = tm_count // nz
    half = per_block // 2
    zx = jnp.arange(nz, dtype=jnp.int32)[:, None] + nz * jnp.arange(nx, dtype=jnp.int32)[None, :]
    xz = nz * jnp.arange(nx, dtype=jnp.int32)[:, None] + jnp.arange(nz, dtype=jnp.int32)[None, :]
    dest = jnp.stack([zx.reshape(-1), xz.reshape(-1)])
    first = inverse[dest] * per_block + jnp.arange(2, dtype=jnp.int32)[:, None] * half
    chan_local = (first[:, :, None] + jnp.arange(half, dtype=jnp.int32)[None, None, :]).reshape(-1)
    own_idx = block_size + chan_local
    base_row = lax.axis_index("chan") * block_size - block_size
    far_idx = jnp.clip(jnp.take(partners, chan_local, axis=0) - base_row, 0, 3 * block_size - 1).reshape(-1)

    partial = pair_lags(near, own_idx, far_idx, lag_table(samples), half)
    summed = scatter_sum(partial.reshape(2, nz, nx, half * K, partial.shape[-1]), nx, nz)
    scale = 1.0 / math.sqrt(windows_dev * tm_count * NFB)
    return summed * scale


def ring_pairs(sizes, axis, shift):
    nx, nz = sizes
    pairs = []
    for d in range(nx * nz):
        x, z = d // nz, d % nz
        if axis == 1:
            pairs.append((d, x * nz + (z + shift) % nz))
        else:
            pairs.append((d, ((x + shift) % nx) * nz + z))
    return pairs


def pick(array, index):
    return lax.dynamic_index_in_dim(array, index, 0, keepdims=False)


def scatter_sum(blocks, nx, nz):
    me = lax.axis_index("tm")
    mx, mz = me // nz, me % nz

    def round_(arrays):
        outs = []
        for array, mine, axis in arrays:
            n = array.shape[0]
            acc = pick(array, mine)
            for shift in range(1, n):
                message = pick(array, (mine + shift) % n)
                acc = acc + lax.ppermute(message, "tm", ring_pairs((nx, nz), axis, shift))
            outs.append(acc)
        return outs

    a, b = round_([(blocks[0], mz, 1), (blocks[1], mx, 0)])
    a, b = round_([(a, mx, 0), (b, mz, 1)])
    return jnp.concatenate([a, b], axis=0)


def solution(mesh):
    placed = (P("chan", "tm", None), P("chan", None), P("chan", None))
    return jax.shard_map(
        shards, mesh=mesh, in_specs=placed, out_specs=P(("chan", "tm"), None), check_vma=False
    )
```

```python
import math

import jax
import jax.numpy as jnp
from jax import lax
import functools

from jax.experimental import pallas as pl
from jax.experimental.pallas import tpu as pltpu
from jax.sharding import PartitionSpec as P

NFB = 512
F0 = 64
K = 8
LAG = 128


def split_length(samples):
    if samples % 128 == 0:
        return samples // 128, 128
    best = 1
    for b in range(1, samples + 1):
        if samples % b == 0 and b * b <= samples:
            best = b
    return samples // best, best


def angle_pair(rows, cols, padded):
    phase = (rows * cols % padded).astype(jnp.float32) * (2.0 * math.pi / padded)
    return jnp.cos(phase), jnp.sin(phase)


def fourier_table_t(samples):
    padded = 2 * samples
    outer, inner = split_length(samples)
    freqs = (F0 + jnp.arange(NFB, dtype=jnp.int32))[:, None]
    ca, sa = angle_pair(freqs, jnp.arange(outer, dtype=jnp.int32)[None, :] * inner, padded)
    cb, sb = angle_pair(freqs, jnp.arange(inner, dtype=jnp.int32)[None, :], padded)
    ca, sa = ca[:, :, None], sa[:, :, None]
    cb, sb = cb[:, None, :], sb[:, None, :]
    cos_t = (ca * cb - sa * sb).reshape(NFB, samples)
    sin_t = (sa * cb + ca * sb).reshape(NFB, samples)
    return jnp.concatenate([cos_t, -sin_t], axis=0).astype(jnp.bfloat16)


def lag_table(samples):
    padded = 2 * samples
    shifts = (jnp.arange(2 * LAG + 1, dtype=jnp.int32) - LAG)[None, :]
    fine = 16
    cu, su = angle_pair((F0 + fine * jnp.arange(NFB // fine, dtype=jnp.int32))[:, None], shifts, padded)
    cv, sv = angle_pair(jnp.arange(fine, dtype=jnp.int32)[:, None], shifts, padded)
    cu, su = cu[:, None, :], su[:, None, :]
    cv, sv = cv[None, :, :], sv[None, :, :]
    cos_t = (cu * cv - su * sv).reshape(NFB, -1)
    sin_t = (su * cv + cu * sv).reshape(NFB, -1)
    return jnp.concatenate([cos_t, -sin_t], axis=0)


def whiten(rows, fourier):
    spectra = lax.dot_general(
        rows, fourier, (((2,), (1,)), ((), ())), preferred_element_type=jnp.float32
    )
    real_part = spectra[..., :NFB]
    imag_part = spectra[..., NFB:]
    energy = real_part * real_part + imag_part * imag_part
    level = jnp.mean(energy, axis=-1, keepdims=True)
    divisor = jnp.sqrt(energy + 0.1 * level + 1e-05)
    whitened = jnp.concatenate([real_part / divisor, imag_part / divisor], axis=-1)
    return whitened.astype(jnp.bfloat16)


def neighbourhood(own):
    size = lax.axis_size("chan")
    up = [(i, i + 1) for i in range(size - 1)]
    down = [(j, i) for i, j in up]
    below = lax.ppermute(own, "chan", up)
    above = lax.ppermute(own, "chan", down)
    return below, own, above


def pair_kernel(own_idx, far_idx, below_ref, mid_ref, above_ref, lag_ref, out_ref,
                near_ref, lhi_ref, llo_ref, cross_ref, sems, *, group):
    step = pl.program_id(0)
    block = mid_ref.shape[0]

    @pl.when(step == 0)
    def _():
        copies = [
            pltpu.make_async_copy(src, near_ref.at[pl.ds(j * block, block)], sems.at[j])
            for j, src in enumerate((below_ref, mid_ref, above_ref))
        ]
        for c in copies:
            c.start()
        lag = lag_ref[...]
        hi = lag.astype(jnp.bfloat16)
        lhi_ref[...] = hi
        llo_ref[...] = (lag - hi.astype(jnp.float32)).astype(jnp.bfloat16)
        for c in copies:
            c.wait()

    def channel(i, carry):
        s = step * group + i
        a = near_ref[own_idx[s]].astype(jnp.float32)
        a_swap = jnp.concatenate([-a[4:8], a[0:4], -a[12:16], a[8:12]], axis=0)
        for k in range(K):
            b = near_ref[far_idx[s * K + k]].astype(jnp.float32)
            m = a * b
            n = a_swap * b
            sm = m[0:8] + m[8:16]
            sn = n[0:8] + n[8:16]
            row = jnp.concatenate([sm[0:4] + sm[4:8], sn[0:4] + sn[4:8]], axis=0)
            cross_ref[pl.ds(pl.multiple_of((i * K + k) * 8, 8), 8), :] = row
        return carry

    lax.fori_loop(0, group, channel, 0)
    pairs = group * K
    half = 4
    sums = []
    for part_rows in (range(0, half), range(half, 8)):
        total = None
        for r in part_rows:
            slab = cross_ref[pl.ds(r, pairs, stride=8), :]
            hi = slab.astype(jnp.bfloat16)
            lo = (slab - hi.astype(jnp.float32)).astype(jnp.bfloat16)
            lh = lhi_ref[:, r * 128 : (r + 1) * 128]
            ll = llo_ref[:, r * 128 : (r + 1) * 128]
            part = (nt_dot(lh, hi) + nt_dot(lh, lo) + nt_dot(ll, hi))
            total = part if total is None else total + part
        sums.append(total)
    wide = lhi_ref.shape[0]
    out_ref[:wide, :] = sums[0] + sums[1]
    out_ref[wide:, :] = sums[0][0:1, :] - sums[1][0:1, :]


def nt_dot(a, b):
    return lax.dot_general(a, b, (((1,), (1,)), ((), ())), preferred_element_type=jnp.float32)


def pair_lags(blocks, own_idx, far_idx, lag, group):
    rows, sub, lanes = blocks[1].shape
    count = own_idx.shape[0]
    nlag = lag.shape[1]
    lag = lag[:, : nlag - 1].T
    steps = count // group
    hbm = pl.BlockSpec(memory_space=pl.ANY)
    spec = pltpu.PrefetchScalarGridSpec(
        num_scalar_prefetch=2,
        grid=(steps,),
        in_specs=[hbm, hbm, hbm, pl.BlockSpec(lag.shape, lambda i, o, f: (0, 0))],
        out_specs=pl.BlockSpec((nlag, group * K), lambda i, o, f: (0, i)),
        scratch_shapes=[
            pltpu.VMEM((3 * rows, sub, lanes), jnp.bfloat16),
            pltpu.VMEM(lag.shape, jnp.bfloat16),
            pltpu.VMEM(lag.shape, jnp.bfloat16),
            pltpu.VMEM((group * K * 8, 128), jnp.float32),
            pltpu.SemaphoreType.DMA((3,)),
        ],
    )
    pairs = count * K
    cost = pl.CostEstimate(flops=pairs * 2048 * 6 + 3 * 2 * pairs * 1024 * (nlag - 1), transcendentals=0,
                           bytes_accessed=3 * rows * sub * lanes * 2 + pairs * nlag * 4)
    return pl.pallas_call(
        functools.partial(pair_kernel, group=group),
        grid_spec=spec,
        out_shape=jax.ShapeDtypeStruct((nlag, pairs), jnp.float32),
        compiler_params=pltpu.CompilerParams(dimension_semantics=("arbitrary",), vmem_limit_bytes=48 * 1024 * 1024),
        cost_estimate=cost,
    )(own_idx, far_idx, *blocks, lag)


def shards(record, partners, block_owner):
    block_size, windows_dev, samples = record.shape
    width = windows_dev * 2 * NFB
    fourier = fourier_table_t(samples)
    own = whiten(record, fourier).reshape(block_size, width // 128, 128)
    near = neighbourhood(own)

    tm_count = lax.axis_size("tm")
    per_block = block_size // tm_count
    owner_row = block_owner[0]
    onehot = (owner_row[None, :] == jnp.arange(tm_count, dtype=jnp.int32)[:, None]).astype(jnp.int32)
    inverse = jnp.sum(onehot * jnp.arange(tm_count, dtype=jnp.int32)[None, :], axis=1)
    nz = 4 if tm_count % 4 == 0 else 1
    nx = tm_count // nz
    half = per_block // 2
    zx = jnp.arange(nz, dtype=jnp.int32)[:, None] + nz * jnp.arange(nx, dtype=jnp.int32)[None, :]
    xz = nz * jnp.arange(nx, dtype=jnp.int32)[:, None] + jnp.arange(nz, dtype=jnp.int32)[None, :]
    dest = jnp.stack([zx.reshape(-1), xz.reshape(-1)])
    first = inverse[dest] * per_block + jnp.arange(2, dtype=jnp.int32)[:, None] * half
    chan_local = (first[:, :, None] + jnp.arange(half, dtype=jnp.int32)[None, None, :]).reshape(-1)
    own_idx = block_size + chan_local
    base_row = lax.axis_index("chan") * block_size - block_size
    far_idx = jnp.clip(jnp.take(partners, chan_local, axis=0) - base_row, 0, 3 * block_size - 1).reshape(-1)

    partial = pair_lags(near, own_idx, far_idx, lag_table(samples), half)
    summed = scatter_sum(partial, nx, nz, half * K)
    scale = 1.0 / math.sqrt(windows_dev * tm_count * NFB)
    return summed.T * scale


def ring_pairs(sizes, axis, shift):
    nx, nz = sizes
    pairs = []
    for d in range(nx * nz):
        x, z = d // nz, d % nz
        if axis == 1:
            pairs.append((d, x * nz + (z + shift) % nz))
        else:
            pairs.append((d, ((x + shift) % nx) * nz + z))
    return pairs


def pick(array, index, width):
    return lax.dynamic_slice_in_dim(array, index * width, width, axis=1)


def scatter_sum(lags, nx, nz, width):
    me = lax.axis_index("tm")
    mx, mz = me // nz, me % nz
    span = nx * nz * width

    def round_(arrays):
        outs = []
        for array, mine, axis, n, size in arrays:
            acc = pick(array, mine, size)
            for shift in range(1, n):
                message = pick(array, (mine + shift) % n, size)
                acc = acc + lax.ppermute(message, "tm", ring_pairs((nx, nz), axis, shift))
            outs.append(acc)
        return outs

    a, b = round_([(lags[:, :span], mz, 1, nz, nx * width), (lags[:, span:], mx, 0, nx, nz * width)])
    a, b = round_([(a, mx, 0, nx, width), (b, mz, 1, nz, width)])
    return jnp.concatenate([a, b], axis=1)


def solution(mesh):
    placed = (P("chan", "tm", None), P("chan", None), P("chan", None))
    return jax.shard_map(
        shards, mesh=mesh, in_specs=placed, out_specs=P(("chan", "tm"), None), check_vma=False
    )
```

```python
import math

import jax
import jax.numpy as jnp
from jax import lax
import functools

from jax.experimental import pallas as pl
from jax.experimental.pallas import tpu as pltpu
from jax.sharding import PartitionSpec as P

NFB = 512
F0 = 64
K = 8
LAG = 128


def split_length(samples):
    if samples % 128 == 0:
        return samples // 128, 128
    best = 1
    for b in range(1, samples + 1):
        if samples % b == 0 and b * b <= samples:
            best = b
    return samples // best, best


def angle_pair(rows, cols, padded):
    phase = (rows * cols % padded).astype(jnp.float32) * (2.0 * math.pi / padded)
    return jnp.cos(phase), jnp.sin(phase)


def fourier_table_t(samples):
    padded = 2 * samples
    outer, inner = split_length(samples)
    freqs = (F0 + jnp.arange(NFB, dtype=jnp.int32))[:, None]
    ca, sa = angle_pair(freqs, jnp.arange(outer, dtype=jnp.int32)[None, :] * inner, padded)
    cb, sb = angle_pair(freqs, jnp.arange(inner, dtype=jnp.int32)[None, :], padded)
    ca, sa = ca[:, :, None], sa[:, :, None]
    cb, sb = cb[:, None, :], sb[:, None, :]
    cos_t = (ca * cb - sa * sb).reshape(NFB, samples)
    sin_t = (sa * cb + ca * sb).reshape(NFB, samples)
    return cos_t.astype(jnp.bfloat16), (-sin_t).astype(jnp.bfloat16)


def lag_table(samples):
    padded = 2 * samples
    shifts = (jnp.arange(2 * LAG + 1, dtype=jnp.int32) - LAG)[None, :]
    fine = 16
    cu, su = angle_pair((F0 + fine * jnp.arange(NFB // fine, dtype=jnp.int32))[:, None], shifts, padded)
    cv, sv = angle_pair(jnp.arange(fine, dtype=jnp.int32)[:, None], shifts, padded)
    cu, su = cu[:, None, :], su[:, None, :]
    cv, sv = cv[None, :, :], sv[None, :, :]
    cos_t = (cu * cv - su * sv).reshape(NFB, -1)
    sin_t = (su * cv + cu * sv).reshape(NFB, -1)
    return jnp.concatenate([cos_t, -sin_t], axis=0)


def whiten(rows, fourier):
    real_part, imag_part = (
        lax.dot_general(rows, table, (((2,), (1,)), ((), ())), preferred_element_type=jnp.float32)
        for table in fourier
    )
    energy = real_part * real_part + imag_part * imag_part
    level = jnp.mean(energy, axis=-1, keepdims=True)
    divisor = jnp.sqrt(energy + 0.1 * level + 1e-05)
    whitened = jnp.concatenate([real_part / divisor, imag_part / divisor], axis=-1)
    return whitened.astype(jnp.bfloat16)


def neighbourhood(own):
    size = lax.axis_size("chan")
    up = [(i, i + 1) for i in range(size - 1)]
    down = [(j, i) for i, j in up]
    below = lax.ppermute(own, "chan", up)
    above = lax.ppermute(own, "chan", down)
    return below, own, above


def pair_kernel(own_idx, far_idx, below_ref, mid_ref, above_ref, lag_ref, out_ref,
                near_ref, lhi_ref, llo_ref, cross_ref, sems, *, group):
    step = pl.program_id(0)
    block = mid_ref.shape[0]

    @pl.when(step == 0)
    def _():
        copies = [
            pltpu.make_async_copy(src, near_ref.at[pl.ds(j * block, block)], sems.at[j])
            for j, src in enumerate((below_ref, mid_ref, above_ref))
        ]
        for c in copies:
            c.start()
        lag = lag_ref[...]
        hi = lag.astype(jnp.bfloat16)
        lhi_ref[...] = hi
        llo_ref[...] = (lag - hi.astype(jnp.float32)).astype(jnp.bfloat16)
        for c in copies:
            c.wait()

    def channel(i, carry):
        s = step * group + i
        a = near_ref[own_idx[s]].astype(jnp.float32)
        a_swap = jnp.concatenate([-a[4:8], a[0:4], -a[12:16], a[8:12]], axis=0)
        for k in range(K):
            b = near_ref[far_idx[s * K + k]].astype(jnp.float32)
            m = a * b
            n = a_swap * b
            sm = m[0:8] + m[8:16]
            sn = n[0:8] + n[8:16]
            row = jnp.concatenate([sm[0:4] + sm[4:8], sn[0:4] + sn[4:8]], axis=0)
            cross_ref[pl.ds(pl.multiple_of((i * K + k) * 8, 8), 8), :] = row
        return carry

    lax.fori_loop(0, group, channel, 0)
    pairs = group * K
    half = 4
    sums = []
    for part_rows in (range(0, half), range(half, 8)):
        total = None
        for r in part_rows:
            slab = cross_ref[pl.ds(r, pairs, stride=8), :]
            hi = slab.astype(jnp.bfloat16)
            lo = (slab - hi.astype(jnp.float32)).astype(jnp.bfloat16)
            lh = lhi_ref[:, r * 128 : (r + 1) * 128]
            ll = llo_ref[:, r * 128 : (r + 1) * 128]
            part = (nt_dot(lh, hi) + nt_dot(lh, lo) + nt_dot(ll, hi))
            total = part if total is None else total + part
        sums.append(total)
    wide = lhi_ref.shape[0]
    out_ref[:wide, :] = sums[0] + sums[1]
    out_ref[wide:, :] = sums[0][0:1, :] - sums[1][0:1, :]


def nt_dot(a, b):
    return lax.dot_general(a, b, (((1,), (1,)), ((), ())), preferred_element_type=jnp.float32)


def pair_lags(blocks, own_idx, far_idx, lag, group):
    rows, sub, lanes = blocks[1].shape
    count = own_idx.shape[0]
    nlag = lag.shape[1]
    lag = lag[:, : nlag - 1].T
    steps = count // group
    hbm = pl.BlockSpec(memory_space=pl.ANY)
    spec = pltpu.PrefetchScalarGridSpec(
        num_scalar_prefetch=2,
        grid=(steps,),
        in_specs=[hbm, hbm, hbm, pl.BlockSpec(lag.shape, lambda i, o, f: (0, 0))],
        out_specs=pl.BlockSpec((nlag, group * K), lambda i, o, f: (0, i)),
        scratch_shapes=[
            pltpu.VMEM((3 * rows, sub, lanes), jnp.bfloat16),
            pltpu.VMEM(lag.shape, jnp.bfloat16),
            pltpu.VMEM(lag.shape, jnp.bfloat16),
            pltpu.VMEM((group * K * 8, 128), jnp.float32),
            pltpu.SemaphoreType.DMA((3,)),
        ],
    )
    pairs = count * K
    cost = pl.CostEstimate(flops=pairs * 2048 * 6 + 3 * 2 * pairs * 1024 * (nlag - 1), transcendentals=0,
                           bytes_accessed=3 * rows * sub * lanes * 2 + pairs * nlag * 4)
    return pl.pallas_call(
        functools.partial(pair_kernel, group=group),
        grid_spec=spec,
        out_shape=jax.ShapeDtypeStruct((nlag, pairs), jnp.float32),
        compiler_params=pltpu.CompilerParams(dimension_semantics=("arbitrary",), vmem_limit_bytes=48 * 1024 * 1024),
        cost_estimate=cost,
    )(own_idx, far_idx, *blocks, lag)


def shards(record, partners, block_owner):
    block_size, windows_dev, samples = record.shape
    width = windows_dev * 2 * NFB
    fourier = fourier_table_t(samples)
    own = whiten(record, fourier).reshape(block_size, width // 128, 128)
    near = neighbourhood(own)

    tm_count = lax.axis_size("tm")
    per_block = block_size // tm_count
    owner_row = block_owner[0]
    onehot = (owner_row[None, :] == jnp.arange(tm_count, dtype=jnp.int32)[:, None]).astype(jnp.int32)
    inverse = jnp.sum(onehot * jnp.arange(tm_count, dtype=jnp.int32)[None, :], axis=1)
    nz = 4 if tm_count % 4 == 0 else 1
    nx = tm_count // nz
    half = per_block // 2
    zx = jnp.arange(nz, dtype=jnp.int32)[:, None] + nz * jnp.arange(nx, dtype=jnp.int32)[None, :]
    xz = nz * jnp.arange(nx, dtype=jnp.int32)[:, None] + jnp.arange(nz, dtype=jnp.int32)[None, :]
    dest = jnp.stack([zx.reshape(-1), xz.reshape(-1)])
    first = inverse[dest] * per_block + jnp.arange(2, dtype=jnp.int32)[:, None] * half
    chan_local = (first[:, :, None] + jnp.arange(half, dtype=jnp.int32)[None, None, :]).reshape(-1)
    own_idx = block_size + chan_local
    base_row = lax.axis_index("chan") * block_size - block_size
    far_idx = jnp.clip(jnp.take(partners, chan_local, axis=0) - base_row, 0, 3 * block_size - 1).reshape(-1)

    partial = pair_lags(near, own_idx, far_idx, lag_table(samples), half)
    summed = scatter_sum(partial, nx, nz, half * K)
    scale = 1.0 / math.sqrt(windows_dev * tm_count * NFB)
    return summed.T * scale


def ring_pairs(sizes, axis, shift):
    nx, nz = sizes
    pairs = []
    for d in range(nx * nz):
        x, z = d // nz, d % nz
        if axis == 1:
            pairs.append((d, x * nz + (z + shift) % nz))
        else:
            pairs.append((d, ((x + shift) % nx) * nz + z))
    return pairs


def pick(array, index, width):
    return lax.dynamic_slice_in_dim(array, index * width, width, axis=1)


def scatter_sum(lags, nx, nz, width):
    me = lax.axis_index("tm")
    mx, mz = me // nz, me % nz
    span = nx * nz * width

    def round_(arrays):
        outs = []
        for array, mine, axis, n, size in arrays:
            acc = pick(array, mine, size)
            for shift in range(1, n):
                message = pick(array, (mine + shift) % n, size)
                acc = acc + lax.ppermute(message, "tm", ring_pairs((nx, nz), axis, shift))
            outs.append(acc)
        return outs

    a, b = round_([(lags[:, :span], mz, 1, nz, nx * width), (lags[:, span:], mx, 0, nx, nz * width)])
    a, b = round_([(a, mx, 0, nx, width), (b, mz, 1, nz, width)])
    return jnp.concatenate([a, b], axis=1)


def solution(mesh):
    placed = (P("chan", "tm", None), P("chan", None), P("chan", None))
    return jax.shard_map(
        shards, mesh=mesh, in_specs=placed, out_specs=P(("chan", "tm"), None), check_vma=False
    )
```

```python
import math

import jax
import jax.numpy as jnp
from jax import lax
import functools

from jax.experimental import pallas as pl
from jax.experimental.pallas import tpu as pltpu
from jax.sharding import PartitionSpec as P

NFB = 512
F0 = 64
K = 8
LAG = 128


def split_length(samples):
    if samples % 128 == 0:
        return samples // 128, 128
    best = 1
    for b in range(1, samples + 1):
        if samples % b == 0 and b * b <= samples:
            best = b
    return samples // best, best


def angle_pair(rows, cols, padded):
    phase = (rows * cols % padded).astype(jnp.float32) * (2.0 * math.pi / padded)
    return jnp.cos(phase), jnp.sin(phase)


def fourier_table_t(samples):
    padded = 2 * samples
    outer, inner = split_length(samples)
    freqs = (F0 + jnp.arange(NFB, dtype=jnp.int32))[:, None]
    ca, sa = angle_pair(freqs, jnp.arange(outer, dtype=jnp.int32)[None, :] * inner, padded)
    cb, sb = angle_pair(freqs, jnp.arange(inner, dtype=jnp.int32)[None, :], padded)
    ca, sa = ca[:, :, None], sa[:, :, None]
    cb, sb = cb[:, None, :], sb[:, None, :]
    cos_t = (ca * cb - sa * sb).reshape(NFB, samples)
    sin_t = (sa * cb + ca * sb).reshape(NFB, samples)
    return cos_t.astype(jnp.bfloat16), (-sin_t).astype(jnp.bfloat16)


def lag_table(samples):
    padded = 2 * samples
    shifts = (jnp.arange(2 * LAG + 1, dtype=jnp.int32) - LAG)[None, :]
    fine = 16
    cu, su = angle_pair((F0 + fine * jnp.arange(NFB // fine, dtype=jnp.int32))[:, None], shifts, padded)
    cv, sv = angle_pair(jnp.arange(fine, dtype=jnp.int32)[:, None], shifts, padded)
    cu, su = cu[:, None, :], su[:, None, :]
    cv, sv = cv[None, :, :], sv[None, :, :]
    cos_t = (cu * cv - su * sv).reshape(NFB, -1)
    sin_t = (su * cv + cu * sv).reshape(NFB, -1)
    return jnp.concatenate([cos_t, -sin_t], axis=0)


def whiten(rows, fourier):
    real_part, imag_part = (
        lax.dot_general(rows, table, (((2,), (1,)), ((), ())), preferred_element_type=jnp.float32)
        for table in fourier
    )
    energy = real_part * real_part + imag_part * imag_part
    level = jnp.mean(energy, axis=-1, keepdims=True)
    divisor = jnp.sqrt(energy + 0.1 * level + 1e-05)
    whitened = jnp.concatenate([real_part / divisor, imag_part / divisor], axis=-1)
    return whitened.astype(jnp.bfloat16)


def neighbourhood(own):
    size = lax.axis_size("chan")
    up = [(i, i + 1) for i in range(size - 1)]
    down = [(j, i) for i, j in up]
    below = lax.ppermute(own, "chan", up)
    above = lax.ppermute(own, "chan", down)
    return below, own, above


def pair_kernel(own_idx, far_idx, below_ref, mid_ref, above_ref, lag_ref, out_ref,
                near_ref, lhi_ref, llo_ref, cross_ref, sems, *, group):
    step = pl.program_id(0)
    block = mid_ref.shape[0]

    @pl.when(step == 0)
    def _():
        copies = [
            pltpu.make_async_copy(src, near_ref.at[pl.ds(j * block, block)], sems.at[j])
            for j, src in enumerate((below_ref, mid_ref, above_ref))
        ]
        for c in copies:
            c.start()
        lag = lag_ref[...]
        hi = lag.astype(jnp.bfloat16)
        lhi_ref[...] = hi
        llo_ref[...] = (lag - hi.astype(jnp.float32)).astype(jnp.bfloat16)
        for c in copies:
            c.wait()

    def channel(i, carry):
        s = step * group + i
        a = near_ref[own_idx[s]].astype(jnp.float32)
        a_swap = jnp.concatenate([-a[4:8], a[0:4], -a[12:16], a[8:12]], axis=0)
        for k in range(K):
            b = near_ref[far_idx[s * K + k]].astype(jnp.float32)
            m = a * b
            n = a_swap * b
            sm = m[0:8] + m[8:16]
            sn = n[0:8] + n[8:16]
            row = jnp.concatenate([sm[0:4] + sm[4:8], sn[0:4] + sn[4:8]], axis=0)
            cross_ref[pl.ds(pl.multiple_of((i * K + k) * 8, 8), 8), :] = row
        return carry

    lax.fori_loop(0, group, channel, 0, unroll=4)
    pairs = group * K
    half = 4
    sums = []
    for part_rows in (range(0, half), range(half, 8)):
        total = None
        for r in part_rows:
            slab = cross_ref[pl.ds(r, pairs, stride=8), :]
            hi = slab.astype(jnp.bfloat16)
            lo = (slab - hi.astype(jnp.float32)).astype(jnp.bfloat16)
            lh = lhi_ref[:, r * 128 : (r + 1) * 128]
            ll = llo_ref[:, r * 128 : (r + 1) * 128]
            part = (nt_dot(lh, hi) + nt_dot(lh, lo) + nt_dot(ll, hi))
            total = part if total is None else total + part
        sums.append(total)
    wide = lhi_ref.shape[0]
    out_ref[:wide, :] = sums[0] + sums[1]
    out_ref[wide:, :] = sums[0][0:1, :] - sums[1][0:1, :]


def nt_dot(a, b):
    return lax.dot_general(a, b, (((1,), (1,)), ((), ())), preferred_element_type=jnp.float32)


def pair_lags(blocks, own_idx, far_idx, lag, group):
    rows, sub, lanes = blocks[1].shape
    count = own_idx.shape[0]
    nlag = lag.shape[1]
    lag = lag[:, : nlag - 1].T
    steps = count // group
    hbm = pl.BlockSpec(memory_space=pl.ANY)
    spec = pltpu.PrefetchScalarGridSpec(
        num_scalar_prefetch=2,
        grid=(steps,),
        in_specs=[hbm, hbm, hbm, pl.BlockSpec(lag.shape, lambda i, o, f: (0, 0))],
        out_specs=pl.BlockSpec((nlag, group * K), lambda i, o, f: (0, i)),
        scratch_shapes=[
            pltpu.VMEM((3 * rows, sub, lanes), jnp.bfloat16),
            pltpu.VMEM(lag.shape, jnp.bfloat16),
            pltpu.VMEM(lag.shape, jnp.bfloat16),
            pltpu.VMEM((group * K * 8, 128), jnp.float32),
            pltpu.SemaphoreType.DMA((3,)),
        ],
    )
    pairs = count * K
    cost = pl.CostEstimate(flops=pairs * 2048 * 6 + 3 * 2 * pairs * 1024 * (nlag - 1), transcendentals=0,
                           bytes_accessed=3 * rows * sub * lanes * 2 + pairs * nlag * 4)
    return pl.pallas_call(
        functools.partial(pair_kernel, group=group),
        grid_spec=spec,
        out_shape=jax.ShapeDtypeStruct((nlag, pairs), jnp.float32),
        compiler_params=pltpu.CompilerParams(dimension_semantics=("arbitrary",), vmem_limit_bytes=48 * 1024 * 1024),
        cost_estimate=cost,
    )(own_idx, far_idx, *blocks, lag)


def shards(record, partners, block_owner):
    block_size, windows_dev, samples = record.shape
    width = windows_dev * 2 * NFB
    fourier = fourier_table_t(samples)
    own = whiten(record, fourier).reshape(block_size, width // 128, 128)
    near = neighbourhood(own)

    tm_count = lax.axis_size("tm")
    per_block = block_size // tm_count
    owner_row = block_owner[0]
    onehot = (owner_row[None, :] == jnp.arange(tm_count, dtype=jnp.int32)[:, None]).astype(jnp.int32)
    inverse = jnp.sum(onehot * jnp.arange(tm_count, dtype=jnp.int32)[None, :], axis=1)
    nz = 4 if tm_count % 4 == 0 else 1
    nx = tm_count // nz
    half = per_block // 2
    zx = jnp.arange(nz, dtype=jnp.int32)[:, None] + nz * jnp.arange(nx, dtype=jnp.int32)[None, :]
    xz = nz * jnp.arange(nx, dtype=jnp.int32)[:, None] + jnp.arange(nz, dtype=jnp.int32)[None, :]
    dest = jnp.stack([zx.reshape(-1), xz.reshape(-1)])
    first = inverse[dest] * per_block + jnp.arange(2, dtype=jnp.int32)[:, None] * half
    chan_local = (first[:, :, None] + jnp.arange(half, dtype=jnp.int32)[None, None, :]).reshape(-1)
    own_idx = block_size + chan_local
    base_row = lax.axis_index("chan") * block_size - block_size
    far_idx = jnp.clip(jnp.take(partners, chan_local, axis=0) - base_row, 0, 3 * block_size - 1).reshape(-1)

    partial = pair_lags(near, own_idx, far_idx, lag_table(samples), half)
    summed = scatter_sum(partial, nx, nz, half * K)
    scale = 1.0 / math.sqrt(windows_dev * tm_count * NFB)
    return summed.T * scale


def ring_pairs(sizes, axis, shift):
    nx, nz = sizes
    pairs = []
    for d in range(nx * nz):
        x, z = d // nz, d % nz
        if axis == 1:
            pairs.append((d, x * nz + (z + shift) % nz))
        else:
            pairs.append((d, ((x + shift) % nx) * nz + z))
    return pairs


def pick(array, index, width):
    return lax.dynamic_slice_in_dim(array, index * width, width, axis=1)


def scatter_sum(lags, nx, nz, width):
    me = lax.axis_index("tm")
    mx, mz = me // nz, me % nz
    span = nx * nz * width

    def round_(arrays):
        outs = []
        for array, mine, axis, n, size in arrays:
            acc = pick(array, mine, size)
            for shift in range(1, n):
                message = pick(array, (mine + shift) % n, size)
                acc = acc + lax.ppermute(message, "tm", ring_pairs((nx, nz), axis, shift))
            outs.append(acc)
        return outs

    a, b = round_([(lags[:, :span], mz, 1, nz, nx * width), (lags[:, span:], mx, 0, nx, nz * width)])
    a, b = round_([(a, mx, 0, nx, width), (b, mz, 1, nz, width)])
    return jnp.concatenate([a, b], axis=1)


def solution(mesh):
    placed = (P("chan", "tm", None), P("chan", None), P("chan", None))
    return jax.shard_map(
        shards, mesh=mesh, in_specs=placed, out_specs=P(("chan", "tm"), None), check_vma=False
    )
```

```python
import math

import jax
import jax.numpy as jnp
from jax import lax
import functools

from jax.experimental import pallas as pl
from jax.experimental.pallas import tpu as pltpu
from jax.sharding import PartitionSpec as P

NFB = 512
F0 = 64
K = 8
LAG = 128


def split_length(samples):
    if samples % 128 == 0:
        return samples // 128, 128
    best = 1
    for b in range(1, samples + 1):
        if samples % b == 0 and b * b <= samples:
            best = b
    return samples // best, best


def angle_pair(rows, cols, padded):
    phase = (rows * cols % padded).astype(jnp.float32) * (2.0 * math.pi / padded)
    return jnp.cos(phase), jnp.sin(phase)


def fourier_table_t(samples):
    padded = 2 * samples
    outer, inner = split_length(samples)
    freqs = (F0 + jnp.arange(NFB, dtype=jnp.int32))[:, None]
    ca, sa = angle_pair(freqs, jnp.arange(outer, dtype=jnp.int32)[None, :] * inner, padded)
    cb, sb = angle_pair(freqs, jnp.arange(inner, dtype=jnp.int32)[None, :], padded)
    ca, sa = ca[:, :, None], sa[:, :, None]
    cb, sb = cb[:, None, :], sb[:, None, :]
    cos_t = (ca * cb - sa * sb).reshape(NFB, samples)
    sin_t = (sa * cb + ca * sb).reshape(NFB, samples)
    return cos_t.astype(jnp.bfloat16), (-sin_t).astype(jnp.bfloat16)


def lag_table(samples):
    padded = 2 * samples
    shifts = (jnp.arange(2 * LAG + 1, dtype=jnp.int32) - LAG)[None, :]
    fine = 16
    cu, su = angle_pair((F0 + fine * jnp.arange(NFB // fine, dtype=jnp.int32))[:, None], shifts, padded)
    cv, sv = angle_pair(jnp.arange(fine, dtype=jnp.int32)[:, None], shifts, padded)
    cu, su = cu[:, None, :], su[:, None, :]
    cv, sv = cv[None, :, :], sv[None, :, :]
    cos_t = (cu * cv - su * sv).reshape(NFB, -1)
    sin_t = (su * cv + cu * sv).reshape(NFB, -1)
    return jnp.concatenate([cos_t, -sin_t], axis=0)


def whiten(rows, fourier):
    real_part, imag_part = (
        lax.dot_general(rows, table, (((2,), (1,)), ((), ())), preferred_element_type=jnp.float32)
        for table in fourier
    )
    energy = real_part * real_part + imag_part * imag_part
    level = jnp.mean(energy, axis=-1, keepdims=True)
    divisor = jnp.sqrt(energy + 0.1 * level + 1e-05)
    whitened = jnp.concatenate([real_part / divisor, imag_part / divisor], axis=-1)
    return whitened.astype(jnp.bfloat16)


def neighbourhood(own):
    size = lax.axis_size("chan")
    up = [(i, i + 1) for i in range(size - 1)]
    down = [(j, i) for i, j in up]
    below = lax.ppermute(own, "chan", up)
    above = lax.ppermute(own, "chan", down)
    return below, own, above


def pair_kernel(own_idx, far_idx, below_ref, mid_ref, above_ref, lag_ref, out_ref,
                near_ref, lhi_ref, llo_ref, cross_ref, sems, *, group):
    step = pl.program_id(0)
    block = mid_ref.shape[0]

    @pl.when(step == 0)
    def _():
        copies = [
            pltpu.make_async_copy(src, near_ref.at[pl.ds(j * block, block)], sems.at[j])
            for j, src in enumerate((below_ref, mid_ref, above_ref))
        ]
        for c in copies:
            c.start()
        lag = lag_ref[...]
        hi = lag.astype(jnp.bfloat16)
        lhi_ref[...] = hi
        llo_ref[...] = (lag - hi.astype(jnp.float32)).astype(jnp.bfloat16)
        for c in copies:
            c.wait()

    def channel(i, carry):
        s = step * group + i
        a = near_ref[own_idx[s]].astype(jnp.float32)
        a_swap = jnp.concatenate([-a[4:8], a[0:4], -a[12:16], a[8:12]], axis=0)
        for k in range(K):
            b = near_ref[far_idx[s * K + k]].astype(jnp.float32)
            m = a * b
            n = a_swap * b
            sm = m[0:8] + m[8:16]
            sn = n[0:8] + n[8:16]
            row = jnp.concatenate([sm[0:4] + sm[4:8], sn[0:4] + sn[4:8]], axis=0)
            cross_ref[pl.ds(pl.multiple_of((i * K + k) * 8, 8), 8), :] = row
        return carry

    lax.fori_loop(0, group, channel, 0, unroll=True)
    pairs = group * K
    half = 4
    sums = []
    for part_rows in (range(0, half), range(half, 8)):
        total = None
        for r in part_rows:
            slab = cross_ref[pl.ds(r, pairs, stride=8), :]
            hi = slab.astype(jnp.bfloat16)
            lo = (slab - hi.astype(jnp.float32)).astype(jnp.bfloat16)
            lh = lhi_ref[:, r * 128 : (r + 1) * 128]
            ll = llo_ref[:, r * 128 : (r + 1) * 128]
            part = (nt_dot(lh, hi) + nt_dot(lh, lo) + nt_dot(ll, hi))
            total = part if total is None else total + part
        sums.append(total)
    wide = lhi_ref.shape[0]
    out_ref[:wide, :] = sums[0] + sums[1]
    out_ref[wide:, :] = sums[0][0:1, :] - sums[1][0:1, :]


def nt_dot(a, b):
    return lax.dot_general(a, b, (((1,), (1,)), ((), ())), preferred_element_type=jnp.float32)


def pair_lags(blocks, own_idx, far_idx, lag, group):
    rows, sub, lanes = blocks[1].shape
    count = own_idx.shape[0]
    nlag = lag.shape[1]
    lag = lag[:, : nlag - 1].T
    steps = count // group
    hbm = pl.BlockSpec(memory_space=pl.ANY)
    spec = pltpu.PrefetchScalarGridSpec(
        num_scalar_prefetch=2,
        grid=(steps,),
        in_specs=[hbm, hbm, hbm, pl.BlockSpec(lag.shape, lambda i, o, f: (0, 0))],
        out_specs=pl.BlockSpec((nlag, group * K), lambda i, o, f: (0, i)),
        scratch_shapes=[
            pltpu.VMEM((3 * rows, sub, lanes), jnp.bfloat16),
            pltpu.VMEM(lag.shape, jnp.bfloat16),
            pltpu.VMEM(lag.shape, jnp.bfloat16),
            pltpu.VMEM((group * K * 8, 128), jnp.float32),
            pltpu.SemaphoreType.DMA((3,)),
        ],
    )
    pairs = count * K
    cost = pl.CostEstimate(flops=pairs * 2048 * 6 + 3 * 2 * pairs * 1024 * (nlag - 1), transcendentals=0,
                           bytes_accessed=3 * rows * sub * lanes * 2 + pairs * nlag * 4)
    return pl.pallas_call(
        functools.partial(pair_kernel, group=group),
        grid_spec=spec,
        out_shape=jax.ShapeDtypeStruct((nlag, pairs), jnp.float32),
        compiler_params=pltpu.CompilerParams(dimension_semantics=("arbitrary",), vmem_limit_bytes=48 * 1024 * 1024),
        cost_estimate=cost,
    )(own_idx, far_idx, *blocks, lag)


def shards(record, partners, block_owner):
    block_size, windows_dev, samples = record.shape
    width = windows_dev * 2 * NFB
    fourier = fourier_table_t(samples)
    own = whiten(record, fourier).reshape(block_size, width // 128, 128)
    near = neighbourhood(own)

    tm_count = lax.axis_size("tm")
    per_block = block_size // tm_count
    owner_row = block_owner[0]
    onehot = (owner_row[None, :] == jnp.arange(tm_count, dtype=jnp.int32)[:, None]).astype(jnp.int32)
    inverse = jnp.sum(onehot * jnp.arange(tm_count, dtype=jnp.int32)[None, :], axis=1)
    nz = 4 if tm_count % 4 == 0 else 1
    nx = tm_count // nz
    half = per_block // 2
    zx = jnp.arange(nz, dtype=jnp.int32)[:, None] + nz * jnp.arange(nx, dtype=jnp.int32)[None, :]
    xz = nz * jnp.arange(nx, dtype=jnp.int32)[:, None] + jnp.arange(nz, dtype=jnp.int32)[None, :]
    dest = jnp.stack([zx.reshape(-1), xz.reshape(-1)])
    first = inverse[dest] * per_block + jnp.arange(2, dtype=jnp.int32)[:, None] * half
    chan_local = (first[:, :, None] + jnp.arange(half, dtype=jnp.int32)[None, None, :]).reshape(-1)
    own_idx = block_size + chan_local
    base_row = lax.axis_index("chan") * block_size - block_size
    far_idx = jnp.clip(jnp.take(partners, chan_local, axis=0) - base_row, 0, 3 * block_size - 1).reshape(-1)

    partial = pair_lags(near, own_idx, far_idx, lag_table(samples), half)
    summed = scatter_sum(partial, nx, nz, half * K)
    scale = 1.0 / math.sqrt(windows_dev * tm_count * NFB)
    return summed.T * scale


def ring_pairs(sizes, axis, shift):
    nx, nz = sizes
    pairs = []
    for d in range(nx * nz):
        x, z = d // nz, d % nz
        if axis == 1:
            pairs.append((d, x * nz + (z + shift) % nz))
        else:
            pairs.append((d, ((x + shift) % nx) * nz + z))
    return pairs


def pick(array, index, width):
    return lax.dynamic_slice_in_dim(array, index * width, width, axis=1)


def scatter_sum(lags, nx, nz, width):
    me = lax.axis_index("tm")
    mx, mz = me // nz, me % nz
    span = nx * nz * width

    def round_(arrays):
        outs = []
        for array, mine, axis, n, size in arrays:
            acc = pick(array, mine, size)
            for shift in range(1, n):
                message = pick(array, (mine + shift) % n, size)
                acc = acc + lax.ppermute(message, "tm", ring_pairs((nx, nz), axis, shift))
            outs.append(acc)
        return outs

    a, b = round_([(lags[:, :span], mz, 1, nz, nx * width), (lags[:, span:], mx, 0, nx, nz * width)])
    a, b = round_([(a, mx, 0, nx, width), (b, mz, 1, nz, width)])
    return jnp.concatenate([a, b], axis=1)


def solution(mesh):
    placed = (P("chan", "tm", None), P("chan", None), P("chan", None))
    return jax.shard_map(
        shards, mesh=mesh, in_specs=placed, out_specs=P(("chan", "tm"), None), check_vma=False
    )
```

```python
import math

import jax
import jax.numpy as jnp
from jax import lax
import functools

from jax.experimental import pallas as pl
from jax.experimental.pallas import tpu as pltpu
from jax.sharding import PartitionSpec as P

NFB = 512
F0 = 64
K = 8
LAG = 128


def split_length(samples):
    if samples % 128 == 0:
        return samples // 128, 128
    best = 1
    for b in range(1, samples + 1):
        if samples % b == 0 and b * b <= samples:
            best = b
    return samples // best, best


def angle_pair(rows, cols, padded):
    phase = (rows * cols % padded).astype(jnp.float32) * (2.0 * math.pi / padded)
    return jnp.cos(phase), jnp.sin(phase)


def fourier_table_t(samples):
    padded = 2 * samples
    outer, inner = split_length(samples)
    freqs = (F0 + jnp.arange(NFB, dtype=jnp.int32))[:, None]
    ca, sa = angle_pair(freqs, jnp.arange(outer, dtype=jnp.int32)[None, :] * inner, padded)
    cb, sb = angle_pair(freqs, jnp.arange(inner, dtype=jnp.int32)[None, :], padded)
    ca, sa = ca[:, :, None], sa[:, :, None]
    cb, sb = cb[:, None, :], sb[:, None, :]
    cos_t = (ca * cb - sa * sb).reshape(NFB, samples)
    sin_t = (sa * cb + ca * sb).reshape(NFB, samples)
    return cos_t.astype(jnp.bfloat16), (-sin_t).astype(jnp.bfloat16)


def lag_table(samples):
    padded = 2 * samples
    shifts = (jnp.arange(2 * LAG + 1, dtype=jnp.int32) - LAG)[None, :]
    fine = 16
    cu, su = angle_pair((F0 + fine * jnp.arange(NFB // fine, dtype=jnp.int32))[:, None], shifts, padded)
    cv, sv = angle_pair(jnp.arange(fine, dtype=jnp.int32)[:, None], shifts, padded)
    cu, su = cu[:, None, :], su[:, None, :]
    cv, sv = cv[None, :, :], sv[None, :, :]
    cos_t = (cu * cv - su * sv).reshape(NFB, -1)
    sin_t = (su * cv + cu * sv).reshape(NFB, -1)
    return jnp.concatenate([cos_t, -sin_t], axis=0)


def whiten(rows, fourier):
    real_part, imag_part = (
        lax.dot_general(rows, table, (((2,), (1,)), ((), ())), preferred_element_type=jnp.float32)
        for table in fourier
    )
    energy = real_part * real_part + imag_part * imag_part
    level = jnp.mean(energy, axis=-1, keepdims=True)
    divisor = jnp.sqrt(energy + 0.1 * level + 1e-05)
    whitened = jnp.concatenate([real_part / divisor, imag_part / divisor], axis=-1)
    return whitened.astype(jnp.bfloat16)


def neighbourhood(own):
    size = lax.axis_size("chan")
    up = [(i, i + 1) for i in range(size - 1)]
    down = [(j, i) for i, j in up]
    below = lax.ppermute(own, "chan", up)
    above = lax.ppermute(own, "chan", down)
    return below, own, above


def pair_kernel(own_idx, far_idx, below_ref, mid_ref, above_ref, lag_ref, out_ref,
                near_ref, lhi_ref, llo_ref, cross_ref, sems, *, group):
    step = pl.program_id(0)
    block = mid_ref.shape[0]

    @pl.when(step == 0)
    def _():
        copies = [
            pltpu.make_async_copy(src, near_ref.at[pl.ds(j * block, block)], sems.at[j])
            for j, src in enumerate((below_ref, mid_ref, above_ref))
        ]
        for c in copies:
            c.start()
        lag = lag_ref[...]
        hi = lag.astype(jnp.bfloat16)
        lhi_ref[...] = hi
        llo_ref[...] = (lag - hi.astype(jnp.float32)).astype(jnp.bfloat16)
        for c in copies:
            c.wait()

    def channel(i, carry):
        s = step * group + i
        a = near_ref[own_idx[s]].astype(jnp.float32)
        a_swap = jnp.concatenate([-a[4:8], a[0:4], -a[12:16], a[8:12]], axis=0)
        for k in range(K):
            b = near_ref[far_idx[s * K + k]].astype(jnp.float32)
            m = a * b
            n = a_swap * b
            sm = m[0:8] + m[8:16]
            sn = n[0:8] + n[8:16]
            row = jnp.concatenate([sm[0:4] + sm[4:8], sn[0:4] + sn[4:8]], axis=0)
            cross_ref[pl.ds(pl.multiple_of((i * K + k) * 8, 8), 8), :] = row
        return carry

    lax.fori_loop(0, group, channel, 0, unroll=True)
    pairs = group * K
    sums = []
    for first in (0, 4):
        slab = jnp.concatenate([cross_ref[pl.ds(r, pairs, stride=8), :] for r in range(first, first + 4)], axis=1)
        hi = slab.astype(jnp.bfloat16)
        lo = (slab - hi.astype(jnp.float32)).astype(jnp.bfloat16)
        lh = lhi_ref[:, first * 128 : (first + 4) * 128]
        ll = llo_ref[:, first * 128 : (first + 4) * 128]
        sums.append(nt_dot(lh, hi) + nt_dot(lh, lo) + nt_dot(ll, hi))
    wide = lhi_ref.shape[0]
    out_ref[:wide, :] = sums[0] + sums[1]
    out_ref[wide:, :] = sums[0][0:1, :] - sums[1][0:1, :]


def nt_dot(a, b):
    return lax.dot_general(a, b, (((1,), (1,)), ((), ())), preferred_element_type=jnp.float32)


def pair_lags(blocks, own_idx, far_idx, lag, group):
    rows, sub, lanes = blocks[1].shape
    count = own_idx.shape[0]
    nlag = lag.shape[1]
    lag = lag[:, : nlag - 1].T
    steps = count // group
    hbm = pl.BlockSpec(memory_space=pl.ANY)
    spec = pltpu.PrefetchScalarGridSpec(
        num_scalar_prefetch=2,
        grid=(steps,),
        in_specs=[hbm, hbm, hbm, pl.BlockSpec(lag.shape, lambda i, o, f: (0, 0))],
        out_specs=pl.BlockSpec((nlag, group * K), lambda i, o, f: (0, i)),
        scratch_shapes=[
            pltpu.VMEM((3 * rows, sub, lanes), jnp.bfloat16),
            pltpu.VMEM(lag.shape, jnp.bfloat16),
            pltpu.VMEM(lag.shape, jnp.bfloat16),
            pltpu.VMEM((group * K * 8, 128), jnp.float32),
            pltpu.SemaphoreType.DMA((3,)),
        ],
    )
    pairs = count * K
    cost = pl.CostEstimate(flops=pairs * 2048 * 6 + 3 * 2 * pairs * 1024 * (nlag - 1), transcendentals=0,
                           bytes_accessed=3 * rows * sub * lanes * 2 + pairs * nlag * 4)
    return pl.pallas_call(
        functools.partial(pair_kernel, group=group),
        grid_spec=spec,
        out_shape=jax.ShapeDtypeStruct((nlag, pairs), jnp.float32),
        compiler_params=pltpu.CompilerParams(dimension_semantics=("arbitrary",), vmem_limit_bytes=48 * 1024 * 1024),
        cost_estimate=cost,
    )(own_idx, far_idx, *blocks, lag)


def shards(record, partners, block_owner):
    block_size, windows_dev, samples = record.shape
    width = windows_dev * 2 * NFB
    fourier = fourier_table_t(samples)
    own = whiten(record, fourier).reshape(block_size, width // 128, 128)
    near = neighbourhood(own)

    tm_count = lax.axis_size("tm")
    per_block = block_size // tm_count
    owner_row = block_owner[0]
    onehot = (owner_row[None, :] == jnp.arange(tm_count, dtype=jnp.int32)[:, None]).astype(jnp.int32)
    inverse = jnp.sum(onehot * jnp.arange(tm_count, dtype=jnp.int32)[None, :], axis=1)
    nz = 4 if tm_count % 4 == 0 else 1
    nx = tm_count // nz
    half = per_block // 2
    zx = jnp.arange(nz, dtype=jnp.int32)[:, None] + nz * jnp.arange(nx, dtype=jnp.int32)[None, :]
    xz = nz * jnp.arange(nx, dtype=jnp.int32)[:, None] + jnp.arange(nz, dtype=jnp.int32)[None, :]
    dest = jnp.stack([zx.reshape(-1), xz.reshape(-1)])
    first = inverse[dest] * per_block + jnp.arange(2, dtype=jnp.int32)[:, None] * half
    chan_local = (first[:, :, None] + jnp.arange(half, dtype=jnp.int32)[None, None, :]).reshape(-1)
    own_idx = block_size + chan_local
    base_row = lax.axis_index("chan") * block_size - block_size
    far_idx = jnp.clip(jnp.take(partners, chan_local, axis=0) - base_row, 0, 3 * block_size - 1).reshape(-1)

    partial = pair_lags(near, own_idx, far_idx, lag_table(samples), per_block)
    summed = scatter_sum(partial, nx, nz, half * K)
    scale = 1.0 / math.sqrt(windows_dev * tm_count * NFB)
    return summed.T * scale


def ring_pairs(sizes, axis, shift):
    nx, nz = sizes
    pairs = []
    for d in range(nx * nz):
        x, z = d // nz, d % nz
        if axis == 1:
            pairs.append((d, x * nz + (z + shift) % nz))
        else:
            pairs.append((d, ((x + shift) % nx) * nz + z))
    return pairs


def pick(array, index, width):
    return lax.dynamic_slice_in_dim(array, index * width, width, axis=1)


def scatter_sum(lags, nx, nz, width):
    me = lax.axis_index("tm")
    mx, mz = me // nz, me % nz
    span = nx * nz * width

    def round_(arrays):
        outs = []
        for array, mine, axis, n, size in arrays:
            acc = pick(array, mine, size)
            for shift in range(1, n):
                message = pick(array, (mine + shift) % n, size)
                acc = acc + lax.ppermute(message, "tm", ring_pairs((nx, nz), axis, shift))
            outs.append(acc)
        return outs

    a, b = round_([(lags[:, :span], mz, 1, nz, nx * width), (lags[:, span:], mx, 0, nx, nz * width)])
    a, b = round_([(a, mx, 0, nx, width), (b, mz, 1, nz, width)])
    return jnp.concatenate([a, b], axis=1)


def solution(mesh):
    placed = (P("chan", "tm", None), P("chan", None), P("chan", None))
    return jax.shard_map(
        shards, mesh=mesh, in_specs=placed, out_specs=P(("chan", "tm"), None), check_vma=False
    )
```

```python
import math

import jax
import jax.numpy as jnp
from jax import lax
import functools

from jax.experimental import pallas as pl
from jax.experimental.pallas import tpu as pltpu
from jax.sharding import PartitionSpec as P

NFB = 512
F0 = 64
K = 8
LAG = 128


def split_length(samples):
    if samples % 128 == 0:
        return samples // 128, 128
    best = 1
    for b in range(1, samples + 1):
        if samples % b == 0 and b * b <= samples:
            best = b
    return samples // best, best


def angle_pair(rows, cols, padded):
    phase = (rows * cols % padded).astype(jnp.float32) * (2.0 * math.pi / padded)
    return jnp.cos(phase), jnp.sin(phase)


def fourier_table_t(samples):
    padded = 2 * samples
    outer, inner = split_length(samples)
    freqs = (F0 + jnp.arange(NFB, dtype=jnp.int32))[:, None]
    ca, sa = angle_pair(freqs, jnp.arange(outer, dtype=jnp.int32)[None, :] * inner, padded)
    cb, sb = angle_pair(freqs, jnp.arange(inner, dtype=jnp.int32)[None, :], padded)
    ca, sa = ca[:, :, None], sa[:, :, None]
    cb, sb = cb[:, None, :], sb[:, None, :]
    cos_t = (ca * cb - sa * sb).reshape(NFB, samples)
    sin_t = (sa * cb + ca * sb).reshape(NFB, samples)
    return cos_t.astype(jnp.bfloat16), (-sin_t).astype(jnp.bfloat16)


def lag_table(samples):
    padded = 2 * samples
    shifts = (jnp.arange(2 * LAG + 1, dtype=jnp.int32) - LAG)[None, :]
    fine = 16
    cu, su = angle_pair((F0 + fine * jnp.arange(NFB // fine, dtype=jnp.int32))[:, None], shifts, padded)
    cv, sv = angle_pair(jnp.arange(fine, dtype=jnp.int32)[:, None], shifts, padded)
    cu, su = cu[:, None, :], su[:, None, :]
    cv, sv = cv[None, :, :], sv[None, :, :]
    cos_t = (cu * cv - su * sv).reshape(NFB, -1)
    sin_t = (su * cv + cu * sv).reshape(NFB, -1)
    return jnp.concatenate([cos_t, -sin_t], axis=0)


def whiten(rows, fourier):
    real_part, imag_part = (
        lax.dot_general(rows, table, (((2,), (1,)), ((), ())), preferred_element_type=jnp.float32)
        for table in fourier
    )
    energy = real_part * real_part + imag_part * imag_part
    level = jnp.mean(energy, axis=-1, keepdims=True)
    divisor = jnp.sqrt(energy + 0.1 * level + 1e-05)
    whitened = jnp.concatenate([real_part / divisor, imag_part / divisor], axis=-1)
    return whitened.astype(jnp.bfloat16)


def neighbourhood(own):
    size = lax.axis_size("chan")
    up = [(i, i + 1) for i in range(size - 1)]
    down = [(j, i) for i, j in up]
    below = lax.ppermute(own, "chan", up)
    above = lax.ppermute(own, "chan", down)
    return below, own, above


def pair_kernel(own_idx, far_idx, below_ref, mid_ref, above_ref, lag_ref, out_ref,
                near_ref, lhi_ref, llo_ref, cross_ref, sems, *, group):
    step = pl.program_id(0)
    block = mid_ref.shape[0]

    @pl.when(step == 0)
    def _():
        copies = [
            pltpu.make_async_copy(src, near_ref.at[pl.ds(j * block, block)], sems.at[j])
            for j, src in enumerate((below_ref, mid_ref, above_ref))
        ]
        for c in copies:
            c.start()
        lag = lag_ref[...]
        hi = lag.astype(jnp.bfloat16)
        lhi_ref[...] = hi
        llo_ref[...] = (lag - hi.astype(jnp.float32)).astype(jnp.bfloat16)
        for c in copies:
            c.wait()

    def channel(i, carry):
        s = step * group + i
        a = near_ref[own_idx[s]].astype(jnp.float32)
        a_swap = jnp.concatenate([-a[4:8], a[0:4], -a[12:16], a[8:12]], axis=0)
        for k in range(K):
            b = near_ref[far_idx[s * K + k]].astype(jnp.float32)
            m = a * b
            n = a_swap * b
            sm = m[0:8] + m[8:16]
            sn = n[0:8] + n[8:16]
            row = jnp.concatenate([sm[0:4] + sm[4:8], sn[0:4] + sn[4:8]], axis=0)
            cross_ref[pl.ds(pl.multiple_of((i * K + k) * 8, 8), 8), :] = row
        return carry

    lax.fori_loop(0, group, channel, 0, unroll=True)
    pairs = group * K
    sums = []
    for first in (0, 4):
        slab = jnp.concatenate([cross_ref[pl.ds(r, pairs, stride=8), :] for r in range(first, first + 4)], axis=1)
        hi = slab.astype(jnp.bfloat16)
        lo = (slab - hi.astype(jnp.float32)).astype(jnp.bfloat16)
        lh = lhi_ref[:, first * 128 : (first + 4) * 128]
        ll = llo_ref[:, first * 128 : (first + 4) * 128]
        sums.append(nt_dot(lh, hi) + nt_dot(lh, lo) + nt_dot(ll, hi))
    wide = lhi_ref.shape[0]
    out_ref[:wide, :] = sums[0] + sums[1]
    out_ref[wide:, :] = sums[0][0:1, :] - sums[1][0:1, :]


def nt_dot(a, b):
    return lax.dot_general(a, b, (((1,), (1,)), ((), ())), preferred_element_type=jnp.float32)


def pair_lags(blocks, own_idx, far_idx, lag, group):
    rows, sub, lanes = blocks[1].shape
    count = own_idx.shape[0]
    nlag = lag.shape[1]
    lag = lag[:, : nlag - 1].T
    steps = count // group
    hbm = pl.BlockSpec(memory_space=pl.ANY)
    spec = pltpu.PrefetchScalarGridSpec(
        num_scalar_prefetch=2,
        grid=(steps,),
        in_specs=[hbm, hbm, hbm, pl.BlockSpec(lag.shape, lambda i, o, f: (0, 0))],
        out_specs=pl.BlockSpec((nlag, group * K), lambda i, o, f: (0, i)),
        scratch_shapes=[
            pltpu.VMEM((3 * rows, sub, lanes), jnp.bfloat16),
            pltpu.VMEM(lag.shape, jnp.bfloat16),
            pltpu.VMEM(lag.shape, jnp.bfloat16),
            pltpu.VMEM((group * K * 8, 128), jnp.float32),
            pltpu.SemaphoreType.DMA((3,)),
        ],
    )
    pairs = count * K
    cost = pl.CostEstimate(flops=pairs * 2048 * 6 + 3 * 2 * pairs * 1024 * (nlag - 1), transcendentals=0,
                           bytes_accessed=3 * rows * sub * lanes * 2 + pairs * nlag * 4)
    return pl.pallas_call(
        functools.partial(pair_kernel, group=group),
        grid_spec=spec,
        out_shape=jax.ShapeDtypeStruct((nlag, pairs), jnp.float32),
        compiler_params=pltpu.CompilerParams(dimension_semantics=("arbitrary",), vmem_limit_bytes=48 * 1024 * 1024),
        cost_estimate=cost,
    )(own_idx, far_idx, *blocks, lag)


def shards(record, partners, block_owner):
    block_size, windows_dev, samples = record.shape
    width = windows_dev * 2 * NFB
    fourier = fourier_table_t(samples)
    own = whiten(record, fourier).reshape(block_size, width // 128, 128)
    near = neighbourhood(own)

    tm_count = lax.axis_size("tm")
    per_block = block_size // tm_count
    owner_row = block_owner[0]
    onehot = (owner_row[None, :] == jnp.arange(tm_count, dtype=jnp.int32)[:, None]).astype(jnp.int32)
    inverse = jnp.sum(onehot * jnp.arange(tm_count, dtype=jnp.int32)[None, :], axis=1)
    nz = 4 if tm_count % 4 == 0 else 1
    nx = tm_count // nz
    half = per_block // 2
    zx = jnp.arange(nz, dtype=jnp.int32)[:, None] + nz * jnp.arange(nx, dtype=jnp.int32)[None, :]
    xz = nz * jnp.arange(nx, dtype=jnp.int32)[:, None] + jnp.arange(nz, dtype=jnp.int32)[None, :]
    dest = jnp.stack([zx.reshape(-1), xz.reshape(-1)])
    first = inverse[dest] * per_block + jnp.arange(2, dtype=jnp.int32)[:, None] * half
    chan_local = (first[:, :, None] + jnp.arange(half, dtype=jnp.int32)[None, None, :]).reshape(-1)
    own_idx = block_size + chan_local
    base_row = lax.axis_index("chan") * block_size - block_size
    far_idx = jnp.clip(jnp.take(partners, chan_local, axis=0) - base_row, 0, 3 * block_size - 1).reshape(-1)

    partial = pair_lags(near, own_idx, far_idx, lag_table(samples), per_block)
    summed = scatter_sum(partial, nx, nz, half * K)
    scale = 1.0 / math.sqrt(windows_dev * tm_count * NFB)
    return summed.T * scale


def ring_pairs(sizes, axis, shift):
    nx, nz = sizes
    pairs = []
    for d in range(nx * nz):
        x, z = d // nz, d % nz
        if axis == 1:
            pairs.append((d, x * nz + (z + shift) % nz))
        else:
            pairs.append((d, ((x + shift) % nx) * nz + z))
    return pairs


def pick(array, index, width):
    return lax.dynamic_slice_in_dim(array, index * width, width, axis=1)


def scatter_sum(lags, nx, nz, width):
    me = lax.axis_index("tm")
    mx, mz = me // nz, me % nz
    span = nx * nz * width

    def round_(arrays):
        outs = []
        for array, mine, axis, n, size in arrays:
            acc = pick(array, mine, size)
            for shift in range(1, n):
                message = pick(array, (mine + shift) % n, size)
                acc = acc + lax.ppermute(message, "tm", ring_pairs((nx, nz), axis, shift))
            outs.append(acc)
        return outs

    def relay_round(arrays):
        firsts, outs = [], []
        for array, mine, axis, n, size in arrays:
            half = size // 2
            up_pairs = ring_pairs((nx, nz), axis, 1)
            down_pairs = ring_pairs((nx, nz), axis, n - 1)
            far = pick(array, (mine + 2) % n, size)
            firsts.append((lax.ppermute(far[:, :half], "tm", up_pairs), lax.ppermute(far[:, half:], "tm", down_pairs)))
        for (array, mine, axis, n, size), (from_below, from_above) in zip(arrays, firsts):
            half = size // 2
            up_pairs = ring_pairs((nx, nz), axis, 1)
            down_pairs = ring_pairs((nx, nz), axis, n - 1)
            up = pick(array, (mine + 1) % n, size)
            up = jnp.concatenate([up[:, :half] + from_below, up[:, half:]], axis=1)
            down = pick(array, (mine + n - 1) % n, size)
            down = jnp.concatenate([down[:, :half], down[:, half:] + from_above], axis=1)
            outs.append((array, mine, size, lax.ppermute(up, "tm", up_pairs), lax.ppermute(down, "tm", down_pairs)))
        return [pick(array, mine, size) + below + above for array, mine, size, below, above in outs]

    first_round = relay_round if nx == 4 and nz == 4 else round_
    a, b = first_round([(lags[:, :span], mz, 1, nz, nx * width), (lags[:, span:], mx, 0, nx, nz * width)])
    a, b = round_([(a, mx, 0, nx, width), (b, mz, 1, nz, width)])
    return jnp.concatenate([a, b], axis=1)


def solution(mesh):
    placed = (P("chan", "tm", None), P("chan", None), P("chan", None))
    return jax.shard_map(
        shards, mesh=mesh, in_specs=placed, out_specs=P(("chan", "tm"), None), check_vma=False
    )
```

```python
import math

import jax
import jax.numpy as jnp
from jax import lax
import functools

from jax.experimental import pallas as pl
from jax.experimental.pallas import tpu as pltpu
from jax.sharding import PartitionSpec as P

NFB = 512
F0 = 64
K = 8
LAG = 128


def split_length(samples):
    if samples % 128 == 0:
        return samples // 128, 128
    best = 1
    for b in range(1, samples + 1):
        if samples % b == 0 and b * b <= samples:
            best = b
    return samples // best, best


def angle_pair(rows, cols, padded):
    phase = (rows * cols % padded).astype(jnp.float32) * (2.0 * math.pi / padded)
    return jnp.cos(phase), jnp.sin(phase)


def fourier_table_t(samples):
    padded = 2 * samples
    outer, inner = split_length(samples)
    freqs = (F0 + jnp.arange(NFB, dtype=jnp.int32))[:, None]
    ca, sa = angle_pair(freqs, jnp.arange(outer, dtype=jnp.int32)[None, :] * inner, padded)
    cb, sb = angle_pair(freqs, jnp.arange(inner, dtype=jnp.int32)[None, :], padded)
    ca, sa = ca[:, :, None], sa[:, :, None]
    cb, sb = cb[:, None, :], sb[:, None, :]
    cos_t = (ca * cb - sa * sb).reshape(NFB, samples)
    sin_t = (sa * cb + ca * sb).reshape(NFB, samples)
    return cos_t.astype(jnp.bfloat16), (-sin_t).astype(jnp.bfloat16)


def lag_table(samples):
    padded = 2 * samples
    shifts = (jnp.arange(2 * LAG + 1, dtype=jnp.int32) - LAG)[None, :]
    fine = 16
    cu, su = angle_pair((F0 + fine * jnp.arange(NFB // fine, dtype=jnp.int32))[:, None], shifts, padded)
    cv, sv = angle_pair(jnp.arange(fine, dtype=jnp.int32)[:, None], shifts, padded)
    cu, su = cu[:, None, :], su[:, None, :]
    cv, sv = cv[None, :, :], sv[None, :, :]
    cos_t = (cu * cv - su * sv).reshape(NFB, -1)
    sin_t = (su * cv + cu * sv).reshape(NFB, -1)
    return jnp.concatenate([cos_t, -sin_t], axis=0)


def whiten(rows, fourier):
    real_part, imag_part = (
        lax.dot_general(rows, table, (((2,), (1,)), ((), ())), preferred_element_type=jnp.float32)
        for table in fourier
    )
    energy = real_part * real_part + imag_part * imag_part
    level = jnp.mean(energy, axis=-1, keepdims=True)
    divisor = jnp.sqrt(energy + 0.1 * level + 1e-05)
    parts = [(p / divisor).astype(jnp.bfloat16).reshape(p.shape[0], p.shape[1], 1, -1, 128) for p in (real_part, imag_part)]
    return jnp.concatenate(parts, axis=2).reshape(real_part.shape[0], -1, 128)


def neighbourhood(own):
    size = lax.axis_size("chan")
    up = [(i, i + 1) for i in range(size - 1)]
    down = [(j, i) for i, j in up]
    below = lax.ppermute(own, "chan", up)
    above = lax.ppermute(own, "chan", down)
    return below, own, above


def pair_kernel(own_idx, far_idx, below_ref, mid_ref, above_ref, lag_ref, out_ref,
                near_ref, lhi_ref, llo_ref, cross_ref, sems, *, group):
    step = pl.program_id(0)
    block = mid_ref.shape[0]

    @pl.when(step == 0)
    def _():
        copies = [
            pltpu.make_async_copy(src, near_ref.at[pl.ds(j * block, block)], sems.at[j])
            for j, src in enumerate((below_ref, mid_ref, above_ref))
        ]
        for c in copies:
            c.start()
        lag = lag_ref[...]
        hi = lag.astype(jnp.bfloat16)
        lhi_ref[...] = hi
        llo_ref[...] = (lag - hi.astype(jnp.float32)).astype(jnp.bfloat16)
        for c in copies:
            c.wait()

    def channel(i, carry):
        s = step * group + i
        a = near_ref[own_idx[s]].astype(jnp.float32)
        a_swap = jnp.concatenate([-a[4:8], a[0:4], -a[12:16], a[8:12]], axis=0)
        for k in range(K):
            b = near_ref[far_idx[s * K + k]].astype(jnp.float32)
            m = a * b
            n = a_swap * b
            sm = m[0:8] + m[8:16]
            sn = n[0:8] + n[8:16]
            row = jnp.concatenate([sm[0:4] + sm[4:8], sn[0:4] + sn[4:8]], axis=0)
            cross_ref[pl.ds(pl.multiple_of((i * K + k) * 8, 8), 8), :] = row
        return carry

    lax.fori_loop(0, group, channel, 0, unroll=True)
    pairs = group * K
    sums = []
    for first in (0, 4):
        slab = jnp.concatenate([cross_ref[pl.ds(r, pairs, stride=8), :] for r in range(first, first + 4)], axis=1)
        hi = slab.astype(jnp.bfloat16)
        lo = (slab - hi.astype(jnp.float32)).astype(jnp.bfloat16)
        lh = lhi_ref[:, first * 128 : (first + 4) * 128]
        ll = llo_ref[:, first * 128 : (first + 4) * 128]
        sums.append(nt_dot(lh, hi) + nt_dot(lh, lo) + nt_dot(ll, hi))
    wide = lhi_ref.shape[0]
    out_ref[:wide, :] = sums[0] + sums[1]
    out_ref[wide:, :] = sums[0][0:1, :] - sums[1][0:1, :]


def nt_dot(a, b):
    return lax.dot_general(a, b, (((1,), (1,)), ((), ())), preferred_element_type=jnp.float32)


def pair_lags(blocks, own_idx, far_idx, lag, group):
    rows, sub, lanes = blocks[1].shape
    count = own_idx.shape[0]
    nlag = lag.shape[1]
    lag = lag[:, : nlag - 1].T
    steps = count // group
    hbm = pl.BlockSpec(memory_space=pl.ANY)
    spec = pltpu.PrefetchScalarGridSpec(
        num_scalar_prefetch=2,
        grid=(steps,),
        in_specs=[hbm, hbm, hbm, pl.BlockSpec(lag.shape, lambda i, o, f: (0, 0))],
        out_specs=pl.BlockSpec((nlag, group * K), lambda i, o, f: (0, i)),
        scratch_shapes=[
            pltpu.VMEM((3 * rows, sub, lanes), jnp.bfloat16),
            pltpu.VMEM(lag.shape, jnp.bfloat16),
            pltpu.VMEM(lag.shape, jnp.bfloat16),
            pltpu.VMEM((group * K * 8, 128), jnp.float32),
            pltpu.SemaphoreType.DMA((3,)),
        ],
    )
    pairs = count * K
    cost = pl.CostEstimate(flops=pairs * 2048 * 6 + 3 * 2 * pairs * 1024 * (nlag - 1), transcendentals=0,
                           bytes_accessed=3 * rows * sub * lanes * 2 + pairs * nlag * 4)
    return pl.pallas_call(
        functools.partial(pair_kernel, group=group),
        grid_spec=spec,
        out_shape=jax.ShapeDtypeStruct((nlag, pairs), jnp.float32),
        compiler_params=pltpu.CompilerParams(dimension_semantics=("arbitrary",), vmem_limit_bytes=48 * 1024 * 1024),
        cost_estimate=cost,
    )(own_idx, far_idx, *blocks, lag)


def shards(record, partners, block_owner):
    block_size, windows_dev, samples = record.shape
    width = windows_dev * 2 * NFB
    fourier = fourier_table_t(samples)
    own = whiten(record, fourier)
    near = neighbourhood(own)

    tm_count = lax.axis_size("tm")
    per_block = block_size // tm_count
    owner_row = block_owner[0]
    onehot = (owner_row[None, :] == jnp.arange(tm_count, dtype=jnp.int32)[:, None]).astype(jnp.int32)
    inverse = jnp.sum(onehot * jnp.arange(tm_count, dtype=jnp.int32)[None, :], axis=1)
    nz = 4 if tm_count % 4 == 0 else 1
    nx = tm_count // nz
    half = per_block // 2
    zx = jnp.arange(nz, dtype=jnp.int32)[:, None] + nz * jnp.arange(nx, dtype=jnp.int32)[None, :]
    xz = nz * jnp.arange(nx, dtype=jnp.int32)[:, None] + jnp.arange(nz, dtype=jnp.int32)[None, :]
    dest = jnp.stack([zx.reshape(-1), xz.reshape(-1)])
    first = inverse[dest] * per_block + jnp.arange(2, dtype=jnp.int32)[:, None] * half
    chan_local = (first[:, :, None] + jnp.arange(half, dtype=jnp.int32)[None, None, :]).reshape(-1)
    own_idx = block_size + chan_local
    base_row = lax.axis_index("chan") * block_size - block_size
    far_idx = jnp.clip(jnp.take(partners, chan_local, axis=0) - base_row, 0, 3 * block_size - 1).reshape(-1)

    partial = pair_lags(near, own_idx, far_idx, lag_table(samples), per_block)
    summed = scatter_sum(partial, nx, nz, half * K)
    scale = 1.0 / math.sqrt(windows_dev * tm_count * NFB)
    return summed.T * scale


def ring_pairs(sizes, axis, shift):
    nx, nz = sizes
    pairs = []
    for d in range(nx * nz):
        x, z = d // nz, d % nz
        if axis == 1:
            pairs.append((d, x * nz + (z + shift) % nz))
        else:
            pairs.append((d, ((x + shift) % nx) * nz + z))
    return pairs


def pick(array, index, width):
    return lax.dynamic_slice_in_dim(array, index * width, width, axis=1)


def scatter_sum(lags, nx, nz, width):
    me = lax.axis_index("tm")
    mx, mz = me // nz, me % nz
    span = nx * nz * width

    def round_(arrays):
        outs = []
        for array, mine, axis, n, size in arrays:
            acc = pick(array, mine, size)
            for shift in range(1, n):
                message = pick(array, (mine + shift) % n, size)
                acc = acc + lax.ppermute(message, "tm", ring_pairs((nx, nz), axis, shift))
            outs.append(acc)
        return outs

    def relay_round(arrays):
        firsts, outs = [], []
        for array, mine, axis, n, size in arrays:
            half = size // 2
            up_pairs = ring_pairs((nx, nz), axis, 1)
            down_pairs = ring_pairs((nx, nz), axis, n - 1)
            far = pick(array, (mine + 2) % n, size)
            firsts.append((lax.ppermute(far[:, :half], "tm", up_pairs), lax.ppermute(far[:, half:], "tm", down_pairs)))
        for (array, mine, axis, n, size), (from_below, from_above) in zip(arrays, firsts):
            half = size // 2
            up_pairs = ring_pairs((nx, nz), axis, 1)
            down_pairs = ring_pairs((nx, nz), axis, n - 1)
            up = pick(array, (mine + 1) % n, size)
            up = jnp.concatenate([up[:, :half] + from_below, up[:, half:]], axis=1)
            down = pick(array, (mine + n - 1) % n, size)
            down = jnp.concatenate([down[:, :half], down[:, half:] + from_above], axis=1)
            outs.append((array, mine, size, lax.ppermute(up, "tm", up_pairs), lax.ppermute(down, "tm", down_pairs)))
        return [pick(array, mine, size) + below + above for array, mine, size, below, above in outs]

    first_round = relay_round if nx == 4 and nz == 4 else round_
    a, b = first_round([(lags[:, :span], mz, 1, nz, nx * width), (lags[:, span:], mx, 0, nx, nz * width)])
    a, b = round_([(a, mx, 0, nx, width), (b, mz, 1, nz, width)])
    return jnp.concatenate([a, b], axis=1)


def solution(mesh):
    placed = (P("chan", "tm", None), P("chan", None), P("chan", None))
    return jax.shard_map(
        shards, mesh=mesh, in_specs=placed, out_specs=P(("chan", "tm"), None), check_vma=False
    )
```

```python
import math

import jax
import jax.numpy as jnp
from jax import lax
import functools

from jax.experimental import pallas as pl
from jax.experimental.pallas import tpu as pltpu
from jax.sharding import PartitionSpec as P

NFB = 512
F0 = 64
K = 8
LAG = 128


def split_length(samples):
    if samples % 128 == 0:
        return samples // 128, 128
    best = 1
    for b in range(1, samples + 1):
        if samples % b == 0 and b * b <= samples:
            best = b
    return samples // best, best


def angle_pair(rows, cols, padded):
    phase = (rows * cols % padded).astype(jnp.float32) * (2.0 * math.pi / padded)
    return jnp.cos(phase), jnp.sin(phase)


def fourier_table_t(samples):
    padded = 2 * samples
    outer, inner = split_length(samples)
    freqs = (F0 + jnp.arange(NFB, dtype=jnp.int32))[:, None]
    ca, sa = angle_pair(freqs, jnp.arange(outer, dtype=jnp.int32)[None, :] * inner, padded)
    cb, sb = angle_pair(freqs, jnp.arange(inner, dtype=jnp.int32)[None, :], padded)
    ca, sa = ca[:, :, None], sa[:, :, None]
    cb, sb = cb[:, None, :], sb[:, None, :]
    cos_t = (ca * cb - sa * sb).reshape(NFB, samples)
    sin_t = (sa * cb + ca * sb).reshape(NFB, samples)
    return cos_t.astype(jnp.bfloat16), (-sin_t).astype(jnp.bfloat16)


def lag_table(samples):
    padded = 2 * samples
    shifts = (jnp.arange(2 * LAG + 1, dtype=jnp.int32) - LAG)[None, :]
    fine = 16
    cu, su = angle_pair((F0 + fine * jnp.arange(NFB // fine, dtype=jnp.int32))[:, None], shifts, padded)
    cv, sv = angle_pair(jnp.arange(fine, dtype=jnp.int32)[:, None], shifts, padded)
    cu, su = cu[:, None, :], su[:, None, :]
    cv, sv = cv[None, :, :], sv[None, :, :]
    cos_t = (cu * cv - su * sv).reshape(NFB, -1)
    sin_t = (su * cv + cu * sv).reshape(NFB, -1)
    return jnp.concatenate([cos_t, -sin_t], axis=0)


def whiten(rows, fourier):
    real_part, imag_part = (
        lax.dot_general(rows, table, (((2,), (1,)), ((), ())), preferred_element_type=jnp.float32)
        for table in fourier
    )
    energy = real_part * real_part + imag_part * imag_part
    level = jnp.mean(energy, axis=-1, keepdims=True)
    divisor = jnp.sqrt(energy + 0.1 * level + 1e-05)
    whitened = jnp.concatenate([real_part / divisor, imag_part / divisor], axis=-1)
    return whitened.astype(jnp.bfloat16)


def neighbourhood(own):
    size = lax.axis_size("chan")
    up = [(i, i + 1) for i in range(size - 1)]
    down = [(j, i) for i, j in up]
    cut = own.shape[0] // 2
    pieces = [own[:cut], own[cut:]]
    below = [lax.ppermute(p, "chan", up) for p in pieces]
    above = [lax.ppermute(p, "chan", down) for p in pieces]
    return below + [own] + above


def pair_kernel(own_idx, far_idx, *refs, group, count):
    block_refs = refs[:count]
    lag_ref, out_ref, near_ref, lhi_ref, llo_ref, cross_ref, sems = refs[count:]
    step = pl.program_id(0)

    @pl.when(step == 0)
    def _():
        copies = []
        start = 0
        for j, src in enumerate(block_refs):
            copies.append(pltpu.make_async_copy(src, near_ref.at[pl.ds(start, src.shape[0])], sems.at[j]))
            start += src.shape[0]
        for c in copies:
            c.start()
        lag = lag_ref[...]
        hi = lag.astype(jnp.bfloat16)
        lhi_ref[...] = hi
        llo_ref[...] = (lag - hi.astype(jnp.float32)).astype(jnp.bfloat16)
        for c in copies:
            c.wait()

    def channel(i, carry):
        s = step * group + i
        a = near_ref[own_idx[s]].astype(jnp.float32)
        a_swap = jnp.concatenate([-a[4:8], a[0:4], -a[12:16], a[8:12]], axis=0)
        for k in range(K):
            b = near_ref[far_idx[s * K + k]].astype(jnp.float32)
            m = a * b
            n = a_swap * b
            sm = m[0:8] + m[8:16]
            sn = n[0:8] + n[8:16]
            row = jnp.concatenate([sm[0:4] + sm[4:8], sn[0:4] + sn[4:8]], axis=0)
            cross_ref[pl.ds(pl.multiple_of((i * K + k) * 8, 8), 8), :] = row
        return carry

    lax.fori_loop(0, group, channel, 0, unroll=True)
    pairs = group * K
    sums = []
    for first in (0, 4):
        slab = jnp.concatenate([cross_ref[pl.ds(r, pairs, stride=8), :] for r in range(first, first + 4)], axis=1)
        hi = slab.astype(jnp.bfloat16)
        lo = (slab - hi.astype(jnp.float32)).astype(jnp.bfloat16)
        lh = lhi_ref[:, first * 128 : (first + 4) * 128]
        ll = llo_ref[:, first * 128 : (first + 4) * 128]
        sums.append(nt_dot(lh, hi) + nt_dot(lh, lo) + nt_dot(ll, hi))
    wide = lhi_ref.shape[0]
    out_ref[:wide, :] = sums[0] + sums[1]
    out_ref[wide:, :] = sums[0][0:1, :] - sums[1][0:1, :]


def nt_dot(a, b):
    return lax.dot_general(a, b, (((1,), (1,)), ((), ())), preferred_element_type=jnp.float32)


def pair_lags(blocks, own_idx, far_idx, lag, group):
    rows = sum(b.shape[0] for b in blocks)
    sub, lanes = blocks[0].shape[1:]
    count = own_idx.shape[0]
    nlag = lag.shape[1]
    lag = lag[:, : nlag - 1].T
    steps = count // group
    hbm = pl.BlockSpec(memory_space=pl.ANY)
    spec = pltpu.PrefetchScalarGridSpec(
        num_scalar_prefetch=2,
        grid=(steps,),
        in_specs=[hbm] * len(blocks) + [pl.BlockSpec(lag.shape, lambda i, o, f: (0, 0))],
        out_specs=pl.BlockSpec((nlag, group * K), lambda i, o, f: (0, i)),
        scratch_shapes=[
            pltpu.VMEM((rows, sub, lanes), jnp.bfloat16),
            pltpu.VMEM(lag.shape, jnp.bfloat16),
            pltpu.VMEM(lag.shape, jnp.bfloat16),
            pltpu.VMEM((group * K * 8, 128), jnp.float32),
            pltpu.SemaphoreType.DMA((len(blocks),)),
        ],
    )
    pairs = count * K
    cost = pl.CostEstimate(flops=pairs * 2048 * 6 + 3 * 2 * pairs * 1024 * (nlag - 1), transcendentals=0,
                           bytes_accessed=rows * sub * lanes * 2 + pairs * nlag * 4)
    return pl.pallas_call(
        functools.partial(pair_kernel, group=group, count=len(blocks)),
        grid_spec=spec,
        out_shape=jax.ShapeDtypeStruct((nlag, pairs), jnp.float32),
        compiler_params=pltpu.CompilerParams(dimension_semantics=("arbitrary",), vmem_limit_bytes=48 * 1024 * 1024),
        cost_estimate=cost,
    )(own_idx, far_idx, *blocks, lag)


def shards(record, partners, block_owner):
    block_size, windows_dev, samples = record.shape
    width = windows_dev * 2 * NFB
    fourier = fourier_table_t(samples)
    own = whiten(record, fourier).reshape(block_size, width // 128, 128)
    near = neighbourhood(own)

    tm_count = lax.axis_size("tm")
    per_block = block_size // tm_count
    owner_row = block_owner[0]
    onehot = (owner_row[None, :] == jnp.arange(tm_count, dtype=jnp.int32)[:, None]).astype(jnp.int32)
    inverse = jnp.sum(onehot * jnp.arange(tm_count, dtype=jnp.int32)[None, :], axis=1)
    nz = 4 if tm_count % 4 == 0 else 1
    nx = tm_count // nz
    half = per_block // 2
    zx = jnp.arange(nz, dtype=jnp.int32)[:, None] + nz * jnp.arange(nx, dtype=jnp.int32)[None, :]
    xz = nz * jnp.arange(nx, dtype=jnp.int32)[:, None] + jnp.arange(nz, dtype=jnp.int32)[None, :]
    dest = jnp.stack([zx.reshape(-1), xz.reshape(-1)])
    first = inverse[dest] * per_block + jnp.arange(2, dtype=jnp.int32)[:, None] * half
    chan_local = (first[:, :, None] + jnp.arange(half, dtype=jnp.int32)[None, None, :]).reshape(-1)
    own_idx = block_size + chan_local
    base_row = lax.axis_index("chan") * block_size - block_size
    far_idx = jnp.clip(jnp.take(partners, chan_local, axis=0) - base_row, 0, 3 * block_size - 1).reshape(-1)

    partial = pair_lags(near, own_idx, far_idx, lag_table(samples), per_block)
    summed = scatter_sum(partial, nx, nz, half * K)
    scale = 1.0 / math.sqrt(windows_dev * tm_count * NFB)
    return summed.T * scale


def ring_pairs(sizes, axis, shift):
    nx, nz = sizes
    pairs = []
    for d in range(nx * nz):
        x, z = d // nz, d % nz
        if axis == 1:
            pairs.append((d, x * nz + (z + shift) % nz))
        else:
            pairs.append((d, ((x + shift) % nx) * nz + z))
    return pairs


def pick(array, index, width):
    return lax.dynamic_slice_in_dim(array, index * width, width, axis=1)


def scatter_sum(lags, nx, nz, width):
    me = lax.axis_index("tm")
    mx, mz = me // nz, me % nz
    span = nx * nz * width

    def round_(arrays):
        outs = []
        for array, mine, axis, n, size in arrays:
            acc = pick(array, mine, size)
            for shift in range(1, n):
                message = pick(array, (mine + shift) % n, size)
                acc = acc + lax.ppermute(message, "tm", ring_pairs((nx, nz), axis, shift))
            outs.append(acc)
        return outs

    def relay_round(arrays):
        firsts, outs = [], []
        for array, mine, axis, n, size in arrays:
            half = size // 2
            up_pairs = ring_pairs((nx, nz), axis, 1)
            down_pairs = ring_pairs((nx, nz), axis, n - 1)
            far = pick(array, (mine + 2) % n, size)
            firsts.append((lax.ppermute(far[:, :half], "tm", up_pairs), lax.ppermute(far[:, half:], "tm", down_pairs)))
        for (array, mine, axis, n, size), (from_below, from_above) in zip(arrays, firsts):
            half = size // 2
            up_pairs = ring_pairs((nx, nz), axis, 1)
            down_pairs = ring_pairs((nx, nz), axis, n - 1)
            up = pick(array, (mine + 1) % n, size)
            up = jnp.concatenate([up[:, :half] + from_below, up[:, half:]], axis=1)
            down = pick(array, (mine + n - 1) % n, size)
            down = jnp.concatenate([down[:, :half], down[:, half:] + from_above], axis=1)
            outs.append((array, mine, size, lax.ppermute(up, "tm", up_pairs), lax.ppermute(down, "tm", down_pairs)))
        return [pick(array, mine, size) + below + above for array, mine, size, below, above in outs]

    first_round = relay_round if nx == 4 and nz == 4 else round_
    a, b = first_round([(lags[:, :span], mz, 1, nz, nx * width), (lags[:, span:], mx, 0, nx, nz * width)])
    a, b = round_([(a, mx, 0, nx, width), (b, mz, 1, nz, width)])
    return jnp.concatenate([a, b], axis=1)


def solution(mesh):
    placed = (P("chan", "tm", None), P("chan", None), P("chan", None))
    return jax.shard_map(
        shards, mesh=mesh, in_specs=placed, out_specs=P(("chan", "tm"), None), check_vma=False
    )
```

```python
import math

import jax
import jax.numpy as jnp
from jax import lax
import functools

from jax.experimental import pallas as pl
from jax.experimental.pallas import tpu as pltpu
from jax.sharding import PartitionSpec as P

NFB = 512
F0 = 64
K = 8
LAG = 128


def split_length(samples):
    if samples % 128 == 0:
        return samples // 128, 128
    best = 1
    for b in range(1, samples + 1):
        if samples % b == 0 and b * b <= samples:
            best = b
    return samples // best, best


def angle_pair(rows, cols, padded):
    phase = (rows * cols % padded).astype(jnp.float32) * (2.0 * math.pi / padded)
    return jnp.cos(phase), jnp.sin(phase)


def fourier_table_t(samples):
    padded = 2 * samples
    outer, inner = split_length(samples)
    freqs = (F0 + jnp.arange(NFB, dtype=jnp.int32))[:, None]
    ca, sa = angle_pair(freqs, jnp.arange(outer, dtype=jnp.int32)[None, :] * inner, padded)
    cb, sb = angle_pair(freqs, jnp.arange(inner, dtype=jnp.int32)[None, :], padded)
    ca, sa = ca[:, :, None], sa[:, :, None]
    cb, sb = cb[:, None, :], sb[:, None, :]
    cos_t = (ca * cb - sa * sb).reshape(NFB, samples)
    sin_t = (sa * cb + ca * sb).reshape(NFB, samples)
    return cos_t.astype(jnp.bfloat16), (-sin_t).astype(jnp.bfloat16)


def lag_table(samples):
    padded = 2 * samples
    shifts = (jnp.arange(2 * LAG + 1, dtype=jnp.int32) - LAG)[None, :]
    fine = 16
    cu, su = angle_pair((F0 + fine * jnp.arange(NFB // fine, dtype=jnp.int32))[:, None], shifts, padded)
    cv, sv = angle_pair(jnp.arange(fine, dtype=jnp.int32)[:, None], shifts, padded)
    cu, su = cu[:, None, :], su[:, None, :]
    cv, sv = cv[None, :, :], sv[None, :, :]
    cos_t = (cu * cv - su * sv).reshape(NFB, -1)
    sin_t = (su * cv + cu * sv).reshape(NFB, -1)
    return jnp.concatenate([cos_t, -sin_t], axis=0)


def whiten(rows, fourier):
    real_part, imag_part = (
        lax.dot_general(rows, table, (((2,), (1,)), ((), ())), preferred_element_type=jnp.float32)
        for table in fourier
    )
    energy = real_part * real_part + imag_part * imag_part
    level = jnp.mean(energy, axis=-1, keepdims=True)
    divisor = jnp.sqrt(energy + 0.1 * level + 1e-05)
    whitened = jnp.concatenate([real_part / divisor, imag_part / divisor], axis=-1)
    return whitened.astype(jnp.bfloat16)


def neighbourhood(own):
    size = lax.axis_size("chan")
    up = [(i, i + 1) for i in range(size - 1)]
    down = [(j, i) for i, j in up]
    below = lax.ppermute(own, "chan", up)
    above = lax.ppermute(own, "chan", down)
    return below, own, above


def pair_kernel(own_idx, far_idx, below_ref, mid_ref, above_ref, lag_ref, out_ref,
                near_ref, lhi_ref, llo_ref, even_ref, odd_ref, sems, *, group, steps):
    step = pl.program_id(0)
    block = mid_ref.shape[0]

    @pl.when(step == 0)
    def _():
        copies = [
            pltpu.make_async_copy(src, near_ref.at[pl.ds(j * block, block)], sems.at[j])
            for j, src in enumerate((below_ref, mid_ref, above_ref))
        ]
        for c in copies:
            c.start()
        lag = lag_ref[...]
        hi = lag.astype(jnp.bfloat16)
        lhi_ref[...] = hi
        llo_ref[...] = (lag - hi.astype(jnp.float32)).astype(jnp.bfloat16)
        odd_ref[...] = jnp.zeros_like(odd_ref)
        for c in copies:
            c.wait()

    current = jnp.minimum(step, steps - 1)
    pairs = group * K

    def body(write_ref, read_ref):
        def channel(i, carry):
            s = current * group + i
            a = near_ref[own_idx[s]].astype(jnp.float32)
            a_swap = jnp.concatenate([-a[4:8], a[0:4], -a[12:16], a[8:12]], axis=0)
            for k in range(K):
                b = near_ref[far_idx[s * K + k]].astype(jnp.float32)
                m = a * b
                n = a_swap * b
                sm = m[0:8] + m[8:16]
                sn = n[0:8] + n[8:16]
                row = jnp.concatenate([sm[0:4] + sm[4:8], sn[0:4] + sn[4:8]], axis=0)
                write_ref[pl.ds(pl.multiple_of((i * K + k) * 8, 8), 8), :] = row
            return carry

        sums = []
        for first in (0, 4):
            slab = jnp.concatenate([read_ref[pl.ds(r, pairs, stride=8), :] for r in range(first, first + 4)], axis=1)
            hi = slab.astype(jnp.bfloat16)
            lo = (slab - hi.astype(jnp.float32)).astype(jnp.bfloat16)
            lh = lhi_ref[:, first * 128 : (first + 4) * 128]
            ll = llo_ref[:, first * 128 : (first + 4) * 128]
            sums.append(nt_dot(lh, hi) + nt_dot(lh, lo) + nt_dot(ll, hi))
        lax.fori_loop(0, group, channel, 0, unroll=True)
        wide = lhi_ref.shape[0]
        out_ref[:wide, :] = sums[0] + sums[1]
        out_ref[wide:, :] = sums[0][0:1, :] - sums[1][0:1, :]

    @pl.when(step % 2 == 0)
    def _():
        body(even_ref, odd_ref)

    @pl.when(step % 2 == 1)
    def _():
        body(odd_ref, even_ref)


def nt_dot(a, b):
    return lax.dot_general(a, b, (((1,), (1,)), ((), ())), preferred_element_type=jnp.float32)


def pair_lags(blocks, own_idx, far_idx, lag, group):
    rows, sub, lanes = blocks[1].shape
    count = own_idx.shape[0]
    nlag = lag.shape[1]
    lag = lag[:, : nlag - 1].T
    steps = count // group
    hbm = pl.BlockSpec(memory_space=pl.ANY)
    spec = pltpu.PrefetchScalarGridSpec(
        num_scalar_prefetch=2,
        grid=(steps + 1,),
        in_specs=[hbm, hbm, hbm, pl.BlockSpec(lag.shape, lambda i, o, f: (0, 0))],
        out_specs=pl.BlockSpec((nlag, group * K), lambda i, o, f: (0, jnp.maximum(i - 1, 0))),
        scratch_shapes=[
            pltpu.VMEM((3 * rows, sub, lanes), jnp.bfloat16),
            pltpu.VMEM(lag.shape, jnp.bfloat16),
            pltpu.VMEM(lag.shape, jnp.bfloat16),
            pltpu.VMEM((group * K * 8, 128), jnp.float32),
            pltpu.VMEM((group * K * 8, 128), jnp.float32),
            pltpu.SemaphoreType.DMA((3,)),
        ],
    )
    pairs = count * K
    cost = pl.CostEstimate(flops=pairs * 2048 * 6 + 3 * 2 * pairs * 1024 * (nlag - 1), transcendentals=0,
                           bytes_accessed=3 * rows * sub * lanes * 2 + pairs * nlag * 4)
    return pl.pallas_call(
        functools.partial(pair_kernel, group=group, steps=steps),
        grid_spec=spec,
        out_shape=jax.ShapeDtypeStruct((nlag, pairs), jnp.float32),
        compiler_params=pltpu.CompilerParams(dimension_semantics=("arbitrary",), vmem_limit_bytes=48 * 1024 * 1024),
        cost_estimate=cost,
    )(own_idx, far_idx, *blocks, lag)


def shards(record, partners, block_owner):
    block_size, windows_dev, samples = record.shape
    width = windows_dev * 2 * NFB
    fourier = fourier_table_t(samples)
    own = whiten(record, fourier).reshape(block_size, width // 128, 128)
    near = neighbourhood(own)

    tm_count = lax.axis_size("tm")
    per_block = block_size // tm_count
    owner_row = block_owner[0]
    onehot = (owner_row[None, :] == jnp.arange(tm_count, dtype=jnp.int32)[:, None]).astype(jnp.int32)
    inverse = jnp.sum(onehot * jnp.arange(tm_count, dtype=jnp.int32)[None, :], axis=1)
    nz = 4 if tm_count % 4 == 0 else 1
    nx = tm_count // nz
    half = per_block // 2
    zx = jnp.arange(nz, dtype=jnp.int32)[:, None] + nz * jnp.arange(nx, dtype=jnp.int32)[None, :]
    xz = nz * jnp.arange(nx, dtype=jnp.int32)[:, None] + jnp.arange(nz, dtype=jnp.int32)[None, :]
    dest = jnp.stack([zx.reshape(-1), xz.reshape(-1)])
    first = inverse[dest] * per_block + jnp.arange(2, dtype=jnp.int32)[:, None] * half
    chan_local = (first[:, :, None] + jnp.arange(half, dtype=jnp.int32)[None, None, :]).reshape(-1)
    own_idx = block_size + chan_local
    base_row = lax.axis_index("chan") * block_size - block_size
    far_idx = jnp.clip(jnp.take(partners, chan_local, axis=0) - base_row, 0, 3 * block_size - 1).reshape(-1)

    partial = pair_lags(near, own_idx, far_idx, lag_table(samples), per_block)
    summed = scatter_sum(partial, nx, nz, half * K)
    scale = 1.0 / math.sqrt(windows_dev * tm_count * NFB)
    return summed.T * scale


def ring_pairs(sizes, axis, shift):
    nx, nz = sizes
    pairs = []
    for d in range(nx * nz):
        x, z = d // nz, d % nz
        if axis == 1:
            pairs.append((d, x * nz + (z + shift) % nz))
        else:
            pairs.append((d, ((x + shift) % nx) * nz + z))
    return pairs


def pick(array, index, width):
    return lax.dynamic_slice_in_dim(array, index * width, width, axis=1)


def scatter_sum(lags, nx, nz, width):
    me = lax.axis_index("tm")
    mx, mz = me // nz, me % nz
    span = nx * nz * width

    def round_(arrays):
        outs = []
        for array, mine, axis, n, size in arrays:
            acc = pick(array, mine, size)
            for shift in range(1, n):
                message = pick(array, (mine + shift) % n, size)
                acc = acc + lax.ppermute(message, "tm", ring_pairs((nx, nz), axis, shift))
            outs.append(acc)
        return outs

    def relay_round(arrays):
        firsts, outs = [], []
        for array, mine, axis, n, size in arrays:
            half = size // 2
            up_pairs = ring_pairs((nx, nz), axis, 1)
            down_pairs = ring_pairs((nx, nz), axis, n - 1)
            far = pick(array, (mine + 2) % n, size)
            firsts.append((lax.ppermute(far[:, :half], "tm", up_pairs), lax.ppermute(far[:, half:], "tm", down_pairs)))
        for (array, mine, axis, n, size), (from_below, from_above) in zip(arrays, firsts):
            half = size // 2
            up_pairs = ring_pairs((nx, nz), axis, 1)
            down_pairs = ring_pairs((nx, nz), axis, n - 1)
            up = pick(array, (mine + 1) % n, size)
            up = jnp.concatenate([up[:, :half] + from_below, up[:, half:]], axis=1)
            down = pick(array, (mine + n - 1) % n, size)
            down = jnp.concatenate([down[:, :half], down[:, half:] + from_above], axis=1)
            outs.append((array, mine, size, lax.ppermute(up, "tm", up_pairs), lax.ppermute(down, "tm", down_pairs)))
        return [pick(array, mine, size) + below + above for array, mine, size, below, above in outs]

    first_round = relay_round if nx == 4 and nz == 4 else round_
    a, b = first_round([(lags[:, :span], mz, 1, nz, nx * width), (lags[:, span:], mx, 0, nx, nz * width)])
    a, b = round_([(a, mx, 0, nx, width), (b, mz, 1, nz, width)])
    return jnp.concatenate([a, b], axis=1)


def solution(mesh):
    placed = (P("chan", "tm", None), P("chan", None), P("chan", None))
    return jax.shard_map(
        shards, mesh=mesh, in_specs=placed, out_specs=P(("chan", "tm"), None), check_vma=False
    )
```

```python
import math

import jax
import jax.numpy as jnp
from jax import lax
import functools

from jax.experimental import pallas as pl
from jax.experimental.pallas import tpu as pltpu
from jax.sharding import PartitionSpec as P

NFB = 512
F0 = 64
K = 8
LAG = 128


def split_length(samples):
    if samples % 128 == 0:
        return samples // 128, 128
    best = 1
    for b in range(1, samples + 1):
        if samples % b == 0 and b * b <= samples:
            best = b
    return samples // best, best


def angle_pair(rows, cols, padded):
    phase = (rows * cols % padded).astype(jnp.float32) * (2.0 * math.pi / padded)
    return jnp.cos(phase), jnp.sin(phase)


def fourier_table_t(samples):
    padded = 2 * samples
    outer, inner = split_length(samples)
    freqs = (F0 + jnp.arange(NFB, dtype=jnp.int32))[:, None]
    ca, sa = angle_pair(freqs, jnp.arange(outer, dtype=jnp.int32)[None, :] * inner, padded)
    cb, sb = angle_pair(freqs, jnp.arange(inner, dtype=jnp.int32)[None, :], padded)
    ca, sa = ca[:, :, None], sa[:, :, None]
    cb, sb = cb[:, None, :], sb[:, None, :]
    cos_t = (ca * cb - sa * sb).reshape(NFB, samples)
    sin_t = (sa * cb + ca * sb).reshape(NFB, samples)
    return cos_t.astype(jnp.bfloat16), (-sin_t).astype(jnp.bfloat16)


def lag_table(samples):
    padded = 2 * samples
    shifts = (jnp.arange(2 * LAG + 1, dtype=jnp.int32) - LAG)[None, :]
    fine = 16
    cu, su = angle_pair((F0 + fine * jnp.arange(NFB // fine, dtype=jnp.int32))[:, None], shifts, padded)
    cv, sv = angle_pair(jnp.arange(fine, dtype=jnp.int32)[:, None], shifts, padded)
    cu, su = cu[:, None, :], su[:, None, :]
    cv, sv = cv[None, :, :], sv[None, :, :]
    cos_t = (cu * cv - su * sv).reshape(NFB, -1)
    sin_t = (su * cv + cu * sv).reshape(NFB, -1)
    return jnp.concatenate([cos_t, -sin_t], axis=0)


def whiten(rows, fourier):
    real_part, imag_part = (
        lax.dot_general(rows, table, (((2,), (1,)), ((), ())), preferred_element_type=jnp.float32)
        for table in fourier
    )
    energy = real_part * real_part + imag_part * imag_part
    level = jnp.mean(energy, axis=-1, keepdims=True)
    divisor = jnp.sqrt(energy + 0.1 * level + 1e-05)
    whitened = jnp.concatenate([real_part / divisor, imag_part / divisor], axis=-1)
    return whitened.astype(jnp.bfloat16)


def neighbourhood(pieces):
    size = lax.axis_size("chan")
    up = [(i, i + 1) for i in range(size - 1)]
    down = [(j, i) for i, j in up]
    below = [lax.ppermute(p, "chan", up) for p in pieces]
    above = [lax.ppermute(p, "chan", down) for p in pieces]
    return below + pieces + above


def pair_kernel(own_idx, far_idx, *refs, group, count):
    block_refs = refs[:count]
    lag_ref, out_ref, near_ref, lhi_ref, llo_ref, cross_ref, sems = refs[count:]
    step = pl.program_id(0)

    @pl.when(step == 0)
    def _():
        copies = []
        start = 0
        for j, src in enumerate(block_refs):
            copies.append(pltpu.make_async_copy(src, near_ref.at[pl.ds(start, src.shape[0])], sems.at[j]))
            start += src.shape[0]
        for c in copies:
            c.start()
        lag = lag_ref[...]
        hi = lag.astype(jnp.bfloat16)
        lhi_ref[...] = hi
        llo_ref[...] = (lag - hi.astype(jnp.float32)).astype(jnp.bfloat16)
        for c in copies:
            c.wait()

    def channel(i, carry):
        s = step * group + i
        a = near_ref[own_idx[s]].astype(jnp.float32)
        a_swap = jnp.concatenate([-a[4:8], a[0:4], -a[12:16], a[8:12]], axis=0)
        for k in range(K):
            b = near_ref[far_idx[s * K + k]].astype(jnp.float32)
            m = a * b
            n = a_swap * b
            sm = m[0:8] + m[8:16]
            sn = n[0:8] + n[8:16]
            row = jnp.concatenate([sm[0:4] + sm[4:8], sn[0:4] + sn[4:8]], axis=0)
            cross_ref[pl.ds(pl.multiple_of((i * K + k) * 8, 8), 8), :] = row
        return carry

    lax.fori_loop(0, group, channel, 0, unroll=True)
    pairs = group * K
    sums = []
    for first in (0, 4):
        slab = jnp.concatenate([cross_ref[pl.ds(r, pairs, stride=8), :] for r in range(first, first + 4)], axis=1)
        hi = slab.astype(jnp.bfloat16)
        lo = (slab - hi.astype(jnp.float32)).astype(jnp.bfloat16)
        lh = lhi_ref[:, first * 128 : (first + 4) * 128]
        ll = llo_ref[:, first * 128 : (first + 4) * 128]
        sums.append(nt_dot(lh, hi) + nt_dot(lh, lo) + nt_dot(ll, hi))
    wide = lhi_ref.shape[0]
    out_ref[:wide, :] = sums[0] + sums[1]
    out_ref[wide:, :] = sums[0][0:1, :] - sums[1][0:1, :]


def nt_dot(a, b):
    return lax.dot_general(a, b, (((1,), (1,)), ((), ())), preferred_element_type=jnp.float32)


def pair_lags(blocks, own_idx, far_idx, lag, group):
    rows = sum(b.shape[0] for b in blocks)
    sub, lanes = blocks[0].shape[1:]
    count = own_idx.shape[0]
    nlag = lag.shape[1]
    lag = lag[:, : nlag - 1].T
    steps = count // group
    hbm = pl.BlockSpec(memory_space=pl.ANY)
    spec = pltpu.PrefetchScalarGridSpec(
        num_scalar_prefetch=2,
        grid=(steps,),
        in_specs=[hbm] * len(blocks) + [pl.BlockSpec(lag.shape, lambda i, o, f: (0, 0))],
        out_specs=pl.BlockSpec((nlag, group * K), lambda i, o, f: (0, i)),
        scratch_shapes=[
            pltpu.VMEM((rows, sub, lanes), jnp.bfloat16),
            pltpu.VMEM(lag.shape, jnp.bfloat16),
            pltpu.VMEM(lag.shape, jnp.bfloat16),
            pltpu.VMEM((group * K * 8, 128), jnp.float32),
            pltpu.SemaphoreType.DMA((len(blocks),)),
        ],
    )
    pairs = count * K
    cost = pl.CostEstimate(flops=pairs * 2048 * 6 + 3 * 2 * pairs * 1024 * (nlag - 1), transcendentals=0,
                           bytes_accessed=rows * sub * lanes * 2 + pairs * nlag * 4)
    return pl.pallas_call(
        functools.partial(pair_kernel, group=group, count=len(blocks)),
        grid_spec=spec,
        out_shape=jax.ShapeDtypeStruct((nlag, pairs), jnp.float32),
        compiler_params=pltpu.CompilerParams(dimension_semantics=("arbitrary",), vmem_limit_bytes=48 * 1024 * 1024),
        cost_estimate=cost,
    )(own_idx, far_idx, *blocks, lag)


def shards(record, partners, block_owner):
    block_size, windows_dev, samples = record.shape
    width = windows_dev * 2 * NFB
    fourier = fourier_table_t(samples)
    cut = block_size // 2
    near = neighbourhood([
        whiten(part, fourier).reshape(cut, width // 128, 128) for part in (record[:cut], record[cut:])
    ])

    tm_count = lax.axis_size("tm")
    per_block = block_size // tm_count
    owner_row = block_owner[0]
    onehot = (owner_row[None, :] == jnp.arange(tm_count, dtype=jnp.int32)[:, None]).astype(jnp.int32)
    inverse = jnp.sum(onehot * jnp.arange(tm_count, dtype=jnp.int32)[None, :], axis=1)
    nz = 4 if tm_count % 4 == 0 else 1
    nx = tm_count // nz
    half = per_block // 2
    zx = jnp.arange(nz, dtype=jnp.int32)[:, None] + nz * jnp.arange(nx, dtype=jnp.int32)[None, :]
    xz = nz * jnp.arange(nx, dtype=jnp.int32)[:, None] + jnp.arange(nz, dtype=jnp.int32)[None, :]
    dest = jnp.stack([zx.reshape(-1), xz.reshape(-1)])
    first = inverse[dest] * per_block + jnp.arange(2, dtype=jnp.int32)[:, None] * half
    chan_local = (first[:, :, None] + jnp.arange(half, dtype=jnp.int32)[None, None, :]).reshape(-1)
    own_idx = block_size + chan_local
    base_row = lax.axis_index("chan") * block_size - block_size
    far_idx = jnp.clip(jnp.take(partners, chan_local, axis=0) - base_row, 0, 3 * block_size - 1).reshape(-1)

    partial = pair_lags(near, own_idx, far_idx, lag_table(samples), per_block)
    summed = scatter_sum(partial, nx, nz, half * K)
    scale = 1.0 / math.sqrt(windows_dev * tm_count * NFB)
    return summed.T * scale


def ring_pairs(sizes, axis, shift):
    nx, nz = sizes
    pairs = []
    for d in range(nx * nz):
        x, z = d // nz, d % nz
        if axis == 1:
            pairs.append((d, x * nz + (z + shift) % nz))
        else:
            pairs.append((d, ((x + shift) % nx) * nz + z))
    return pairs


def pick(array, index, width):
    return lax.dynamic_slice_in_dim(array, index * width, width, axis=1)


def scatter_sum(lags, nx, nz, width):
    me = lax.axis_index("tm")
    mx, mz = me // nz, me % nz
    span = nx * nz * width

    def round_(arrays):
        outs = []
        for array, mine, axis, n, size in arrays:
            acc = pick(array, mine, size)
            for shift in range(1, n):
                message = pick(array, (mine + shift) % n, size)
                acc = acc + lax.ppermute(message, "tm", ring_pairs((nx, nz), axis, shift))
            outs.append(acc)
        return outs

    def relay_round(arrays):
        firsts, outs = [], []
        for array, mine, axis, n, size in arrays:
            half = size // 2
            up_pairs = ring_pairs((nx, nz), axis, 1)
            down_pairs = ring_pairs((nx, nz), axis, n - 1)
            far = pick(array, (mine + 2) % n, size)
            firsts.append((lax.ppermute(far[:, :half], "tm", up_pairs), lax.ppermute(far[:, half:], "tm", down_pairs)))
        for (array, mine, axis, n, size), (from_below, from_above) in zip(arrays, firsts):
            half = size // 2
            up_pairs = ring_pairs((nx, nz), axis, 1)
            down_pairs = ring_pairs((nx, nz), axis, n - 1)
            up = pick(array, (mine + 1) % n, size)
            up = jnp.concatenate([up[:, :half] + from_below, up[:, half:]], axis=1)
            down = pick(array, (mine + n - 1) % n, size)
            down = jnp.concatenate([down[:, :half], down[:, half:] + from_above], axis=1)
            outs.append((array, mine, size, lax.ppermute(up, "tm", up_pairs), lax.ppermute(down, "tm", down_pairs)))
        return [pick(array, mine, size) + below + above for array, mine, size, below, above in outs]

    first_round = relay_round if nx == 4 and nz == 4 else round_
    a, b = first_round([(lags[:, :span], mz, 1, nz, nx * width), (lags[:, span:], mx, 0, nx, nz * width)])
    a, b = round_([(a, mx, 0, nx, width), (b, mz, 1, nz, width)])
    return jnp.concatenate([a, b], axis=1)


def solution(mesh):
    placed = (P("chan", "tm", None), P("chan", None), P("chan", None))
    return jax.shard_map(
        shards, mesh=mesh, in_specs=placed, out_specs=P(("chan", "tm"), None), check_vma=False
    )
```

```python
import math

import jax
import jax.numpy as jnp
from jax import lax
import functools

from jax.experimental import pallas as pl
from jax.experimental.pallas import tpu as pltpu
from jax.sharding import PartitionSpec as P

NFB = 512
F0 = 64
K = 8
LAG = 128


def split_length(samples):
    if samples % 128 == 0:
        return samples // 128, 128
    best = 1
    for b in range(1, samples + 1):
        if samples % b == 0 and b * b <= samples:
            best = b
    return samples // best, best


def angle_pair(rows, cols, padded):
    phase = (rows * cols % padded).astype(jnp.float32) * (2.0 * math.pi / padded)
    return jnp.cos(phase), jnp.sin(phase)


def fourier_table_t(samples):
    padded = 2 * samples
    outer, inner = split_length(samples)
    freqs = (F0 + jnp.arange(NFB, dtype=jnp.int32))[:, None]
    ca, sa = angle_pair(freqs, jnp.arange(outer, dtype=jnp.int32)[None, :] * inner, padded)
    cb, sb = angle_pair(freqs, jnp.arange(inner, dtype=jnp.int32)[None, :], padded)
    ca, sa = ca[:, :, None], sa[:, :, None]
    cb, sb = cb[:, None, :], sb[:, None, :]
    cos_t = (ca * cb - sa * sb).reshape(NFB, samples)
    sin_t = (sa * cb + ca * sb).reshape(NFB, samples)
    return cos_t.astype(jnp.bfloat16), (-sin_t).astype(jnp.bfloat16)


def lag_table(samples):
    padded = 2 * samples
    shifts = (jnp.arange(2 * LAG + 1, dtype=jnp.int32) - LAG)[None, :]
    fine = 16
    cu, su = angle_pair((F0 + fine * jnp.arange(NFB // fine, dtype=jnp.int32))[:, None], shifts, padded)
    cv, sv = angle_pair(jnp.arange(fine, dtype=jnp.int32)[:, None], shifts, padded)
    cu, su = cu[:, None, :], su[:, None, :]
    cv, sv = cv[None, :, :], sv[None, :, :]
    cos_t = (cu * cv - su * sv).reshape(NFB, -1)
    sin_t = (su * cv + cu * sv).reshape(NFB, -1)
    return jnp.concatenate([cos_t, -sin_t], axis=0)


def whiten(rows, fourier):
    real_part, imag_part = (
        lax.dot_general(rows, table, (((2,), (1,)), ((), ())), preferred_element_type=jnp.float32)
        for table in fourier
    )
    energy = real_part * real_part + imag_part * imag_part
    level = jnp.mean(energy, axis=-1, keepdims=True)
    divisor = jnp.sqrt(energy + 0.1 * level + 1e-05)
    whitened = jnp.concatenate([real_part / divisor, imag_part / divisor], axis=-1)
    return whitened.astype(jnp.bfloat16)


def neighbourhood(own):
    size = lax.axis_size("chan")
    up = [(i, i + 1) for i in range(size - 1)]
    down = [(j, i) for i, j in up]
    below = lax.ppermute(own, "chan", up)
    above = lax.ppermute(own, "chan", down)
    return below, own, above


def pair_kernel(own_idx, far_idx, below_ref, mid_ref, above_ref, lag_ref, out_ref,
                near_ref, lhi_ref, llo_ref, cross_ref, sems, *, group):
    step = pl.program_id(0)
    block = mid_ref.shape[0]

    @pl.when(step == 0)
    def _():
        copies = [
            pltpu.make_async_copy(src, near_ref.at[pl.ds(j * block, block)], sems.at[j])
            for j, src in enumerate((below_ref, mid_ref, above_ref))
        ]
        for c in copies:
            c.start()
        lag = lag_ref[...]
        hi = lag.astype(jnp.bfloat16)
        lhi_ref[...] = hi
        llo_ref[...] = (lag - hi.astype(jnp.float32)).astype(jnp.bfloat16)
        for c in copies:
            c.wait()

    def channel(i, carry):
        s = step * group + i
        a = near_ref[own_idx[s]].astype(jnp.float32)
        a_swap = jnp.concatenate([-a[4:8], a[0:4], -a[12:16], a[8:12]], axis=0)
        for k in range(K):
            b = near_ref[far_idx[s * K + k]].astype(jnp.float32)
            m = a * b
            n = a_swap * b
            sm = m[0:8] + m[8:16]
            sn = n[0:8] + n[8:16]
            row = jnp.concatenate([sm[0:4] + sm[4:8], sn[0:4] + sn[4:8]], axis=0)
            cross_ref[pl.ds(pl.multiple_of((i * K + k) * 8, 8), 8), :] = row
        return carry

    lax.fori_loop(0, group, channel, 0, unroll=True)
    pairs = group * K
    sums = []
    for first in (0, 4):
        slab = jnp.concatenate([cross_ref[pl.ds(r, pairs, stride=8), :] for r in range(first, first + 4)], axis=1)
        hi = slab.astype(jnp.bfloat16)
        lo = (slab - hi.astype(jnp.float32)).astype(jnp.bfloat16)
        lh = lhi_ref[:, first * 128 : (first + 4) * 128]
        ll = llo_ref[:, first * 128 : (first + 4) * 128]
        sums.append(nt_dot(lh, hi) + nt_dot(lh, lo) + nt_dot(ll, hi))
    wide = lhi_ref.shape[0]
    out_ref[:wide, :] = sums[0] + sums[1]
    out_ref[wide:, :] = sums[0][0:1, :] - sums[1][0:1, :]


def nt_dot(a, b):
    return lax.dot_general(a, b, (((1,), (1,)), ((), ())), preferred_element_type=jnp.float32)


def pair_lags(blocks, own_idx, far_idx, lag, group):
    rows, sub, lanes = blocks[1].shape
    count = own_idx.shape[0]
    nlag = lag.shape[1]
    lag = lag[:, : nlag - 1].T
    steps = count // group
    hbm = pl.BlockSpec(memory_space=pl.ANY)
    spec = pltpu.PrefetchScalarGridSpec(
        num_scalar_prefetch=2,
        grid=(steps,),
        in_specs=[hbm, hbm, hbm, pl.BlockSpec(lag.shape, lambda i, o, f: (0, 0))],
        out_specs=pl.BlockSpec((nlag, group * K), lambda i, o, f: (0, i)),
        scratch_shapes=[
            pltpu.VMEM((3 * rows, sub, lanes), jnp.bfloat16),
            pltpu.VMEM(lag.shape, jnp.bfloat16),
            pltpu.VMEM(lag.shape, jnp.bfloat16),
            pltpu.VMEM((group * K * 8, 128), jnp.float32),
            pltpu.SemaphoreType.DMA((3,)),
        ],
    )
    pairs = count * K
    cost = pl.CostEstimate(flops=pairs * 2048 * 6 + 3 * 2 * pairs * 1024 * (nlag - 1), transcendentals=0,
                           bytes_accessed=3 * rows * sub * lanes * 2 + pairs * nlag * 4)
    return pl.pallas_call(
        functools.partial(pair_kernel, group=group),
        grid_spec=spec,
        out_shape=jax.ShapeDtypeStruct((nlag, pairs), jnp.float32),
        compiler_params=pltpu.CompilerParams(dimension_semantics=("arbitrary",), vmem_limit_bytes=48 * 1024 * 1024),
        cost_estimate=cost,
    )(own_idx, far_idx, *blocks, lag)


def shards(record, partners, block_owner):
    block_size, windows_dev, samples = record.shape
    width = windows_dev * 2 * NFB
    fourier = fourier_table_t(samples)
    own = whiten(record, fourier).reshape(block_size, width // 128, 128)
    near = neighbourhood(own)

    tm_count = lax.axis_size("tm")
    per_block = block_size // tm_count
    owner_row = block_owner[0]
    onehot = (owner_row[None, :] == jnp.arange(tm_count, dtype=jnp.int32)[:, None]).astype(jnp.int32)
    inverse = jnp.sum(onehot * jnp.arange(tm_count, dtype=jnp.int32)[None, :], axis=1)
    nz = 4 if tm_count % 4 == 0 else 1
    nx = tm_count // nz
    half = per_block // 2
    zx = jnp.arange(nz, dtype=jnp.int32)[:, None] + nz * jnp.arange(nx, dtype=jnp.int32)[None, :]
    xz = nz * jnp.arange(nx, dtype=jnp.int32)[:, None] + jnp.arange(nz, dtype=jnp.int32)[None, :]
    dest = jnp.stack([zx.reshape(-1), xz.reshape(-1)])
    first = inverse[dest] * per_block + jnp.arange(2, dtype=jnp.int32)[:, None] * half
    chan_local = (first[:, :, None] + jnp.arange(half, dtype=jnp.int32)[None, None, :]).reshape(-1)
    own_idx = block_size + chan_local
    base_row = lax.axis_index("chan") * block_size - block_size
    far_idx = jnp.clip(jnp.take(partners, chan_local, axis=0) - base_row, 0, 3 * block_size - 1).reshape(-1)

    partial = pair_lags(near, own_idx, far_idx, lag_table(samples), per_block)
    summed = scatter_sum(partial, nx, nz, half * K)
    scale = 1.0 / math.sqrt(windows_dev * tm_count * NFB)
    return summed.T * scale


def ring_pairs(sizes, axis, shift):
    nx, nz = sizes
    pairs = []
    for d in range(nx * nz):
        x, z = d // nz, d % nz
        if axis == 1:
            pairs.append((d, x * nz + (z + shift) % nz))
        else:
            pairs.append((d, ((x + shift) % nx) * nz + z))
    return pairs


def pick(array, index, width):
    return lax.dynamic_slice_in_dim(array, index * width, width, axis=1)


def scatter_sum(lags, nx, nz, width):
    me = lax.axis_index("tm")
    mx, mz = me // nz, me % nz
    span = nx * nz * width

    def round_(arrays):
        outs = []
        for array, mine, axis, n, size in arrays:
            acc = pick(array, mine, size)
            for shift in range(1, n):
                message = pick(array, (mine + shift) % n, size)
                acc = acc + lax.ppermute(message, "tm", ring_pairs((nx, nz), axis, shift))
            outs.append(acc)
        return outs

    def split_axis(size):
        return 1 if size >= 256 else 0

    def halves(block):
        axis = split_axis(block.shape[1])
        cut = block.shape[axis] // 2 // 128 * 128 if axis == 0 else block.shape[1] // 2
        return lax.slice_in_dim(block, 0, cut, axis=axis), lax.slice_in_dim(block, cut, block.shape[axis], axis=axis)

    def relay_round(arrays):
        firsts, outs = [], []
        for array, mine, axis, n, size in arrays:
            up_pairs = ring_pairs((nx, nz), axis, 1)
            down_pairs = ring_pairs((nx, nz), axis, n - 1)
            low, high = halves(pick(array, (mine + 2) % n, size))
            firsts.append((lax.ppermute(low, "tm", up_pairs), lax.ppermute(high, "tm", down_pairs)))
        for (array, mine, axis, n, size), (from_below, from_above) in zip(arrays, firsts):
            up_pairs = ring_pairs((nx, nz), axis, 1)
            down_pairs = ring_pairs((nx, nz), axis, n - 1)
            low, high = halves(pick(array, (mine + 1) % n, size))
            up = jnp.concatenate([low + from_below, high], axis=split_axis(size))
            low, high = halves(pick(array, (mine + n - 1) % n, size))
            down = jnp.concatenate([low, high + from_above], axis=split_axis(size))
            outs.append((array, mine, size, lax.ppermute(up, "tm", up_pairs), lax.ppermute(down, "tm", down_pairs)))
        return [pick(array, mine, size) + below + above for array, mine, size, below, above in outs]

    first_round = relay_round if nx == 4 and nz == 4 else round_
    a, b = first_round([(lags[:, :span], mz, 1, nz, nx * width), (lags[:, span:], mx, 0, nx, nz * width)])
    a, b = first_round([(a, mx, 0, nx, width), (b, mz, 1, nz, width)])
    return jnp.concatenate([a, b], axis=1)


def solution(mesh):
    placed = (P("chan", "tm", None), P("chan", None), P("chan", None))
    return jax.shard_map(
        shards, mesh=mesh, in_specs=placed, out_specs=P(("chan", "tm"), None), check_vma=False
    )
```

```python
import math

import jax
import jax.numpy as jnp
from jax import lax
import functools

from jax.experimental import pallas as pl
from jax.experimental.pallas import tpu as pltpu
from jax.sharding import PartitionSpec as P

NFB = 512
F0 = 64
K = 8
LAG = 128


def split_length(samples):
    if samples % 128 == 0:
        return samples // 128, 128
    best = 1
    for b in range(1, samples + 1):
        if samples % b == 0 and b * b <= samples:
            best = b
    return samples // best, best


def angle_pair(rows, cols, padded):
    phase = (rows * cols % padded).astype(jnp.float32) * (2.0 * math.pi / padded)
    return jnp.cos(phase), jnp.sin(phase)


def fourier_table_t(samples):
    padded = 2 * samples
    outer, inner = split_length(samples)
    freqs = (F0 + jnp.arange(NFB, dtype=jnp.int32))[:, None]
    ca, sa = angle_pair(freqs, jnp.arange(outer, dtype=jnp.int32)[None, :] * inner, padded)
    cb, sb = angle_pair(freqs, jnp.arange(inner, dtype=jnp.int32)[None, :], padded)
    ca, sa = ca[:, :, None], sa[:, :, None]
    cb, sb = cb[:, None, :], sb[:, None, :]
    cos_t = (ca * cb - sa * sb).reshape(NFB, samples)
    sin_t = (sa * cb + ca * sb).reshape(NFB, samples)
    return cos_t.astype(jnp.bfloat16), (-sin_t).astype(jnp.bfloat16)


def lag_table(samples):
    padded = 2 * samples
    shifts = (jnp.arange(2 * LAG + 1, dtype=jnp.int32) - LAG)[None, :]
    fine = 16
    cu, su = angle_pair((F0 + fine * jnp.arange(NFB // fine, dtype=jnp.int32))[:, None], shifts, padded)
    cv, sv = angle_pair(jnp.arange(fine, dtype=jnp.int32)[:, None], shifts, padded)
    cu, su = cu[:, None, :], su[:, None, :]
    cv, sv = cv[None, :, :], sv[None, :, :]
    cos_t = (cu * cv - su * sv).reshape(NFB, -1)
    sin_t = (su * cv + cu * sv).reshape(NFB, -1)
    return jnp.concatenate([cos_t, -sin_t], axis=0)


def whiten(rows, fourier):
    real_part, imag_part = (
        lax.dot_general(rows, table, (((2,), (1,)), ((), ())), preferred_element_type=jnp.float32)
        for table in fourier
    )
    energy = real_part * real_part + imag_part * imag_part
    level = jnp.mean(energy, axis=-1, keepdims=True)
    divisor = jnp.sqrt(energy + 0.1 * level + 1e-05)
    whitened = jnp.concatenate([real_part / divisor, imag_part / divisor], axis=-1)
    return whitened.astype(jnp.bfloat16)


def neighbourhood(own):
    size = lax.axis_size("chan")
    up = [(i, i + 1) for i in range(size - 1)]
    down = [(j, i) for i, j in up]
    below = lax.ppermute(own, "chan", up)
    above = lax.ppermute(own, "chan", down)
    return below, own, above


def pair_kernel(own_idx, far_idx, below_ref, mid_ref, above_ref, lag_ref, out_ref,
                near_ref, lhi_ref, llo_ref, cross_ref, sems, *, group):
    step = pl.program_id(0)
    block = mid_ref.shape[0]

    @pl.when(step == 0)
    def _():
        copies = [
            pltpu.make_async_copy(src, near_ref.at[pl.ds(j * block, block)], sems.at[j])
            for j, src in enumerate((below_ref, mid_ref, above_ref))
        ]
        for c in copies:
            c.start()
        lag = lag_ref[...]
        hi = lag.astype(jnp.bfloat16)
        lhi_ref[...] = hi
        llo_ref[...] = (lag - hi.astype(jnp.float32)).astype(jnp.bfloat16)
        for c in copies:
            c.wait()

    def channel(i, carry):
        s = step * group + i
        a = near_ref[own_idx[s]].astype(jnp.float32)
        a_swap = jnp.concatenate([-a[4:8], a[0:4], -a[12:16], a[8:12]], axis=0)
        for k in range(K):
            b = near_ref[far_idx[s * K + k]].astype(jnp.float32)
            m = a * b
            n = a_swap * b
            sm = m[0:8] + m[8:16]
            sn = n[0:8] + n[8:16]
            row = jnp.concatenate([sm[0:4] + sm[4:8], sn[0:4] + sn[4:8]], axis=0)
            cross_ref[pl.ds(pl.multiple_of((i * K + k) * 8, 8), 8), :] = row
        return carry

    lax.fori_loop(0, group, channel, 0, unroll=True)
    pairs = group * K
    sums = []
    for first in (0, 4):
        slab = jnp.concatenate([cross_ref[pl.ds(r, pairs, stride=8), :] for r in range(first, first + 4)], axis=1)
        hi = slab.astype(jnp.bfloat16)
        lo = (slab - hi.astype(jnp.float32)).astype(jnp.bfloat16)
        lh = lhi_ref[:, first * 128 : (first + 4) * 128]
        ll = llo_ref[:, first * 128 : (first + 4) * 128]
        sums.append(nt_dot(lh, hi) + nt_dot(lh, lo) + nt_dot(ll, hi))
    wide = lhi_ref.shape[0]
    out_ref[:wide, :] = sums[0] + sums[1]
    out_ref[wide:, :] = sums[0][0:1, :] - sums[1][0:1, :]


def nt_dot(a, b):
    return lax.dot_general(a, b, (((1,), (1,)), ((), ())), preferred_element_type=jnp.float32)


def pair_lags(blocks, own_idx, far_idx, lag, group):
    rows, sub, lanes = blocks[1].shape
    count = own_idx.shape[0]
    nlag = lag.shape[1]
    lag = lag[:, : nlag - 1].T
    steps = count // group
    hbm = pl.BlockSpec(memory_space=pl.ANY)
    spec = pltpu.PrefetchScalarGridSpec(
        num_scalar_prefetch=2,
        grid=(steps,),
        in_specs=[hbm, hbm, hbm, pl.BlockSpec(lag.shape, lambda i, o, f: (0, 0))],
        out_specs=pl.BlockSpec((nlag, group * K), lambda i, o, f: (0, i)),
        scratch_shapes=[
            pltpu.VMEM((3 * rows, sub, lanes), jnp.bfloat16),
            pltpu.VMEM(lag.shape, jnp.bfloat16),
            pltpu.VMEM(lag.shape, jnp.bfloat16),
            pltpu.VMEM((group * K * 8, 128), jnp.float32),
            pltpu.SemaphoreType.DMA((3,)),
        ],
    )
    pairs = count * K
    cost = pl.CostEstimate(flops=pairs * 2048 * 6 + 3 * 2 * pairs * 1024 * (nlag - 1), transcendentals=0,
                           bytes_accessed=3 * rows * sub * lanes * 2 + pairs * nlag * 4)
    return pl.pallas_call(
        functools.partial(pair_kernel, group=group),
        grid_spec=spec,
        out_shape=jax.ShapeDtypeStruct((nlag, pairs), jnp.float32),
        compiler_params=pltpu.CompilerParams(dimension_semantics=("arbitrary",), vmem_limit_bytes=48 * 1024 * 1024),
        cost_estimate=cost,
    )(own_idx, far_idx, *blocks, lag)


def shards(record, partners, block_owner):
    block_size, windows_dev, samples = record.shape
    width = windows_dev * 2 * NFB
    fourier = fourier_table_t(samples)
    own = whiten(record, fourier).reshape(block_size, width // 128, 128)
    near = neighbourhood(own)

    tm_count = lax.axis_size("tm")
    per_block = block_size // tm_count
    owner_row = block_owner[0]
    onehot = (owner_row[None, :] == jnp.arange(tm_count, dtype=jnp.int32)[:, None]).astype(jnp.int32)
    inverse = jnp.sum(onehot * jnp.arange(tm_count, dtype=jnp.int32)[None, :], axis=1)
    nz = 4 if tm_count % 4 == 0 else 1
    nx = tm_count // nz
    half = per_block // 2
    zx = jnp.arange(nz, dtype=jnp.int32)[:, None] + nz * jnp.arange(nx, dtype=jnp.int32)[None, :]
    xz = nz * jnp.arange(nx, dtype=jnp.int32)[:, None] + jnp.arange(nz, dtype=jnp.int32)[None, :]
    dest = jnp.stack([zx.reshape(-1), xz.reshape(-1)])
    first = inverse[dest] * per_block + jnp.arange(2, dtype=jnp.int32)[:, None] * half
    chan_local = (first[:, :, None] + jnp.arange(half, dtype=jnp.int32)[None, None, :]).reshape(-1)
    own_idx = block_size + chan_local
    base_row = lax.axis_index("chan") * block_size - block_size
    far_idx = jnp.clip(jnp.take(partners, chan_local, axis=0) - base_row, 0, 3 * block_size - 1).reshape(-1)

    partial = pair_lags(near, own_idx, far_idx, lag_table(samples), 2 * per_block)
    summed = scatter_sum(partial, nx, nz, half * K)
    scale = 1.0 / math.sqrt(windows_dev * tm_count * NFB)
    return summed.T * scale


def ring_pairs(sizes, axis, shift):
    nx, nz = sizes
    pairs = []
    for d in range(nx * nz):
        x, z = d // nz, d % nz
        if axis == 1:
            pairs.append((d, x * nz + (z + shift) % nz))
        else:
            pairs.append((d, ((x + shift) % nx) * nz + z))
    return pairs


def pick(array, index, width):
    return lax.dynamic_slice_in_dim(array, index * width, width, axis=1)


def scatter_sum(lags, nx, nz, width):
    me = lax.axis_index("tm")
    mx, mz = me // nz, me % nz
    span = nx * nz * width

    def round_(arrays):
        outs = []
        for array, mine, axis, n, size in arrays:
            acc = pick(array, mine, size)
            for shift in range(1, n):
                message = pick(array, (mine + shift) % n, size)
                acc = acc + lax.ppermute(message, "tm", ring_pairs((nx, nz), axis, shift))
            outs.append(acc)
        return outs

    def relay_round(arrays):
        firsts, outs = [], []
        for array, mine, axis, n, size in arrays:
            half = size // 2
            up_pairs = ring_pairs((nx, nz), axis, 1)
            down_pairs = ring_pairs((nx, nz), axis, n - 1)
            far = pick(array, (mine + 2) % n, size)
            firsts.append((lax.ppermute(far[:, :half], "tm", up_pairs), lax.ppermute(far[:, half:], "tm", down_pairs)))
        for (array, mine, axis, n, size), (from_below, from_above) in zip(arrays, firsts):
            half = size // 2
            up_pairs = ring_pairs((nx, nz), axis, 1)
            down_pairs = ring_pairs((nx, nz), axis, n - 1)
            up = pick(array, (mine + 1) % n, size)
            up = jnp.concatenate([up[:, :half] + from_below, up[:, half:]], axis=1)
            down = pick(array, (mine + n - 1) % n, size)
            down = jnp.concatenate([down[:, :half], down[:, half:] + from_above], axis=1)
            outs.append((array, mine, size, lax.ppermute(up, "tm", up_pairs), lax.ppermute(down, "tm", down_pairs)))
        return [pick(array, mine, size) + below + above for array, mine, size, below, above in outs]

    first_round = relay_round if nx == 4 and nz == 4 else round_
    a, b = first_round([(lags[:, :span], mz, 1, nz, nx * width), (lags[:, span:], mx, 0, nx, nz * width)])
    a, b = round_([(a, mx, 0, nx, width), (b, mz, 1, nz, width)])
    return jnp.concatenate([a, b], axis=1)


def solution(mesh):
    placed = (P("chan", "tm", None), P("chan", None), P("chan", None))
    return jax.shard_map(
        shards, mesh=mesh, in_specs=placed, out_specs=P(("chan", "tm"), None), check_vma=False
    )
```

```python
import math

import jax
import jax.numpy as jnp
from jax import lax
import functools

from jax.experimental import pallas as pl
from jax.experimental.pallas import tpu as pltpu
from jax.sharding import PartitionSpec as P

NFB = 512
F0 = 64
K = 8
LAG = 128


def split_length(samples):
    if samples % 128 == 0:
        return samples // 128, 128
    best = 1
    for b in range(1, samples + 1):
        if samples % b == 0 and b * b <= samples:
            best = b
    return samples // best, best


def angle_pair(rows, cols, padded):
    phase = (rows * cols % padded).astype(jnp.float32) * (2.0 * math.pi / padded)
    return jnp.cos(phase), jnp.sin(phase)


def fourier_table_t(samples):
    padded = 2 * samples
    outer, inner = split_length(samples)
    freqs = (F0 + jnp.arange(NFB, dtype=jnp.int32))[:, None]
    ca, sa = angle_pair(freqs, jnp.arange(outer, dtype=jnp.int32)[None, :] * inner, padded)
    cb, sb = angle_pair(freqs, jnp.arange(inner, dtype=jnp.int32)[None, :], padded)
    ca, sa = ca[:, :, None], sa[:, :, None]
    cb, sb = cb[:, None, :], sb[:, None, :]
    cos_t = (ca * cb - sa * sb).reshape(NFB, samples)
    sin_t = (sa * cb + ca * sb).reshape(NFB, samples)
    return cos_t.astype(jnp.bfloat16), (-sin_t).astype(jnp.bfloat16)


def lag_table(samples):
    padded = 2 * samples
    shifts = (jnp.arange(2 * LAG + 1, dtype=jnp.int32) - LAG)[None, :]
    fine = 16
    cu, su = angle_pair((F0 + fine * jnp.arange(NFB // fine, dtype=jnp.int32))[:, None], shifts, padded)
    cv, sv = angle_pair(jnp.arange(fine, dtype=jnp.int32)[:, None], shifts, padded)
    cu, su = cu[:, None, :], su[:, None, :]
    cv, sv = cv[None, :, :], sv[None, :, :]
    cos_t = (cu * cv - su * sv).reshape(NFB, -1)
    sin_t = (su * cv + cu * sv).reshape(NFB, -1)
    return jnp.concatenate([cos_t, -sin_t], axis=0)


def whiten(rows, fourier):
    real_part, imag_part = (
        lax.dot_general(rows, table, (((2,), (1,)), ((), ())), preferred_element_type=jnp.float32)
        for table in fourier
    )
    energy = real_part * real_part + imag_part * imag_part
    level = jnp.mean(energy, axis=-1, keepdims=True)
    divisor = jnp.sqrt(energy + 0.1 * level + 1e-05)
    whitened = jnp.concatenate([real_part / divisor, imag_part / divisor], axis=-1)
    return whitened.astype(jnp.bfloat16)


def neighbourhood(own):
    size = lax.axis_size("chan")
    up = [(i, i + 1) for i in range(size - 1)]
    down = [(j, i) for i, j in up]
    below = lax.ppermute(own, "chan", up)
    above = lax.ppermute(own, "chan", down)
    return below, own, above


def pair_kernel(own_idx, far_idx, below_ref, mid_ref, above_ref, lag_ref, out_ref,
                near_ref, lhi_ref, llo_ref, cross_ref, sems, *, group):
    step = pl.program_id(0)
    block = mid_ref.shape[0]

    @pl.when(step == 0)
    def _():
        copies = [
            pltpu.make_async_copy(src, near_ref.at[pl.ds(j * block, block)], sems.at[j])
            for j, src in enumerate((below_ref, mid_ref, above_ref))
        ]
        for c in copies:
            c.start()
        lag = lag_ref[...]
        hi = lag.astype(jnp.bfloat16)
        lhi_ref[...] = hi
        llo_ref[...] = (lag - hi.astype(jnp.float32)).astype(jnp.bfloat16)
        for c in copies:
            c.wait()

    def channel(i, carry):
        s = step * group + i
        a = near_ref[own_idx[s]].astype(jnp.float32)
        a_swap = jnp.concatenate([-a[4:8], a[0:4], -a[12:16], a[8:12]], axis=0)
        for k in range(K):
            b = near_ref[far_idx[s * K + k]].astype(jnp.float32)
            m = a * b
            n = a_swap * b
            sm = m[0:8] + m[8:16]
            sn = n[0:8] + n[8:16]
            row = jnp.concatenate([sm[0:4] + sm[4:8], sn[0:4] + sn[4:8]], axis=0)
            cross_ref[pl.ds(pl.multiple_of((i * K + k) * 8, 8), 8), :] = row
        return carry

    lax.fori_loop(0, group, channel, 0, unroll=True)
    pairs = group * K
    sums = []
    for first in (0, 4):
        slab = jnp.concatenate([cross_ref[pl.ds(r, pairs, stride=8), :] for r in range(first, first + 4)], axis=1)
        hi = slab.astype(jnp.bfloat16)
        lo = (slab - hi.astype(jnp.float32)).astype(jnp.bfloat16)
        lh = lhi_ref[:, first * 128 : (first + 4) * 128]
        ll = llo_ref[:, first * 128 : (first + 4) * 128]
        sums.append(nt_dot(lh, hi) + nt_dot(lh, lo) + nt_dot(ll, hi))
    wide = lhi_ref.shape[0]
    out_ref[:wide, :] = sums[0] + sums[1]
    out_ref[wide:, :] = sums[0][0:1, :] - sums[1][0:1, :]


def nt_dot(a, b):
    return lax.dot_general(a, b, (((1,), (1,)), ((), ())), preferred_element_type=jnp.float32)


def pair_lags(blocks, own_idx, far_idx, lag, group):
    rows, sub, lanes = blocks[1].shape
    count = own_idx.shape[0]
    nlag = lag.shape[1]
    lag = lag[:, : nlag - 1].T
    steps = count // group
    hbm = pl.BlockSpec(memory_space=pl.ANY)
    spec = pltpu.PrefetchScalarGridSpec(
        num_scalar_prefetch=2,
        grid=(steps,),
        in_specs=[hbm, hbm, hbm, pl.BlockSpec(lag.shape, lambda i, o, f: (0, 0))],
        out_specs=pl.BlockSpec((nlag, group * K), lambda i, o, f: (0, i)),
        scratch_shapes=[
            pltpu.VMEM((3 * rows, sub, lanes), jnp.bfloat16),
            pltpu.VMEM(lag.shape, jnp.bfloat16),
            pltpu.VMEM(lag.shape, jnp.bfloat16),
            pltpu.VMEM((group * K * 8, 128), jnp.float32),
            pltpu.SemaphoreType.DMA((3,)),
        ],
    )
    pairs = count * K
    cost = pl.CostEstimate(flops=pairs * 2048 * 6 + 3 * 2 * pairs * 1024 * (nlag - 1), transcendentals=0,
                           bytes_accessed=3 * rows * sub * lanes * 2 + pairs * nlag * 4)
    return pl.pallas_call(
        functools.partial(pair_kernel, group=group),
        grid_spec=spec,
        out_shape=jax.ShapeDtypeStruct((nlag, pairs), jnp.float32),
        compiler_params=pltpu.CompilerParams(dimension_semantics=("arbitrary",), vmem_limit_bytes=48 * 1024 * 1024),
        cost_estimate=cost,
    )(own_idx, far_idx, *blocks, lag)


def shards(record, partners, block_owner):
    block_size, windows_dev, samples = record.shape
    width = windows_dev * 2 * NFB
    fourier = fourier_table_t(samples)
    own = whiten(record, fourier).reshape(block_size, width // 128, 128)
    near = neighbourhood(own)

    tm_count = lax.axis_size("tm")
    per_block = block_size // tm_count
    owner_row = block_owner[0]
    onehot = (owner_row[None, :] == jnp.arange(tm_count, dtype=jnp.int32)[:, None]).astype(jnp.int32)
    inverse = jnp.sum(onehot * jnp.arange(tm_count, dtype=jnp.int32)[None, :], axis=1)
    nz = 4 if tm_count % 4 == 0 else 1
    nx = tm_count // nz
    half = per_block // 2
    zx = jnp.arange(nz, dtype=jnp.int32)[:, None] + nz * jnp.arange(nx, dtype=jnp.int32)[None, :]
    xz = nz * jnp.arange(nx, dtype=jnp.int32)[:, None] + jnp.arange(nz, dtype=jnp.int32)[None, :]
    dest = jnp.stack([zx.reshape(-1), xz.reshape(-1)])
    first = inverse[dest] * per_block + jnp.arange(2, dtype=jnp.int32)[:, None] * half
    chan_local = (first[:, :, None] + jnp.arange(half, dtype=jnp.int32)[None, None, :]).reshape(-1)
    own_idx = block_size + chan_local
    base_row = lax.axis_index("chan") * block_size - block_size
    far_idx = jnp.clip(jnp.take(partners, chan_local, axis=0) - base_row, 0, 3 * block_size - 1).reshape(-1)

    partial = pair_lags(near, own_idx, far_idx, lag_table(samples), 4 * per_block)
    summed = scatter_sum(partial, nx, nz, half * K)
    scale = 1.0 / math.sqrt(windows_dev * tm_count * NFB)
    return summed.T * scale


def ring_pairs(sizes, axis, shift):
    nx, nz = sizes
    pairs = []
    for d in range(nx * nz):
        x, z = d // nz, d % nz
        if axis == 1:
            pairs.append((d, x * nz + (z + shift) % nz))
        else:
            pairs.append((d, ((x + shift) % nx) * nz + z))
    return pairs


def pick(array, index, width):
    return lax.dynamic_slice_in_dim(array, index * width, width, axis=1)


def scatter_sum(lags, nx, nz, width):
    me = lax.axis_index("tm")
    mx, mz = me // nz, me % nz
    span = nx * nz * width

    def round_(arrays):
        outs = []
        for array, mine, axis, n, size in arrays:
            acc = pick(array, mine, size)
            for shift in range(1, n):
                message = pick(array, (mine + shift) % n, size)
                acc = acc + lax.ppermute(message, "tm", ring_pairs((nx, nz), axis, shift))
            outs.append(acc)
        return outs

    def relay_round(arrays):
        firsts, outs = [], []
        for array, mine, axis, n, size in arrays:
            half = size // 2
            up_pairs = ring_pairs((nx, nz), axis, 1)
            down_pairs = ring_pairs((nx, nz), axis, n - 1)
            far = pick(array, (mine + 2) % n, size)
            firsts.append((lax.ppermute(far[:, :half], "tm", up_pairs), lax.ppermute(far[:, half:], "tm", down_pairs)))
        for (array, mine, axis, n, size), (from_below, from_above) in zip(arrays, firsts):
            half = size // 2
            up_pairs = ring_pairs((nx, nz), axis, 1)
            down_pairs = ring_pairs((nx, nz), axis, n - 1)
            up = pick(array, (mine + 1) % n, size)
            up = jnp.concatenate([up[:, :half] + from_below, up[:, half:]], axis=1)
            down = pick(array, (mine + n - 1) % n, size)
            down = jnp.concatenate([down[:, :half], down[:, half:] + from_above], axis=1)
            outs.append((array, mine, size, lax.ppermute(up, "tm", up_pairs), lax.ppermute(down, "tm", down_pairs)))
        return [pick(array, mine, size) + below + above for array, mine, size, below, above in outs]

    first_round = relay_round if nx == 4 and nz == 4 else round_
    a, b = first_round([(lags[:, :span], mz, 1, nz, nx * width), (lags[:, span:], mx, 0, nx, nz * width)])
    a, b = round_([(a, mx, 0, nx, width), (b, mz, 1, nz, width)])
    return jnp.concatenate([a, b], axis=1)


def solution(mesh):
    placed = (P("chan", "tm", None), P("chan", None), P("chan", None))
    return jax.shard_map(
        shards, mesh=mesh, in_specs=placed, out_specs=P(("chan", "tm"), None), check_vma=False
    )
```

```python
import math

import jax
import jax.numpy as jnp
from jax import lax
import functools

from jax.experimental import pallas as pl
from jax.experimental.pallas import tpu as pltpu
from jax.sharding import PartitionSpec as P

NFB = 512
F0 = 64
K = 8
LAG = 128


def split_length(samples):
    if samples % 128 == 0:
        return samples // 128, 128
    best = 1
    for b in range(1, samples + 1):
        if samples % b == 0 and b * b <= samples:
            best = b
    return samples // best, best


def angle_pair(rows, cols, padded):
    phase = (rows * cols % padded).astype(jnp.float32) * (2.0 * math.pi / padded)
    return jnp.cos(phase), jnp.sin(phase)


def fourier_table_t(samples):
    padded = 2 * samples
    outer, inner = split_length(samples)
    freqs = (F0 + jnp.arange(NFB, dtype=jnp.int32))[:, None]
    ca, sa = angle_pair(freqs, jnp.arange(outer, dtype=jnp.int32)[None, :] * inner, padded)
    cb, sb = angle_pair(freqs, jnp.arange(inner, dtype=jnp.int32)[None, :], padded)
    ca, sa = ca[:, :, None], sa[:, :, None]
    cb, sb = cb[:, None, :], sb[:, None, :]
    cos_t = (ca * cb - sa * sb).reshape(NFB, samples)
    sin_t = (sa * cb + ca * sb).reshape(NFB, samples)
    return cos_t.astype(jnp.bfloat16), (-sin_t).astype(jnp.bfloat16)


def lag_table(samples):
    padded = 2 * samples
    shifts = (jnp.arange(2 * LAG + 1, dtype=jnp.int32) - LAG)[None, :]
    fine = 16
    cu, su = angle_pair((F0 + fine * jnp.arange(NFB // fine, dtype=jnp.int32))[:, None], shifts, padded)
    cv, sv = angle_pair(jnp.arange(fine, dtype=jnp.int32)[:, None], shifts, padded)
    cu, su = cu[:, None, :], su[:, None, :]
    cv, sv = cv[None, :, :], sv[None, :, :]
    cos_t = (cu * cv - su * sv).reshape(NFB, -1)
    sin_t = (su * cv + cu * sv).reshape(NFB, -1)
    return jnp.concatenate([cos_t, -sin_t], axis=0)


def whiten(rows, fourier):
    real_part, imag_part = (
        lax.dot_general(rows, table, (((2,), (1,)), ((), ())), preferred_element_type=jnp.float32)
        for table in fourier
    )
    energy = real_part * real_part + imag_part * imag_part
    level = jnp.mean(energy, axis=-1, keepdims=True)
    divisor = jnp.sqrt(energy + 0.1 * level + 1e-05)
    whitened = jnp.concatenate([real_part / divisor, imag_part / divisor], axis=-1)
    return whitened.astype(jnp.bfloat16)


def neighbourhood(own):
    size = lax.axis_size("chan")
    across = [(i, i + 1) for i in range(1, size - 1, 2)] + [(i + 1, i) for i in range(1, size - 1, 2)]
    within = [(i, i + 1) for i in range(0, size - 1, 2)] + [(i + 1, i) for i in range(0, size - 1, 2)]
    far = lax.ppermute(own, "chan", across)
    near = lax.ppermute(own, "chan", within)
    return far, own, near


def pair_kernel(own_idx, far_idx, below_ref, mid_ref, above_ref, lag_ref, out_ref,
                near_ref, lhi_ref, llo_ref, cross_ref, sems, *, group):
    step = pl.program_id(0)
    block = mid_ref.shape[0]

    @pl.when(step == 0)
    def _():
        odd = lax.axis_index("chan") % 2
        starts = (odd * 2 * block, block, (1 - odd) * 2 * block)
        copies = [
            pltpu.make_async_copy(src, near_ref.at[pl.ds(start, block)], sems.at[j])
            for j, (src, start) in enumerate(zip((below_ref, mid_ref, above_ref), starts))
        ]
        for c in copies:
            c.start()
        lag = lag_ref[...]
        hi = lag.astype(jnp.bfloat16)
        lhi_ref[...] = hi
        llo_ref[...] = (lag - hi.astype(jnp.float32)).astype(jnp.bfloat16)
        for c in copies:
            c.wait()

    def channel(i, carry):
        s = step * group + i
        a = near_ref[own_idx[s]].astype(jnp.float32)
        a_swap = jnp.concatenate([-a[4:8], a[0:4], -a[12:16], a[8:12]], axis=0)
        for k in range(K):
            b = near_ref[far_idx[s * K + k]].astype(jnp.float32)
            m = a * b
            n = a_swap * b
            sm = m[0:8] + m[8:16]
            sn = n[0:8] + n[8:16]
            row = jnp.concatenate([sm[0:4] + sm[4:8], sn[0:4] + sn[4:8]], axis=0)
            cross_ref[pl.ds(pl.multiple_of((i * K + k) * 8, 8), 8), :] = row
        return carry

    lax.fori_loop(0, group, channel, 0, unroll=True)
    pairs = group * K
    sums = []
    for first in (0, 4):
        slab = jnp.concatenate([cross_ref[pl.ds(r, pairs, stride=8), :] for r in range(first, first + 4)], axis=1)
        hi = slab.astype(jnp.bfloat16)
        lo = (slab - hi.astype(jnp.float32)).astype(jnp.bfloat16)
        lh = lhi_ref[:, first * 128 : (first + 4) * 128]
        ll = llo_ref[:, first * 128 : (first + 4) * 128]
        sums.append(nt_dot(lh, hi) + nt_dot(lh, lo) + nt_dot(ll, hi))
    wide = lhi_ref.shape[0]
    out_ref[:wide, :] = sums[0] + sums[1]
    out_ref[wide:, :] = sums[0][0:1, :] - sums[1][0:1, :]


def nt_dot(a, b):
    return lax.dot_general(a, b, (((1,), (1,)), ((), ())), preferred_element_type=jnp.float32)


def pair_lags(blocks, own_idx, far_idx, lag, group):
    rows, sub, lanes = blocks[1].shape
    count = own_idx.shape[0]
    nlag = lag.shape[1]
    lag = lag[:, : nlag - 1].T
    steps = count // group
    hbm = pl.BlockSpec(memory_space=pl.ANY)
    spec = pltpu.PrefetchScalarGridSpec(
        num_scalar_prefetch=2,
        grid=(steps,),
        in_specs=[hbm, hbm, hbm, pl.BlockSpec(lag.shape, lambda i, o, f: (0, 0))],
        out_specs=pl.BlockSpec((nlag, group * K), lambda i, o, f: (0, i)),
        scratch_shapes=[
            pltpu.VMEM((3 * rows, sub, lanes), jnp.bfloat16),
            pltpu.VMEM(lag.shape, jnp.bfloat16),
            pltpu.VMEM(lag.shape, jnp.bfloat16),
            pltpu.VMEM((group * K * 8, 128), jnp.float32),
            pltpu.SemaphoreType.DMA((3,)),
        ],
    )
    pairs = count * K
    cost = pl.CostEstimate(flops=pairs * 2048 * 6 + 3 * 2 * pairs * 1024 * (nlag - 1), transcendentals=0,
                           bytes_accessed=3 * rows * sub * lanes * 2 + pairs * nlag * 4)
    return pl.pallas_call(
        functools.partial(pair_kernel, group=group),
        grid_spec=spec,
        out_shape=jax.ShapeDtypeStruct((nlag, pairs), jnp.float32),
        compiler_params=pltpu.CompilerParams(dimension_semantics=("arbitrary",), vmem_limit_bytes=48 * 1024 * 1024),
        cost_estimate=cost,
    )(own_idx, far_idx, *blocks, lag)


def shards(record, partners, block_owner):
    block_size, windows_dev, samples = record.shape
    width = windows_dev * 2 * NFB
    fourier = fourier_table_t(samples)
    own = whiten(record, fourier).reshape(block_size, width // 128, 128)
    near = neighbourhood(own)

    tm_count = lax.axis_size("tm")
    per_block = block_size // tm_count
    owner_row = block_owner[0]
    onehot = (owner_row[None, :] == jnp.arange(tm_count, dtype=jnp.int32)[:, None]).astype(jnp.int32)
    inverse = jnp.sum(onehot * jnp.arange(tm_count, dtype=jnp.int32)[None, :], axis=1)
    nz = 4 if tm_count % 4 == 0 else 1
    nx = tm_count // nz
    half = per_block // 2
    zx = jnp.arange(nz, dtype=jnp.int32)[:, None] + nz * jnp.arange(nx, dtype=jnp.int32)[None, :]
    xz = nz * jnp.arange(nx, dtype=jnp.int32)[:, None] + jnp.arange(nz, dtype=jnp.int32)[None, :]
    dest = jnp.stack([zx.reshape(-1), xz.reshape(-1)])
    first = inverse[dest] * per_block + jnp.arange(2, dtype=jnp.int32)[:, None] * half
    chan_local = (first[:, :, None] + jnp.arange(half, dtype=jnp.int32)[None, None, :]).reshape(-1)
    own_idx = block_size + chan_local
    base_row = lax.axis_index("chan") * block_size - block_size
    far_idx = jnp.clip(jnp.take(partners, chan_local, axis=0) - base_row, 0, 3 * block_size - 1).reshape(-1)

    partial = pair_lags(near, own_idx, far_idx, lag_table(samples), 2 * per_block)
    summed = scatter_sum(partial, nx, nz, half * K)
    scale = 1.0 / math.sqrt(windows_dev * tm_count * NFB)
    return summed.T * scale


def ring_pairs(sizes, axis, shift):
    nx, nz = sizes
    pairs = []
    for d in range(nx * nz):
        x, z = d // nz, d % nz
        if axis == 1:
            pairs.append((d, x * nz + (z + shift) % nz))
        else:
            pairs.append((d, ((x + shift) % nx) * nz + z))
    return pairs


def pick(array, index, width):
    return lax.dynamic_slice_in_dim(array, index * width, width, axis=1)


def scatter_sum(lags, nx, nz, width):
    me = lax.axis_index("tm")
    mx, mz = me // nz, me % nz
    span = nx * nz * width

    def round_(arrays):
        outs = []
        for array, mine, axis, n, size in arrays:
            acc = pick(array, mine, size)
            for shift in range(1, n):
                message = pick(array, (mine + shift) % n, size)
                acc = acc + lax.ppermute(message, "tm", ring_pairs((nx, nz), axis, shift))
            outs.append(acc)
        return outs

    def relay_round(arrays):
        firsts, outs = [], []
        for array, mine, axis, n, size in arrays:
            half = size // 2
            up_pairs = ring_pairs((nx, nz), axis, 1)
            down_pairs = ring_pairs((nx, nz), axis, n - 1)
            far = pick(array, (mine + 2) % n, size)
            firsts.append((lax.ppermute(far[:, :half], "tm", up_pairs), lax.ppermute(far[:, half:], "tm", down_pairs)))
        for (array, mine, axis, n, size), (from_below, from_above) in zip(arrays, firsts):
            half = size // 2
            up_pairs = ring_pairs((nx, nz), axis, 1)
            down_pairs = ring_pairs((nx, nz), axis, n - 1)
            up = pick(array, (mine + 1) % n, size)
            up = jnp.concatenate([up[:, :half] + from_below, up[:, half:]], axis=1)
            down = pick(array, (mine + n - 1) % n, size)
            down = jnp.concatenate([down[:, :half], down[:, half:] + from_above], axis=1)
            outs.append((array, mine, size, lax.ppermute(up, "tm", up_pairs), lax.ppermute(down, "tm", down_pairs)))
        return [pick(array, mine, size) + below + above for array, mine, size, below, above in outs]

    first_round = relay_round if nx == 4 and nz == 4 else round_
    a, b = first_round([(lags[:, :span], mz, 1, nz, nx * width), (lags[:, span:], mx, 0, nx, nz * width)])
    a, b = round_([(a, mx, 0, nx, width), (b, mz, 1, nz, width)])
    return jnp.concatenate([a, b], axis=1)


def solution(mesh):
    placed = (P("chan", "tm", None), P("chan", None), P("chan", None))
    return jax.shard_map(
        shards, mesh=mesh, in_specs=placed, out_specs=P(("chan", "tm"), None), check_vma=False
    )
```

```python
import math

import jax
import jax.numpy as jnp
from jax import lax
import functools

from jax.experimental import pallas as pl
from jax.experimental.pallas import tpu as pltpu
from jax.sharding import PartitionSpec as P

NFB = 512
F0 = 64
K = 8
LAG = 128


def split_length(samples):
    if samples % 128 == 0:
        return samples // 128, 128
    best = 1
    for b in range(1, samples + 1):
        if samples % b == 0 and b * b <= samples:
            best = b
    return samples // best, best


def angle_pair(rows, cols, padded):
    phase = (rows * cols % padded).astype(jnp.float32) * (2.0 * math.pi / padded)
    return jnp.cos(phase), jnp.sin(phase)


def fourier_table_t(samples):
    padded = 2 * samples
    outer, inner = split_length(samples)
    freqs = (F0 + jnp.arange(NFB, dtype=jnp.int32))[:, None]
    ca, sa = angle_pair(freqs, jnp.arange(outer, dtype=jnp.int32)[None, :] * inner, padded)
    cb, sb = angle_pair(freqs, jnp.arange(inner, dtype=jnp.int32)[None, :], padded)
    ca, sa = ca[:, :, None], sa[:, :, None]
    cb, sb = cb[:, None, :], sb[:, None, :]
    cos_t = (ca * cb - sa * sb).reshape(NFB, samples)
    sin_t = (sa * cb + ca * sb).reshape(NFB, samples)
    return cos_t.astype(jnp.bfloat16), (-sin_t).astype(jnp.bfloat16)


def lag_table_t(samples):
    padded = 2 * samples
    shifts = (jnp.arange(2 * LAG, dtype=jnp.int32) - LAG)[:, None]
    fine = 16
    cu, su = angle_pair(shifts, (F0 + fine * jnp.arange(NFB // fine, dtype=jnp.int32))[None, :], padded)
    cv, sv = angle_pair(shifts, jnp.arange(fine, dtype=jnp.int32)[None, :], padded)
    cu, su = cu[:, :, None], su[:, :, None]
    cv, sv = cv[:, None, :], sv[:, None, :]
    cos_t = (cu * cv - su * sv).reshape(2 * LAG, NFB)
    sin_t = (su * cv + cu * sv).reshape(2 * LAG, NFB)
    return jnp.concatenate([cos_t, -sin_t], axis=1)


def whiten(rows, fourier):
    real_part, imag_part = (
        lax.dot_general(rows, table, (((2,), (1,)), ((), ())), preferred_element_type=jnp.float32)
        for table in fourier
    )
    energy = real_part * real_part + imag_part * imag_part
    level = jnp.mean(energy, axis=-1, keepdims=True)
    divisor = jnp.sqrt(energy + 0.1 * level + 1e-05)
    whitened = jnp.concatenate([real_part / divisor, imag_part / divisor], axis=-1)
    return whitened.astype(jnp.bfloat16)


def neighbourhood(own):
    size = lax.axis_size("chan")
    across = [(i, i + 1) for i in range(1, size - 1, 2)] + [(i + 1, i) for i in range(1, size - 1, 2)]
    within = [(i, i + 1) for i in range(0, size - 1, 2)] + [(i + 1, i) for i in range(0, size - 1, 2)]
    far = lax.ppermute(own, "chan", across)
    near = lax.ppermute(own, "chan", within)
    return far, own, near


def pair_kernel(own_idx, far_idx, below_ref, mid_ref, above_ref, lag_ref, out_ref,
                near_ref, lhi_ref, llo_ref, cross_ref, sems, *, group):
    step = pl.program_id(0)
    block = mid_ref.shape[0]

    @pl.when(step == 0)
    def _():
        odd = lax.axis_index("chan") % 2
        starts = (odd * 2 * block, block, (1 - odd) * 2 * block)
        copies = [
            pltpu.make_async_copy(src, near_ref.at[pl.ds(start, block)], sems.at[j])
            for j, (src, start) in enumerate(zip((below_ref, mid_ref, above_ref), starts))
        ]
        for c in copies:
            c.start()
        lag = lag_ref[...]
        hi = lag.astype(jnp.bfloat16)
        lhi_ref[...] = hi
        llo_ref[...] = (lag - hi.astype(jnp.float32)).astype(jnp.bfloat16)
        for c in copies:
            c.wait()

    def channel(i, carry):
        s = step * group + i
        a = near_ref[own_idx[s]].astype(jnp.float32)
        a_swap = jnp.concatenate([-a[4:8], a[0:4], -a[12:16], a[8:12]], axis=0)
        for k in range(K):
            b = near_ref[far_idx[s * K + k]].astype(jnp.float32)
            m = a * b
            n = a_swap * b
            sm = m[0:8] + m[8:16]
            sn = n[0:8] + n[8:16]
            row = jnp.concatenate([sm[0:4] + sm[4:8], sn[0:4] + sn[4:8]], axis=0)
            cross_ref[pl.ds(pl.multiple_of((i * K + k) * 8, 8), 8), :] = row
        return carry

    lax.fori_loop(0, group, channel, 0, unroll=True)
    pairs = group * K
    sums = []
    for first in (0, 4):
        slab = jnp.concatenate([cross_ref[pl.ds(r, pairs, stride=8), :] for r in range(first, first + 4)], axis=1)
        hi = slab.astype(jnp.bfloat16)
        lo = (slab - hi.astype(jnp.float32)).astype(jnp.bfloat16)
        lh = lhi_ref[:, first * 128 : (first + 4) * 128]
        ll = llo_ref[:, first * 128 : (first + 4) * 128]
        sums.append(nt_dot(lh, hi) + nt_dot(lh, lo) + nt_dot(ll, hi))
    wide = lhi_ref.shape[0]
    out_ref[:wide, :] = sums[0] + sums[1]
    out_ref[wide:, :] = sums[0][0:1, :] - sums[1][0:1, :]


def nt_dot(a, b):
    return lax.dot_general(a, b, (((1,), (1,)), ((), ())), preferred_element_type=jnp.float32)


def pair_lags(blocks, own_idx, far_idx, lag, group):
    rows, sub, lanes = blocks[1].shape
    count = own_idx.shape[0]
    nlag = lag.shape[0] + 1
    steps = count // group
    hbm = pl.BlockSpec(memory_space=pl.ANY)
    spec = pltpu.PrefetchScalarGridSpec(
        num_scalar_prefetch=2,
        grid=(steps,),
        in_specs=[hbm, hbm, hbm, pl.BlockSpec(lag.shape, lambda i, o, f: (0, 0))],
        out_specs=pl.BlockSpec((nlag, group * K), lambda i, o, f: (0, i)),
        scratch_shapes=[
            pltpu.VMEM((3 * rows, sub, lanes), jnp.bfloat16),
            pltpu.VMEM(lag.shape, jnp.bfloat16),
            pltpu.VMEM(lag.shape, jnp.bfloat16),
            pltpu.VMEM((group * K * 8, 128), jnp.float32),
            pltpu.SemaphoreType.DMA((3,)),
        ],
    )
    pairs = count * K
    cost = pl.CostEstimate(flops=pairs * 2048 * 6 + 3 * 2 * pairs * 1024 * (nlag - 1), transcendentals=0,
                           bytes_accessed=3 * rows * sub * lanes * 2 + pairs * nlag * 4)
    return pl.pallas_call(
        functools.partial(pair_kernel, group=group),
        grid_spec=spec,
        out_shape=jax.ShapeDtypeStruct((nlag, pairs), jnp.float32),
        compiler_params=pltpu.CompilerParams(dimension_semantics=("arbitrary",), vmem_limit_bytes=48 * 1024 * 1024),
        cost_estimate=cost,
    )(own_idx, far_idx, *blocks, lag)


def shards(record, partners, block_owner):
    block_size, windows_dev, samples = record.shape
    width = windows_dev * 2 * NFB
    fourier = fourier_table_t(samples)
    own = whiten(record, fourier).reshape(block_size, width // 128, 128)
    near = neighbourhood(own)

    tm_count = lax.axis_size("tm")
    per_block = block_size // tm_count
    owner_row = block_owner[0]
    onehot = (owner_row[None, :] == jnp.arange(tm_count, dtype=jnp.int32)[:, None]).astype(jnp.int32)
    inverse = jnp.sum(onehot * jnp.arange(tm_count, dtype=jnp.int32)[None, :], axis=1)
    nz = 4 if tm_count % 4 == 0 else 1
    nx = tm_count // nz
    half = per_block // 2
    zx = jnp.arange(nz, dtype=jnp.int32)[:, None] + nz * jnp.arange(nx, dtype=jnp.int32)[None, :]
    xz = nz * jnp.arange(nx, dtype=jnp.int32)[:, None] + jnp.arange(nz, dtype=jnp.int32)[None, :]
    dest = jnp.stack([zx.reshape(-1), xz.reshape(-1)])
    first = inverse[dest] * per_block + jnp.arange(2, dtype=jnp.int32)[:, None] * half
    chan_local = (first[:, :, None] + jnp.arange(half, dtype=jnp.int32)[None, None, :]).reshape(-1)
    own_idx = block_size + chan_local
    base_row = lax.axis_index("chan") * block_size - block_size
    far_idx = jnp.clip(jnp.take(partners, chan_local, axis=0) - base_row, 0, 3 * block_size - 1).reshape(-1)

    partial = pair_lags(near, own_idx, far_idx, lag_table_t(samples), 2 * per_block)
    summed = scatter_sum(partial, nx, nz, half * K)
    scale = 1.0 / math.sqrt(windows_dev * tm_count * NFB)
    return summed.T * scale


def ring_pairs(sizes, axis, shift):
    nx, nz = sizes
    pairs = []
    for d in range(nx * nz):
        x, z = d // nz, d % nz
        if axis == 1:
            pairs.append((d, x * nz + (z + shift) % nz))
        else:
            pairs.append((d, ((x + shift) % nx) * nz + z))
    return pairs


def pick(array, index, width):
    return lax.dynamic_slice_in_dim(array, index * width, width, axis=1)


def scatter_sum(lags, nx, nz, width):
    me = lax.axis_index("tm")
    mx, mz = me // nz, me % nz
    span = nx * nz * width

    def round_(arrays):
        outs = []
        for array, mine, axis, n, size in arrays:
            acc = pick(array, mine, size)
            for shift in range(1, n):
                message = pick(array, (mine + shift) % n, size)
                acc = acc + lax.ppermute(message, "tm", ring_pairs((nx, nz), axis, shift))
            outs.append(acc)
        return outs

    def relay_round(arrays):
        firsts, outs = [], []
        for array, mine, axis, n, size in arrays:
            half = size // 2
            up_pairs = ring_pairs((nx, nz), axis, 1)
            down_pairs = ring_pairs((nx, nz), axis, n - 1)
            far = pick(array, (mine + 2) % n, size)
            firsts.append((lax.ppermute(far[:, :half], "tm", up_pairs), lax.ppermute(far[:, half:], "tm", down_pairs)))
        for (array, mine, axis, n, size), (from_below, from_above) in zip(arrays, firsts):
            half = size // 2
            up_pairs = ring_pairs((nx, nz), axis, 1)
            down_pairs = ring_pairs((nx, nz), axis, n - 1)
            up = pick(array, (mine + 1) % n, size)
            up = jnp.concatenate([up[:, :half] + from_below, up[:, half:]], axis=1)
            down = pick(array, (mine + n - 1) % n, size)
            down = jnp.concatenate([down[:, :half], down[:, half:] + from_above], axis=1)
            outs.append((array, mine, size, lax.ppermute(up, "tm", up_pairs), lax.ppermute(down, "tm", down_pairs)))
        return [pick(array, mine, size) + below + above for array, mine, size, below, above in outs]

    first_round = relay_round if nx == 4 and nz == 4 else round_
    a, b = first_round([(lags[:, :span], mz, 1, nz, nx * width), (lags[:, span:], mx, 0, nx, nz * width)])
    a, b = round_([(a, mx, 0, nx, width), (b, mz, 1, nz, width)])
    return jnp.concatenate([a, b], axis=1)


def solution(mesh):
    placed = (P("chan", "tm", None), P("chan", None), P("chan", None))
    return jax.shard_map(
        shards, mesh=mesh, in_specs=placed, out_specs=P(("chan", "tm"), None), check_vma=False
    )
```
